32 devices in a mesh: gx: 4 (over z), gy: 4 (over x, core), gz: 2 (over y).
Axes of the slice: x: 2, y: 2, z: 4, core: 2. Of those that a mesh axis runs over, the one named last changes fastest.
Arguments:
- tokens: bfloat16 [64, 128, 3072], P('gx', ('gy', 'gz')), may hold values from -20 to 20
- grads_out: bfloat16 [64, 128, 3072], P('gx', ('gy', 'gz')), may hold values from -6 to 6
- labels: int32 [64, 128, 16], P('gx', ('gy', 'gz')), may hold values from 0 to 2
- ln_gain: float32 [192], replicated, may hold values from 0.1 to 1.9
- qkv_weight: bfloat16 [192, 576], replicated, may hold values from -0.4375 to 0.4375
- proj_weight: bfloat16 [192, 192], replicated, may hold values from -0.4375 to 0.4375
Outputs:
- grad_tokens: bfloat16 [64, 128, 3072], P('gx', ('gy', 'gz'))
- grad_gain: float32 [192], replicated
- grad_qkv: float32 [110592], replicated
- grad_proj: float32 [36864], replicated
The draws below stay inside these ranges and needn't reach their ends.
Inputs may be any that keep to these rules, and one draw needn't show every extreme that they name: labels are given on the shifted grid.
All inputs are finite; a program needn't handle non-finite values.
Results may differ from the reference program's by a relative error of at most 0.0087.
Values may be sent and summed in bfloat16 or wider, within the bound.
No kernel may reach another device: no remote copies, remote signals or barrier semaphores. Data moves between devices by JAX's collectives and lax.ppermute only.
A program may use at most 64 MiB of HBM per device.

```python
import math
import jax
import jax.numpy as jnp
from jax import lax

HEADS = 6
C = 192
WIN = 8
SHIFT = 4
NZ = 16
N0 = 64
N1 = 128


def draw_tokens(key, part):
    key_noise, key_rows, key_cols = jax.random.split(key, 3)
    shape = (N0, N1, NZ, C)
    noise = jax.random.truncated_normal(key_noise, -4.0, 4.0, shape, jnp.float32)
    row_scale = jnp.exp(jax.random.uniform(key_rows, (N0, N1, NZ, 1), jnp.float32, math.log(0.05), math.log(0.5)))
    col_scale = jnp.exp(jax.random.uniform(key_cols, (C,), jnp.float32, 0.0, math.log(10.0)))
    values = noise * col_scale
    return (values * row_scale).reshape(N0, N1, NZ * C).astype(jnp.bfloat16)


def with_ends(drawn, stream_key, smallest, high):
    shape = drawn.shape
    place = [jax.random.randint(jax.random.fold_in(stream_key, axis), (), 0, shape[axis]) for axis in range(len(shape))]
    drawn = drawn.at[tuple(place)].set(smallest)
    longest = shape.index(max(shape))
    place[longest] = (place[longest] + 1) % shape[longest]
    return drawn.at[tuple(place)].set(high)


def shard_levels(key, shape, shards, low, top_value):
    factor_of = 1.0
    for dim, parts in shards:
        steps = jax.random.uniform(jax.random.fold_in(jax.random.fold_in(key, 6), dim), (parts,), jnp.float32, low / len(shards), top_value / len(shards))
        factor_of = factor_of * jnp.repeat(jnp.exp(steps), shape[dim] // parts).reshape((-1,) + (1,) * (len(shape) - 1 - dim))
    return factor_of


def normal_values(own_key, dims, deviation, limit, pieces=(), dtype=jnp.bfloat16):
    entries = jax.random.normal(own_key, dims, jnp.float32) * deviation
    if len(pieces) > 0:
        entries = shard_levels(own_key, dims, pieces, -0.22, 0.18) * entries
    return jnp.clip(entries, min=-limit, max=limit).astype(dtype)


def setup_inputs(seed: int = 0) -> dict:
    key_list = jax.random.split(jax.random.key(seed), 7)
    tokens = draw_tokens(jax.random.fold_in(key_list[6], 71), 0)
    grads_out = normal_values(key_list[1], (N0, N1, NZ * C), 1.0, 6.0, ((0, 4), (1, 8)))
    labels = with_ends(jax.random.randint(key_list[2], (N0, N1, NZ), 0, 3), jax.random.fold_in(key_list[2], 1), 0, 2).astype(jnp.int32)
    ln_gain = jnp.clip(1.0 + 0.18 * jax.random.normal(key_list[3], (C,), jnp.float32), 0.1, 1.9)
    qkv_weight = normal_values(key_list[4], (C, 3 * C), C ** -0.5, 0.4375)
    proj_weight = normal_values(key_list[5], (C, C), C ** -0.5, 0.4375)
    return {"tokens": tokens, "grads_out": grads_out, "labels": labels, "ln_gain": ln_gain, "qkv_weight": qkv_weight, "proj_weight": proj_weight}


def to_windows(values):
    extent_a, extent_b, extent_c = (values.shape[0], values.shape[1], values.shape[2])
    trailing = values.shape[3:]
    shaped = values.reshape((extent_a // WIN, WIN, extent_b // WIN, WIN, extent_c // WIN, WIN) + trailing)
    axes_order = (0, 2, 4, 1, 3, 5) + tuple(range(6, 6 + len(trailing)))
    return shaped.transpose(axes_order).reshape((-1, WIN ** 3) + trailing)

def from_windows(values, extent_a, extent_b, extent_c):
    trailing = values.shape[2:]
    shaped = values.reshape((extent_a // WIN, extent_b // WIN, extent_c // WIN, WIN, WIN, WIN) + trailing)
    axes_order = (0, 3, 1, 4, 2, 5) + tuple(range(6, 6 + len(trailing)))
    return shaped.transpose(axes_order).reshape((extent_a, extent_b, extent_c) + trailing)

def window_grads(window_tokens, window_grads_out, mask_keys, ln_gain, qkv_weight, proj_weight):
    channels = window_tokens.shape[1]
    head_size = channels // HEADS
    score_scale = head_size ** (-0.5)
    as_float = window_tokens.astype(jnp.float32)
    row_mean = lax.optimization_barrier(jnp.mean(as_float, axis=1, keepdims=True))
    centred = as_float - row_mean
    inv_std = lax.rsqrt(lax.optimization_barrier(jnp.mean(centred * centred, axis=1, keepdims=True)) + 1e-05)
    x_hat = centred * inv_std
    normed = (x_hat * ln_gain).astype(jnp.bfloat16)
    qkv_rows = jnp.dot(normed, qkv_weight, preferred_element_type=jnp.float32).astype(jnp.bfloat16)
    queries = qkv_rows[:, :channels].reshape(-1, HEADS, head_size).astype(jnp.float32)
    keys_all = qkv_rows[:, channels:2 * channels].reshape(-1, HEADS, head_size).astype(jnp.float32)
    values_all = qkv_rows[:, 2 * channels:].reshape(-1, HEADS, head_size).astype(jnp.float32)
    scores = jnp.einsum('ihd,jhd->hij', queries, keys_all) * score_scale
    allowed = mask_keys[:, None] == mask_keys[None, :]
    weights = jnp.where(allowed[None], jnp.exp(scores), jnp.float32(0.0))
    softmax_probs = weights / lax.optimization_barrier(jnp.sum(weights, axis=2, keepdims=True))
    probs_bf = softmax_probs.astype(jnp.bfloat16).astype(jnp.float32)
    attended = jnp.einsum('hij,jhd->ihd', probs_bf, values_all).reshape(-1, channels).astype(jnp.bfloat16)
    proj_grad = jnp.einsum('tc,td->cd', attended.astype(jnp.float32), window_grads_out.astype(jnp.float32))
    grad_attended = jnp.dot(window_grads_out, proj_weight.T, preferred_element_type=jnp.float32).astype(jnp.bfloat16)
    grad_heads = grad_attended.reshape(-1, HEADS, head_size).astype(jnp.float32)
    grad_probs = jnp.einsum('ihd,jhd->hij', grad_heads, values_all)
    grad_values = jnp.einsum('hij,ihd->jhd', probs_bf, grad_heads).astype(jnp.bfloat16)
    row_total = lax.optimization_barrier(jnp.sum(softmax_probs * grad_probs, axis=2, keepdims=True))
    grad_scores = (softmax_probs * (grad_probs - row_total) * score_scale).astype(jnp.bfloat16).astype(jnp.float32)
    grad_queries = jnp.einsum('hij,jhd->ihd', grad_scores, keys_all).astype(jnp.bfloat16)
    grad_keys = jnp.einsum('hij,ihd->jhd', grad_scores, queries).astype(jnp.bfloat16)
    grad_qkv_rows = jnp.concatenate([grad_queries.reshape(-1, channels), grad_keys.reshape(-1, channels), grad_values.reshape(-1, channels)], axis=1)
    qkv_grad = jnp.einsum('tc,td->cd', normed.astype(jnp.float32), grad_qkv_rows.astype(jnp.float32))
    grad_normed = jnp.dot(grad_qkv_rows, qkv_weight.T, preferred_element_type=jnp.float32)
    gain_grad = lax.optimization_barrier(jnp.sum(grad_normed * x_hat, axis=0))
    scaled_grad = grad_normed * ln_gain
    grad_shifted = inv_std * (scaled_grad - lax.optimization_barrier(jnp.mean(scaled_grad, axis=1, keepdims=True)) - x_hat * lax.optimization_barrier(jnp.mean(scaled_grad * x_hat, axis=1, keepdims=True)))
    return (grad_shifted.astype(jnp.bfloat16), qkv_grad, proj_grad, gain_grad)

def reference(tokens, grads_out, labels, ln_gain, qkv_weight, proj_weight):
    extent_a, extent_b = (tokens.shape[0], tokens.shape[1])
    extent_c = NZ
    channels = C
    tokens_cells = tokens.reshape(extent_a, extent_b, extent_c, channels)
    grads_cells = grads_out.reshape(extent_a, extent_b, extent_c, channels)
    shifted_tokens = jnp.roll(tokens_cells, (-SHIFT, -SHIFT, -SHIFT), axis=(0, 1, 2))
    shifted_grads = jnp.roll(grads_cells, (-SHIFT, -SHIFT, -SHIFT), axis=(0, 1, 2))
    wrap_first = (jnp.arange(extent_a) >= extent_a - SHIFT).astype(jnp.int32)
    wrap_second = (jnp.arange(extent_b) >= extent_b - SHIFT).astype(jnp.int32)
    wrap_third = (jnp.arange(extent_c) >= extent_c - SHIFT).astype(jnp.int32)
    region = wrap_first[:, None, None] * 4 + wrap_second[None, :, None] * 2 + wrap_third[None, None, :]
    mask_key = labels.astype(jnp.int32) * 8 + region.astype(jnp.int32)

    def window_step(totals, window_item):
        grad_win, qkv_part, proj_part, gain_part = window_grads(window_item[0], window_item[1], window_item[2], ln_gain, qkv_weight, proj_weight)
        return ((totals[0] + qkv_part, totals[1] + proj_part, totals[2] + gain_part), grad_win)
    zero_sums = (jnp.zeros((channels, 3 * channels), jnp.float32), jnp.zeros((channels, channels), jnp.float32), jnp.zeros((channels,), jnp.float32))
    sums, grad_windows = lax.scan(window_step, zero_sums, (to_windows(shifted_tokens), to_windows(shifted_grads), to_windows(mask_key)))
    grad_shifted = from_windows(grad_windows, extent_a, extent_b, extent_c)
    grad_branch = jnp.roll(grad_shifted, (SHIFT, SHIFT, SHIFT), axis=(0, 1, 2)).reshape(extent_a, extent_b, extent_c * channels)
    grad_tokens = (grads_out.astype(jnp.float32) + grad_branch.astype(jnp.float32)).astype(jnp.bfloat16)
    return (grad_tokens, sums[2], sums[0].reshape(-1), sums[1].reshape(-1))
```

```python
import jax
import jax.numpy as jnp
from jax import lax
from jax.experimental import pallas as pl
from jax.experimental.pallas import tpu as pltpu
from jax.sharding import PartitionSpec as P

HEADS = 6
C = 192
WIN = 8
SHIFT = 4
NZ = 16
CELLS = WIN**3
HEAD = C // HEADS
SCALE = HEAD ** (-0.5)


def passed_along(block, axis, distance):
    devices = range(lax.axis_size(axis))
    route = [((i - distance) % len(devices), i) for i in devices]
    return lax.ppermute(block, axis, route)


def to_windows_cm(values):
    extent_a, extent_b, extent_c, ch = values.shape
    shaped = values.reshape(extent_a // WIN, WIN, extent_b // WIN, WIN, extent_c // WIN, WIN, ch)
    return shaped.transpose(0, 2, 4, 6, 1, 3, 5).reshape(-1, ch, CELLS)


def from_windows_cm(values, extent_a, extent_b, extent_c):
    ch = values.shape[1]
    shaped = values.reshape(extent_a // WIN, extent_b // WIN, extent_c // WIN, ch, WIN, WIN, WIN)
    return shaped.transpose(0, 4, 1, 5, 2, 6, 3).reshape(extent_a, extent_b, extent_c, ch)


def to_windows_key(values):
    extent_a, extent_b, extent_c = values.shape
    shaped = values.reshape(extent_a // WIN, WIN, extent_b // WIN, WIN, extent_c // WIN, WIN)
    return shaped.transpose(0, 2, 4, 1, 3, 5).reshape(-1, CELLS)


def window_kernel(xt_ref, gt_ref, kcol_ref, krow_ref, gain_ref, wqkvT_ref, wqkv_ref, wp_ref,
                  gs_ref, gqkvT_ref, gproj_ref, ggain_ref, qkv_s, ga_s, drow_s):
    f32 = jnp.float32
    bf16 = jnp.bfloat16
    w = pl.program_id(0)

    @pl.when(w == 0)
    def _():
        gqkvT_ref[...] = jnp.zeros_like(gqkvT_ref)
        gproj_ref[...] = jnp.zeros_like(gproj_ref)
        ggain_ref[...] = jnp.zeros_like(ggain_ref)

    gain = gain_ref[...]
    x = xt_ref[0].astype(f32)
    row_mean = jnp.mean(x, axis=0, keepdims=True)
    centred = x - row_mean
    inv_std = lax.rsqrt(jnp.mean(centred * centred, axis=0, keepdims=True) + 1e-05)
    x_hat = centred * inv_std
    normed = (x_hat * gain).astype(bf16)
    qkv_t = jnp.dot(wqkvT_ref[...], normed, preferred_element_type=f32)
    qkv_s[...] = qkv_t.astype(bf16).astype(f32)
    g = gt_ref[0]
    ga_t = jnp.dot(wp_ref[...], g, preferred_element_type=f32)
    ga_s[...] = ga_t.astype(bf16).astype(f32)
    allowed = kcol_ref[0] == krow_ref[0]
    nt = (((1,), (1,)), ((), ()))

    def head_step(h, carry):
        qo = pl.multiple_of(h * HEAD, HEAD)
        q_t = qkv_s[pl.ds(qo, HEAD), :]
        k_t = qkv_s[pl.ds(qo + C, HEAD), :]
        v_t = qkv_s[pl.ds(qo + 2 * C, HEAD), :]
        ga_th = ga_s[pl.ds(qo, HEAD), :]
        q = q_t.T.astype(bf16)
        scores = jnp.dot(q, k_t.astype(bf16), preferred_element_type=f32) * SCALE
        weights = jnp.where(allowed, jnp.exp(scores), 0.0)
        probs = weights / jnp.sum(weights, axis=1, keepdims=True)
        probs_bf = probs.astype(bf16)
        att_t = lax.dot_general(v_t.astype(bf16), probs_bf, nt, preferred_element_type=f32)
        att_t = att_t.astype(bf16)
        gproj_ref[pl.ds(qo, HEAD), :] += lax.dot_general(att_t, g, nt, preferred_element_type=f32)
        ga = ga_th.T.astype(bf16)
        grad_probs = jnp.dot(ga, v_t.astype(bf16), preferred_element_type=f32)
        dv_t = jnp.dot(ga_th.astype(bf16), probs_bf, preferred_element_type=f32)
        row_total = jnp.sum(probs * grad_probs, axis=1, keepdims=True)
        grad_scores = (probs * (grad_probs - row_total) * SCALE).astype(bf16)
        dq_t = lax.dot_general(k_t.astype(bf16), grad_scores, nt, preferred_element_type=f32)
        dk_t = jnp.dot(q_t.astype(bf16), grad_scores, preferred_element_type=f32)
        drow_s[pl.ds(qo, HEAD), :] = dq_t.astype(bf16).astype(f32)
        drow_s[pl.ds(qo + C, HEAD), :] = dk_t.astype(bf16).astype(f32)
        drow_s[pl.ds(qo + 2 * C, HEAD), :] = dv_t.astype(bf16).astype(f32)
        return carry

    lax.fori_loop(0, HEADS, head_step, 0)
    rows_t = drow_s[...].astype(bf16)
    gqkvT_ref[...] += lax.dot_general(rows_t, normed, nt, preferred_element_type=f32)
    grad_normed = jnp.dot(wqkv_ref[...], rows_t, preferred_element_type=f32)
    ggain_ref[...] += jnp.sum(grad_normed * x_hat, axis=1, keepdims=True)
    scaled = grad_normed * gain
    grad_shifted = inv_std * (
        scaled
        - jnp.mean(scaled, axis=0, keepdims=True)
        - x_hat * jnp.mean(scaled * x_hat, axis=0, keepdims=True)
    )
    gs_ref[0] = grad_shifted.astype(bf16)


def window_grads(xt, gt, kcol, krow, gain_col, wqkv_t, wqkv, wp):
    n_win = xt.shape[0]
    win_spec = pl.BlockSpec((1, C, CELLS), lambda w: (w, 0, 0))
    full = lambda shape: pl.BlockSpec(shape, lambda w: (0,) * len(shape))
    return pl.pallas_call(
        window_kernel,
        grid=(n_win,),
        in_specs=[
            win_spec,
            win_spec,
            pl.BlockSpec((1, CELLS, 1), lambda w: (w, 0, 0)),
            pl.BlockSpec((1, 1, CELLS), lambda w: (w, 0, 0)),
            full((C, 1)),
            full((3 * C, C)),
            full((C, 3 * C)),
            full((C, C)),
        ],
        out_specs=[
            win_spec,
            full((3 * C, C)),
            full((C, C)),
            full((C, 1)),
        ],
        out_shape=[
            jax.ShapeDtypeStruct((n_win, C, CELLS), jnp.bfloat16),
            jax.ShapeDtypeStruct((3 * C, C), jnp.float32),
            jax.ShapeDtypeStruct((C, C), jnp.float32),
            jax.ShapeDtypeStruct((C, 1), jnp.float32),
        ],
        scratch_shapes=[
            pltpu.VMEM((3 * C, CELLS), jnp.float32),
            pltpu.VMEM((C, CELLS), jnp.float32),
            pltpu.VMEM((3 * C, CELLS), jnp.float32),
        ],
        compiler_params=pltpu.CompilerParams(dimension_semantics=("arbitrary",)),
    )(xt, gt, kcol, krow, gain_col, wqkv_t, wqkv, wp)


def ahead_first(both_arrays):
    arrived = passed_along((both_arrays[0][:SHIFT], both_arrays[1][:SHIFT]), "gx", -1)
    return (
        jnp.concatenate([both_arrays[0][SHIFT:], arrived[0]], axis=0),
        jnp.concatenate([both_arrays[1][SHIFT:], arrived[1]], axis=0),
    )


def ahead_second(both_arrays):
    arrived = passed_along((both_arrays[0][:, :SHIFT], both_arrays[1][:, :SHIFT]), ("gy", "gz"), -1)
    return (
        jnp.concatenate([both_arrays[0][:, SHIFT:], arrived[0]], axis=1),
        jnp.concatenate([both_arrays[1][:, SHIFT:], arrived[1]], axis=1),
    )


def back_first(gradient):
    arrived = passed_along(gradient[-SHIFT:], "gx", 1)
    return jnp.concatenate([arrived, gradient[:-SHIFT]], axis=0)


def back_second(gradient):
    arrived = passed_along(gradient[:, -SHIFT:], ("gy", "gz"), 1)
    return jnp.concatenate([arrived, gradient[:, :-SHIFT]], axis=1)


def per_device(tokens, grads_out, labels, ln_gain, qkv_weight, proj_weight):
    brick_a, brick_b = (tokens.shape[0], tokens.shape[1])
    brick_c = NZ
    channels = C
    both_arrays = (tokens, grads_out)
    both_arrays = ahead_second(ahead_first(both_arrays))
    shifted_tokens = jnp.roll(
        both_arrays[0].reshape(brick_a, brick_b, brick_c, channels), -SHIFT, axis=2
    )
    shifted_grads = jnp.roll(
        both_arrays[1].reshape(brick_a, brick_b, brick_c, channels), -SHIFT, axis=2
    )
    extent_a = brick_a * lax.axis_size("gx")
    extent_b = brick_b * lax.axis_size(("gy", "gz"))
    first_index = lax.axis_index("gx") * brick_a + jnp.arange(brick_a, dtype=jnp.int32)
    second_index = lax.axis_index(("gy", "gz")) * brick_b + jnp.arange(brick_b, dtype=jnp.int32)
    wrap_first = (first_index >= extent_a - SHIFT).astype(jnp.int32)
    wrap_second = (second_index >= extent_b - SHIFT).astype(jnp.int32)
    wrap_third = (jnp.arange(brick_c, dtype=jnp.int32) >= brick_c - SHIFT).astype(jnp.int32)
    region = (
        wrap_first[:, None, None] * 4 + wrap_second[None, :, None] * 2 + wrap_third[None, None, :]
    )
    mask_key = to_windows_key(labels * 8 + region)

    grad_windows, qkv_grad_t, proj_grad, gain_grad = window_grads(
        to_windows_cm(shifted_tokens),
        to_windows_cm(shifted_grads),
        mask_key[:, :, None],
        mask_key[:, None, :],
        ln_gain.reshape(channels, 1),
        qkv_weight.T,
        qkv_weight,
        proj_weight,
    )
    qkv_grad_t, proj_grad, gain_grad = lax.psum(
        (qkv_grad_t, proj_grad, gain_grad), ("gx", "gy", "gz")
    )
    qkv_grad = qkv_grad_t.T
    grad_branch = jnp.roll(from_windows_cm(grad_windows, brick_a, brick_b, brick_c), SHIFT, axis=2)
    grad_branch = grad_branch.reshape(brick_a, brick_b, brick_c * channels)
    grad_branch = back_first(back_second(grad_branch))
    grad_tokens = (grads_out.astype(jnp.float32) + grad_branch.astype(jnp.float32)).astype(
        jnp.bfloat16
    )
    return (grad_tokens, gain_grad.reshape(-1), qkv_grad.reshape(-1), proj_grad.reshape(-1))


def solution(mesh):
    return jax.shard_map(
        per_device,
        mesh=mesh,
        in_specs=(
            P("gx", ("gy", "gz"), None),
            P("gx", ("gy", "gz"), None),
            P("gx", ("gy", "gz"), None),
            P(),
            P(),
            P(),
        ),
        out_specs=(P("gx", ("gy", "gz"), None), P(), P(), P()),
        check_vma=False,
    )
```

```python
import jax
import jax.numpy as jnp
from jax import lax
from jax.experimental import pallas as pl
from jax.experimental.pallas import tpu as pltpu
from jax.sharding import PartitionSpec as P

HEADS = 6
C = 192
WIN = 8
SHIFT = 4
NZ = 16
CELLS = WIN**3
HEAD = C // HEADS
SCALE = HEAD ** (-0.5)


def passed_along(block, axis, distance):
    devices = range(lax.axis_size(axis))
    route = [((i - distance) % len(devices), i) for i in devices]
    return lax.ppermute(block, axis, route)


def to_windows_cm(values):
    extent_a, extent_b, extent_c, ch = values.shape
    shaped = values.reshape(extent_a // WIN, WIN, extent_b // WIN, WIN, extent_c // WIN, WIN, ch)
    return shaped.transpose(0, 2, 4, 6, 1, 3, 5).reshape(-1, ch, CELLS)


def from_windows_cm(values, extent_a, extent_b, extent_c):
    ch = values.shape[1]
    shaped = values.reshape(extent_a // WIN, extent_b // WIN, extent_c // WIN, ch, WIN, WIN, WIN)
    return shaped.transpose(0, 4, 1, 5, 2, 6, 3).reshape(extent_a, extent_b, extent_c, ch)


def to_windows_key(values):
    extent_a, extent_b, extent_c = values.shape
    shaped = values.reshape(extent_a // WIN, WIN, extent_b // WIN, WIN, extent_c // WIN, WIN)
    return shaped.transpose(0, 2, 4, 1, 3, 5).reshape(-1, CELLS)


def window_kernel(xt_ref, gt_ref, kcol_ref, krow_ref, gain_ref, wqkvT_ref, wqkv_ref, wp_ref,
                  gs_ref, gqkvT_ref, gproj_ref, ggain_ref, qkv_s, ga_s, drow_s):
    f32 = jnp.float32
    bf16 = jnp.bfloat16
    w = pl.program_id(0)

    @pl.when(w == 0)
    def _():
        gqkvT_ref[...] = jnp.zeros_like(gqkvT_ref)
        gproj_ref[...] = jnp.zeros_like(gproj_ref)
        ggain_ref[...] = jnp.zeros_like(ggain_ref)

    gain = gain_ref[...]
    x = xt_ref[0].astype(f32)
    row_mean = jnp.mean(x, axis=0, keepdims=True)
    centred = x - row_mean
    inv_std = lax.rsqrt(jnp.mean(centred * centred, axis=0, keepdims=True) + 1e-05)
    x_hat = centred * inv_std
    normed = (x_hat * gain).astype(bf16)
    qkv_t = jnp.dot(wqkvT_ref[...], normed, preferred_element_type=f32)
    qkv_s[...] = qkv_t.astype(bf16).astype(f32)
    g = gt_ref[0]
    ga_t = jnp.dot(wp_ref[...], g, preferred_element_type=f32)
    ga_s[...] = ga_t.astype(bf16).astype(f32)
    allowed = kcol_ref[0] == krow_ref[0]
    nt = (((1,), (1,)), ((), ()))

    def head_step(h, carry):
        qo = pl.multiple_of(h * HEAD, HEAD)
        q_t = qkv_s[pl.ds(qo, HEAD), :]
        k_t = qkv_s[pl.ds(qo + C, HEAD), :]
        v_t = qkv_s[pl.ds(qo + 2 * C, HEAD), :]
        ga_th = ga_s[pl.ds(qo, HEAD), :]
        q = q_t.T.astype(bf16)
        scores = jnp.dot(q, k_t.astype(bf16), preferred_element_type=f32) * SCALE
        weights = jnp.where(allowed, jnp.exp(scores), 0.0)
        probs = weights / jnp.sum(weights, axis=1, keepdims=True)
        probs_bf = probs.astype(bf16)
        att_t = lax.dot_general(v_t.astype(bf16), probs_bf, nt, preferred_element_type=f32)
        att_t = att_t.astype(bf16)
        gproj_ref[pl.ds(qo, HEAD), :] += lax.dot_general(att_t, g, nt, preferred_element_type=f32)
        ga = ga_th.T.astype(bf16)
        grad_probs = jnp.dot(ga, v_t.astype(bf16), preferred_element_type=f32)
        dv_t = jnp.dot(ga_th.astype(bf16), probs_bf, preferred_element_type=f32)
        row_total = jnp.sum(probs * grad_probs, axis=1, keepdims=True)
        grad_scores = (probs * (grad_probs - row_total) * SCALE).astype(bf16)
        dq_t = lax.dot_general(k_t.astype(bf16), grad_scores, nt, preferred_element_type=f32)
        dk_t = jnp.dot(q_t.astype(bf16), grad_scores, preferred_element_type=f32)
        drow_s[pl.ds(qo, HEAD), :] = dq_t.astype(bf16).astype(f32)
        drow_s[pl.ds(qo + C, HEAD), :] = dk_t.astype(bf16).astype(f32)
        drow_s[pl.ds(qo + 2 * C, HEAD), :] = dv_t.astype(bf16).astype(f32)
        return carry

    lax.fori_loop(0, HEADS, head_step, 0)
    rows_t = drow_s[...].astype(bf16)
    gqkvT_ref[...] += lax.dot_general(rows_t, normed, nt, preferred_element_type=f32)
    grad_normed = jnp.dot(wqkv_ref[...], rows_t, preferred_element_type=f32)
    ggain_ref[...] += jnp.sum(grad_normed * x_hat, axis=1, keepdims=True)
    scaled = grad_normed * gain
    grad_shifted = inv_std * (
        scaled
        - jnp.mean(scaled, axis=0, keepdims=True)
        - x_hat * jnp.mean(scaled * x_hat, axis=0, keepdims=True)
    )
    gs_ref[0] = grad_shifted.astype(bf16)


def window_grads(xt, gt, kcol, krow, gain_col, wqkv_t, wqkv, wp):
    n_win = xt.shape[0]
    win_spec = pl.BlockSpec((1, C, CELLS), lambda w: (w, 0, 0))
    full = lambda shape: pl.BlockSpec(shape, lambda w: (0,) * len(shape))
    return pl.pallas_call(
        window_kernel,
        grid=(n_win,),
        in_specs=[
            win_spec,
            win_spec,
            pl.BlockSpec((1, CELLS, 1), lambda w: (w, 0, 0)),
            pl.BlockSpec((1, 1, CELLS), lambda w: (w, 0, 0)),
            full((C, 1)),
            full((3 * C, C)),
            full((C, 3 * C)),
            full((C, C)),
        ],
        out_specs=[
            win_spec,
            full((3 * C, C)),
            full((C, C)),
            full((C, 1)),
        ],
        out_shape=[
            jax.ShapeDtypeStruct((n_win, C, CELLS), jnp.bfloat16),
            jax.ShapeDtypeStruct((3 * C, C), jnp.float32),
            jax.ShapeDtypeStruct((C, C), jnp.float32),
            jax.ShapeDtypeStruct((C, 1), jnp.float32),
        ],
        scratch_shapes=[
            pltpu.VMEM((3 * C, CELLS), jnp.float32),
            pltpu.VMEM((C, CELLS), jnp.float32),
            pltpu.VMEM((3 * C, CELLS), jnp.float32),
        ],
        compiler_params=pltpu.CompilerParams(dimension_semantics=("arbitrary",)),
    )(xt, gt, kcol, krow, gain_col, wqkv_t, wqkv, wp)


SUM_AXES = ("gy", "gx", "gz")


def swapped(block, axis, distance):
    return lax.ppermute(block, axis, [(i, i ^ distance) for i in range(lax.axis_size(axis))])


def summed_everywhere(parts):
    sizes = [lax.axis_size(axis) for axis in SUM_AXES]
    if any(size & (size - 1) for size in sizes):
        return lax.psum(parts, SUM_AXES)
    flat = jnp.concatenate([part.reshape(-1) for part in parts])
    total = flat.shape[0]
    devices = 1
    for size in sizes:
        devices *= size
    padded = -(-total // devices) * devices
    values = jnp.pad(flat, (0, padded - total))
    steps = []
    for axis, size in zip(SUM_AXES, sizes):
        distance = 1
        while distance < size:
            bit = (lax.axis_index(axis) // distance) % 2
            half = values.shape[0] // 2
            keep = lax.dynamic_slice_in_dim(values, bit * half, half)
            send = lax.dynamic_slice_in_dim(values, (1 - bit) * half, half)
            values = keep + swapped(send, axis, distance)
            steps.append((axis, distance))
            distance *= 2
    for axis, distance in reversed(steps):
        bit = (lax.axis_index(axis) // distance) % 2
        other = swapped(values, axis, distance)
        values = jnp.where(
            bit == 0, jnp.concatenate([values, other]), jnp.concatenate([other, values])
        )
    out = []
    start = 0
    for part in parts:
        out.append(values[start : start + part.size].reshape(part.shape))
        start += part.size
    return tuple(out)


def ahead_first(both_arrays):
    arrived = passed_along((both_arrays[0][:SHIFT], both_arrays[1][:SHIFT]), "gx", -1)
    return (
        jnp.concatenate([both_arrays[0][SHIFT:], arrived[0]], axis=0),
        jnp.concatenate([both_arrays[1][SHIFT:], arrived[1]], axis=0),
    )


def ahead_second(both_arrays):
    arrived = passed_along((both_arrays[0][:, :SHIFT], both_arrays[1][:, :SHIFT]), ("gy", "gz"), -1)
    return (
        jnp.concatenate([both_arrays[0][:, SHIFT:], arrived[0]], axis=1),
        jnp.concatenate([both_arrays[1][:, SHIFT:], arrived[1]], axis=1),
    )


def back_first(gradient):
    arrived = passed_along(gradient[-SHIFT:], "gx", 1)
    return jnp.concatenate([arrived, gradient[:-SHIFT]], axis=0)


def back_second(gradient):
    arrived = passed_along(gradient[:, -SHIFT:], ("gy", "gz"), 1)
    return jnp.concatenate([arrived, gradient[:, :-SHIFT]], axis=1)


def per_device(tokens, grads_out, labels, ln_gain, qkv_weight, proj_weight):
    brick_a, brick_b = (tokens.shape[0], tokens.shape[1])
    brick_c = NZ
    channels = C
    both_arrays = (tokens, grads_out)
    both_arrays = ahead_second(ahead_first(both_arrays))
    shifted_tokens = jnp.roll(
        both_arrays[0].reshape(brick_a, brick_b, brick_c, channels), -SHIFT, axis=2
    )
    shifted_grads = jnp.roll(
        both_arrays[1].reshape(brick_a, brick_b, brick_c, channels), -SHIFT, axis=2
    )
    extent_a = brick_a * lax.axis_size("gx")
    extent_b = brick_b * lax.axis_size(("gy", "gz"))
    first_index = lax.axis_index("gx") * brick_a + jnp.arange(brick_a, dtype=jnp.int32)
    second_index = lax.axis_index(("gy", "gz")) * brick_b + jnp.arange(brick_b, dtype=jnp.int32)
    wrap_first = (first_index >= extent_a - SHIFT).astype(jnp.int32)
    wrap_second = (second_index >= extent_b - SHIFT).astype(jnp.int32)
    wrap_third = (jnp.arange(brick_c, dtype=jnp.int32) >= brick_c - SHIFT).astype(jnp.int32)
    region = (
        wrap_first[:, None, None] * 4 + wrap_second[None, :, None] * 2 + wrap_third[None, None, :]
    )
    mask_key = to_windows_key(labels * 8 + region)

    grad_windows, qkv_grad_t, proj_grad, gain_grad = window_grads(
        to_windows_cm(shifted_tokens),
        to_windows_cm(shifted_grads),
        mask_key[:, :, None],
        mask_key[:, None, :],
        ln_gain.reshape(channels, 1),
        qkv_weight.T,
        qkv_weight,
        proj_weight,
    )
    qkv_grad_t, proj_grad, gain_grad = summed_everywhere((qkv_grad_t, proj_grad, gain_grad))
    qkv_grad = qkv_grad_t.T
    grad_branch = jnp.roll(from_windows_cm(grad_windows, brick_a, brick_b, brick_c), SHIFT, axis=2)
    grad_branch = grad_branch.reshape(brick_a, brick_b, brick_c * channels)
    grad_branch = back_first(back_second(grad_branch))
    grad_tokens = (grads_out.astype(jnp.float32) + grad_branch.astype(jnp.float32)).astype(
        jnp.bfloat16
    )
    return (grad_tokens, gain_grad.reshape(-1), qkv_grad.reshape(-1), proj_grad.reshape(-1))


def solution(mesh):
    return jax.shard_map(
        per_device,
        mesh=mesh,
        in_specs=(
            P("gx", ("gy", "gz"), None),
            P("gx", ("gy", "gz"), None),
            P("gx", ("gy", "gz"), None),
            P(),
            P(),
            P(),
        ),
        out_specs=(P("gx", ("gy", "gz"), None), P(), P(), P()),
        check_vma=False,
    )
```

```python
import jax
import jax.numpy as jnp
from jax import lax
from jax.experimental import pallas as pl
from jax.experimental.pallas import tpu as pltpu
from jax.sharding import PartitionSpec as P

HEADS = 6
C = 192
WIN = 8
SHIFT = 4
NZ = 16
CELLS = WIN**3
HEAD = C // HEADS
SCALE = HEAD ** (-0.5)


def passed_along(block, axis, distance):
    devices = range(lax.axis_size(axis))
    route = [((i - distance) % len(devices), i) for i in devices]
    return lax.ppermute(block, axis, route)


def to_windows_cm(values):
    extent_a, extent_b, extent_c, ch = values.shape
    shaped = values.reshape(extent_a // WIN, WIN, extent_b // WIN, WIN, extent_c // WIN, WIN, ch)
    return shaped.transpose(0, 2, 4, 6, 1, 3, 5).reshape(-1, ch, CELLS)


def from_windows_cm(values, extent_a, extent_b, extent_c):
    ch = values.shape[1]
    shaped = values.reshape(extent_a // WIN, extent_b // WIN, extent_c // WIN, ch, WIN, WIN, WIN)
    return shaped.transpose(0, 4, 1, 5, 2, 6, 3).reshape(extent_a, extent_b, extent_c, ch)


def to_windows_key(values):
    extent_a, extent_b, extent_c = values.shape
    shaped = values.reshape(extent_a // WIN, WIN, extent_b // WIN, WIN, extent_c // WIN, WIN)
    return shaped.transpose(0, 2, 4, 1, 3, 5).reshape(-1, CELLS)


def window_kernel(xt_ref, gt_ref, kcol_ref, krow_ref, gain_ref, wqkvT_ref, wqkv_ref, wp_ref,
                  gs_ref, gqkvT_ref, gproj_ref, ggain_ref, qkv_s, ga_s, drow_s):
    f32 = jnp.float32
    bf16 = jnp.bfloat16
    w = pl.program_id(0)

    @pl.when(w == 0)
    def _():
        gqkvT_ref[...] = jnp.zeros_like(gqkvT_ref)
        gproj_ref[...] = jnp.zeros_like(gproj_ref)
        ggain_ref[...] = jnp.zeros_like(ggain_ref)

    gain = gain_ref[...]
    x = xt_ref[0].astype(f32)
    row_mean = jnp.mean(x, axis=0, keepdims=True)
    centred = x - row_mean
    inv_std = lax.rsqrt(jnp.mean(centred * centred, axis=0, keepdims=True) + 1e-05)
    x_hat = centred * inv_std
    normed = (x_hat * gain).astype(bf16)
    qkv_t = jnp.dot(wqkvT_ref[...], normed, preferred_element_type=f32)
    qkv_s[...] = qkv_t.astype(bf16).astype(f32)
    g = gt_ref[0]
    ga_t = jnp.dot(wp_ref[...], g, preferred_element_type=f32)
    ga_s[...] = ga_t.astype(bf16).astype(f32)
    allowed = kcol_ref[0] == krow_ref[0]
    nt = (((1,), (1,)), ((), ()))

    def head_step(h, carry):
        qo = pl.multiple_of(h * HEAD, HEAD)
        q_t = qkv_s[pl.ds(qo, HEAD), :]
        k_t = qkv_s[pl.ds(qo + C, HEAD), :]
        v_t = qkv_s[pl.ds(qo + 2 * C, HEAD), :]
        ga_th = ga_s[pl.ds(qo, HEAD), :]
        q = q_t.T.astype(bf16)
        scores = jnp.dot(q, k_t.astype(bf16), preferred_element_type=f32) * SCALE
        weights = jnp.where(allowed, jnp.exp(scores), 0.0)
        probs = weights / jnp.sum(weights, axis=1, keepdims=True)
        probs_bf = probs.astype(bf16)
        att_t = lax.dot_general(v_t.astype(bf16), probs_bf, nt, preferred_element_type=f32)
        att_t = att_t.astype(bf16)
        gproj_ref[pl.ds(qo, HEAD), :] += lax.dot_general(att_t, g, nt, preferred_element_type=f32)
        ga = ga_th.T.astype(bf16)
        grad_probs = jnp.dot(ga, v_t.astype(bf16), preferred_element_type=f32)
        dv_t = jnp.dot(ga_th.astype(bf16), probs_bf, preferred_element_type=f32)
        row_total = jnp.sum(probs * grad_probs, axis=1, keepdims=True)
        grad_scores = (probs * (grad_probs - row_total) * SCALE).astype(bf16)
        dq_t = lax.dot_general(k_t.astype(bf16), grad_scores, nt, preferred_element_type=f32)
        dk_t = jnp.dot(q_t.astype(bf16), grad_scores, preferred_element_type=f32)
        drow_s[pl.ds(qo, HEAD), :] = dq_t.astype(bf16).astype(f32)
        drow_s[pl.ds(qo + C, HEAD), :] = dk_t.astype(bf16).astype(f32)
        drow_s[pl.ds(qo + 2 * C, HEAD), :] = dv_t.astype(bf16).astype(f32)
        return carry

    lax.fori_loop(0, HEADS, head_step, 0)
    rows_t = drow_s[...].astype(bf16)
    gqkvT_ref[...] += lax.dot_general(rows_t, normed, nt, preferred_element_type=f32)
    grad_normed = jnp.dot(wqkv_ref[...], rows_t, preferred_element_type=f32)
    ggain_ref[...] += jnp.sum(grad_normed * x_hat, axis=1, keepdims=True)
    scaled = grad_normed * gain
    grad_shifted = inv_std * (
        scaled
        - jnp.mean(scaled, axis=0, keepdims=True)
        - x_hat * jnp.mean(scaled * x_hat, axis=0, keepdims=True)
    )
    gs_ref[0] = grad_shifted.astype(bf16)


def window_grads(xt, gt, kcol, krow, gain_col, wqkv_t, wqkv, wp):
    n_win = xt.shape[0]
    win_spec = pl.BlockSpec((1, C, CELLS), lambda w: (w, 0, 0))
    full = lambda shape: pl.BlockSpec(shape, lambda w: (0,) * len(shape))
    return pl.pallas_call(
        window_kernel,
        grid=(n_win,),
        in_specs=[
            win_spec,
            win_spec,
            pl.BlockSpec((1, CELLS, 1), lambda w: (w, 0, 0)),
            pl.BlockSpec((1, 1, CELLS), lambda w: (w, 0, 0)),
            full((C, 1)),
            full((3 * C, C)),
            full((C, 3 * C)),
            full((C, C)),
        ],
        out_specs=[
            win_spec,
            full((3 * C, C)),
            full((C, C)),
            full((C, 1)),
        ],
        out_shape=[
            jax.ShapeDtypeStruct((n_win, C, CELLS), jnp.bfloat16),
            jax.ShapeDtypeStruct((3 * C, C), jnp.float32),
            jax.ShapeDtypeStruct((C, C), jnp.float32),
            jax.ShapeDtypeStruct((C, 1), jnp.float32),
        ],
        scratch_shapes=[
            pltpu.VMEM((3 * C, CELLS), jnp.float32),
            pltpu.VMEM((C, CELLS), jnp.float32),
            pltpu.VMEM((3 * C, CELLS), jnp.float32),
        ],
        compiler_params=pltpu.CompilerParams(dimension_semantics=("arbitrary",)),
    )(xt, gt, kcol, krow, gain_col, wqkv_t, wqkv, wp)


SUM_AXES = ("gy", "gx", "gz")


def swapped(block, axis, distance):
    return lax.ppermute(block, axis, [(i, i ^ distance) for i in range(lax.axis_size(axis))])


def summed_everywhere(parts):
    sizes = [lax.axis_size(axis) for axis in SUM_AXES]
    if any(size & (size - 1) for size in sizes):
        return lax.psum(parts, SUM_AXES)
    flat = jnp.concatenate([part.reshape(-1) for part in parts])
    total = flat.shape[0]
    devices = 1
    for size in sizes:
        devices *= size
    padded = -(-total // devices) * devices
    values = jnp.pad(flat, (0, padded - total))
    steps = []
    for axis, size in zip(SUM_AXES, sizes):
        distance = 1
        while distance < size:
            bit = (lax.axis_index(axis) // distance) % 2
            half = values.shape[0] // 2
            keep = lax.dynamic_slice_in_dim(values, bit * half, half)
            send = lax.dynamic_slice_in_dim(values, (1 - bit) * half, half)
            values = keep + swapped(send, axis, distance)
            steps.append((axis, distance))
            distance *= 2
    for axis, distance in reversed(steps):
        bit = (lax.axis_index(axis) // distance) % 2
        other = swapped(values, axis, distance)
        values = jnp.where(
            bit == 0, jnp.concatenate([values, other]), jnp.concatenate([other, values])
        )
    out = []
    start = 0
    for part in parts:
        out.append(values[start : start + part.size].reshape(part.shape))
        start += part.size
    return tuple(out)


def halo_route(distance_a, distance_b):
    size_a = lax.axis_size("gx")
    size_b = lax.axis_size(("gy", "gz"))
    route = []
    for ia in range(size_a):
        for ib in range(size_b):
            target = ((ia + distance_a) % size_a) * size_b + (ib + distance_b) % size_b
            route.append((ia * size_b + ib, target))
    return route


def moved(block, distance_a, distance_b):
    return lax.ppermute(block, ("gx", "gy", "gz"), halo_route(distance_a, distance_b))


def shifted_block(both):
    from_a = moved(both[:, :SHIFT, SHIFT:], -1, 0)
    from_b = moved(both[:, SHIFT:, :SHIFT], 0, -1)
    from_ab = moved(both[:, :SHIFT, :SHIFT], -1, -1)
    upper = jnp.concatenate([both[:, SHIFT:, SHIFT:], from_b], axis=2)
    lower = jnp.concatenate([from_a, from_ab], axis=2)
    return jnp.concatenate([upper, lower], axis=1)


def unshifted_sum(grads_out, grad_shifted):
    to_a = moved(grad_shifted[-SHIFT:, :-SHIFT], 1, 0)
    to_b = moved(grad_shifted[:-SHIFT, -SHIFT:], 0, 1)
    to_ab = moved(grad_shifted[-SHIFT:, -SHIFT:], 1, 1)
    upper = jnp.concatenate([to_ab, to_a], axis=1)
    lower = jnp.concatenate([to_b, grad_shifted[:-SHIFT, :-SHIFT]], axis=1)
    branch = jnp.concatenate([upper, lower], axis=0)
    return (grads_out.astype(jnp.float32) + branch.astype(jnp.float32)).astype(jnp.bfloat16)


def per_device(tokens, grads_out, labels, ln_gain, qkv_weight, proj_weight):
    brick_a, brick_b = (tokens.shape[0], tokens.shape[1])
    brick_c = NZ
    channels = C
    both = shifted_block(jnp.stack([tokens, grads_out]))
    both = jnp.roll(both.reshape(2, brick_a, brick_b, brick_c, channels), -SHIFT, axis=3)
    extent_a = brick_a * lax.axis_size("gx")
    extent_b = brick_b * lax.axis_size(("gy", "gz"))
    first_index = lax.axis_index("gx") * brick_a + jnp.arange(brick_a, dtype=jnp.int32)
    second_index = lax.axis_index(("gy", "gz")) * brick_b + jnp.arange(brick_b, dtype=jnp.int32)
    wrap_first = (first_index >= extent_a - SHIFT).astype(jnp.int32)
    wrap_second = (second_index >= extent_b - SHIFT).astype(jnp.int32)
    wrap_third = (jnp.arange(brick_c, dtype=jnp.int32) >= brick_c - SHIFT).astype(jnp.int32)
    region = (
        wrap_first[:, None, None] * 4 + wrap_second[None, :, None] * 2 + wrap_third[None, None, :]
    )
    mask_key = to_windows_key(labels * 8 + region)

    grad_windows, qkv_grad_t, proj_grad, gain_grad = window_grads(
        to_windows_cm(both[0]),
        to_windows_cm(both[1]),
        mask_key[:, :, None],
        mask_key[:, None, :],
        ln_gain.reshape(channels, 1),
        qkv_weight.T,
        qkv_weight,
        proj_weight,
    )
    qkv_grad_t, proj_grad, gain_grad = summed_everywhere((qkv_grad_t, proj_grad, gain_grad))
    qkv_grad = qkv_grad_t.T
    grad_branch = jnp.roll(from_windows_cm(grad_windows, brick_a, brick_b, brick_c), SHIFT, axis=2)
    grad_branch = grad_branch.reshape(brick_a, brick_b, brick_c * channels)
    grad_tokens = unshifted_sum(grads_out, grad_branch)
    return (grad_tokens, gain_grad.reshape(-1), qkv_grad.reshape(-1), proj_grad.reshape(-1))


def solution(mesh):
    return jax.shard_map(
        per_device,
        mesh=mesh,
        in_specs=(
            P("gx", ("gy", "gz"), None),
            P("gx", ("gy", "gz"), None),
            P("gx", ("gy", "gz"), None),
            P(),
            P(),
            P(),
        ),
        out_specs=(P("gx", ("gy", "gz"), None), P(), P(), P()),
        check_vma=False,
    )
```

```python
import jax
import jax.numpy as jnp
from jax import lax
from jax.experimental import pallas as pl
from jax.experimental.pallas import tpu as pltpu
from jax.sharding import PartitionSpec as P

HEADS = 6
C = 192
WIN = 8
SHIFT = 4
NZ = 16
CELLS = WIN**3
HEAD = C // HEADS
SCALE = HEAD ** (-0.5)


def passed_along(block, axis, distance):
    devices = range(lax.axis_size(axis))
    route = [((i - distance) % len(devices), i) for i in devices]
    return lax.ppermute(block, axis, route)


def to_windows_cm(values):
    extent_a, extent_b, extent_c, ch = values.shape
    shaped = values.reshape(extent_a // WIN, WIN, extent_b // WIN, WIN, extent_c // WIN, WIN, ch)
    return shaped.transpose(0, 2, 4, 6, 1, 3, 5).reshape(-1, ch, CELLS)


def from_windows_cm(values, extent_a, extent_b, extent_c):
    ch = values.shape[1]
    shaped = values.reshape(extent_a // WIN, extent_b // WIN, extent_c // WIN, ch, WIN, WIN, WIN)
    return shaped.transpose(0, 4, 1, 5, 2, 6, 3).reshape(extent_a, extent_b, extent_c, ch)


def to_windows_key(values):
    extent_a, extent_b, extent_c = values.shape
    shaped = values.reshape(extent_a // WIN, WIN, extent_b // WIN, WIN, extent_c // WIN, WIN)
    return shaped.transpose(0, 2, 4, 5, 1, 3).reshape(-1, CELLS)


def window_kernel(both_ref, kcol_ref, krow_ref, gain_ref, wqkvT_ref, wqkv_ref, wp_ref,
                  gs_ref, gqkvT_ref, gproj_ref, ggain_ref, qkv_s, ga_s, drow_s):
    f32 = jnp.float32
    bf16 = jnp.bfloat16
    gqkvT_ref[...] = jnp.zeros_like(gqkvT_ref)
    gproj_ref[...] = jnp.zeros_like(gproj_ref)
    ggain_ref[...] = jnp.zeros_like(ggain_ref)
    gain = gain_ref[...]
    nt = (((1,), (1,)), ((), ()))
    pair = 2 * C
    n_pairs = NZ // 2

    def gathered(which, i, j, l):
        pieces = []
        for q in range(WIN // 2):
            p = (WIN // 2 * l + SHIFT // 2 + q) % n_pairs
            block = both_ref[which, pl.ds(i * WIN, WIN), :, pl.ds(p * pair, pair)].astype(f32)
            block = jnp.where(j == 0, block[:, :WIN], block[:, WIN:]).reshape(WIN * WIN, pair)
            pieces.append(block[:, :C])
            pieces.append(block[:, C:])
        return jnp.concatenate(pieces, axis=0).T

    def scattered(values_t, i, j, l):
        rows = values_t.T
        for q in range(WIN // 2):
            p = (WIN // 2 * l + SHIFT // 2 + q) % n_pairs
            even = rows[2 * q * WIN * WIN:(2 * q + 1) * WIN * WIN]
            odd = rows[(2 * q + 1) * WIN * WIN:(2 * q + 2) * WIN * WIN]
            block = jnp.concatenate([even, odd], axis=1).reshape(WIN, WIN, pair)
            gs_ref[pl.ds(i * WIN, WIN), pl.ds(pl.multiple_of(j * WIN, WIN), WIN), pl.ds(p * pair, pair)] = block

    def window(ij, l):
        i = ij // 2
        j = ij % 2
        w = ij * 2 + l
        x = gathered(0, i, j, l)
        row_mean = jnp.mean(x, axis=0, keepdims=True)
        centred = x - row_mean
        inv_std = lax.rsqrt(jnp.mean(centred * centred, axis=0, keepdims=True) + 1e-05)
        x_hat = centred * inv_std
        normed = (x_hat * gain).astype(bf16)
        qkv_t = jnp.dot(wqkvT_ref[...], normed, preferred_element_type=f32)
        qkv_s[...] = qkv_t.astype(bf16).astype(f32)
        g = gathered(1, i, j, l).astype(bf16)
        ga_t = jnp.dot(wp_ref[...], g, preferred_element_type=f32)
        ga_s[...] = ga_t.astype(bf16).astype(f32)
        allowed = kcol_ref[w] == krow_ref[w]

        def head_step(h, carry):
            qo = pl.multiple_of(h * HEAD, HEAD)
            q_t = qkv_s[pl.ds(qo, HEAD), :]
            k_t = qkv_s[pl.ds(qo + C, HEAD), :]
            v_t = qkv_s[pl.ds(qo + 2 * C, HEAD), :]
            ga_th = ga_s[pl.ds(qo, HEAD), :]
            q = q_t.T.astype(bf16)
            scores = jnp.dot(q, k_t.astype(bf16), preferred_element_type=f32) * SCALE
            weights = jnp.where(allowed, jnp.exp(scores), 0.0)
            probs = weights / jnp.sum(weights, axis=1, keepdims=True)
            probs_bf = probs.astype(bf16)
            att_t = lax.dot_general(v_t.astype(bf16), probs_bf, nt, preferred_element_type=f32)
            att_t = att_t.astype(bf16)
            gproj_ref[pl.ds(qo, HEAD), :] += lax.dot_general(
                att_t, g, nt, preferred_element_type=f32
            )
            ga = ga_th.T.astype(bf16)
            grad_probs = jnp.dot(ga, v_t.astype(bf16), preferred_element_type=f32)
            dv_t = jnp.dot(ga_th.astype(bf16), probs_bf, preferred_element_type=f32)
            row_total = jnp.sum(probs * grad_probs, axis=1, keepdims=True)
            grad_scores = (probs * (grad_probs - row_total) * SCALE).astype(bf16)
            dq_t = lax.dot_general(k_t.astype(bf16), grad_scores, nt, preferred_element_type=f32)
            dk_t = jnp.dot(q_t.astype(bf16), grad_scores, preferred_element_type=f32)
            drow_s[pl.ds(qo, HEAD), :] = dq_t.astype(bf16).astype(f32)
            drow_s[pl.ds(qo + C, HEAD), :] = dk_t.astype(bf16).astype(f32)
            drow_s[pl.ds(qo + 2 * C, HEAD), :] = dv_t.astype(bf16).astype(f32)
            return carry

        lax.fori_loop(0, HEADS, head_step, 0)
        rows_t = drow_s[...].astype(bf16)
        gqkvT_ref[...] += lax.dot_general(rows_t, normed, nt, preferred_element_type=f32)
        grad_normed = jnp.dot(wqkv_ref[...], rows_t, preferred_element_type=f32)
        ggain_ref[...] += jnp.sum(grad_normed * x_hat, axis=1, keepdims=True)
        scaled = grad_normed * gain
        grad_shifted = inv_std * (
            scaled
            - jnp.mean(scaled, axis=0, keepdims=True)
            - x_hat * jnp.mean(scaled * x_hat, axis=0, keepdims=True)
        )
        scattered(grad_shifted.astype(bf16).astype(f32), i, j, l)

    def block_step(ij, carry):
        for l in range(2):
            window(ij, l)
        return carry

    lax.fori_loop(0, 4, block_step, 0)


def window_grads(both, kcol, krow, gain_col, wqkv_t, wqkv, wp):
    extent_a, extent_b, width = both.shape[1:]
    return pl.pallas_call(
        window_kernel,
        out_shape=[
            jax.ShapeDtypeStruct((extent_a, extent_b, width), jnp.float32),
            jax.ShapeDtypeStruct((3 * C, C), jnp.float32),
            jax.ShapeDtypeStruct((C, C), jnp.float32),
            jax.ShapeDtypeStruct((C, 1), jnp.float32),
        ],
        scratch_shapes=[
            pltpu.VMEM((3 * C, CELLS), jnp.float32),
            pltpu.VMEM((C, CELLS), jnp.float32),
            pltpu.VMEM((3 * C, CELLS), jnp.float32),
        ],
    )(both, kcol, krow, gain_col, wqkv_t, wqkv, wp)


SUM_AXES = ("gy", "gx", "gz")


def swapped(block, axis, distance):
    return lax.ppermute(block, axis, [(i, i ^ distance) for i in range(lax.axis_size(axis))])


def summed_everywhere(parts):
    sizes = [lax.axis_size(axis) for axis in SUM_AXES]
    if any(size & (size - 1) for size in sizes):
        return lax.psum(parts, SUM_AXES)
    flat = jnp.concatenate([part.reshape(-1) for part in parts])
    total = flat.shape[0]
    devices = 1
    for size in sizes:
        devices *= size
    padded = -(-total // devices) * devices
    values = jnp.pad(flat, (0, padded - total))
    steps = []
    for axis, size in zip(SUM_AXES, sizes):
        distance = 1
        while distance < size:
            bit = (lax.axis_index(axis) // distance) % 2
            half = values.shape[0] // 2
            keep = lax.dynamic_slice_in_dim(values, bit * half, half)
            send = lax.dynamic_slice_in_dim(values, (1 - bit) * half, half)
            values = keep + swapped(send, axis, distance)
            steps.append((axis, distance))
            distance *= 2
    for axis, distance in reversed(steps):
        bit = (lax.axis_index(axis) // distance) % 2
        other = swapped(values, axis, distance)
        values = jnp.where(
            bit == 0, jnp.concatenate([values, other]), jnp.concatenate([other, values])
        )
    out = []
    start = 0
    for part in parts:
        out.append(values[start : start + part.size].reshape(part.shape))
        start += part.size
    return tuple(out)


def halo_route(distance_a, distance_b):
    size_a = lax.axis_size("gx")
    size_b = lax.axis_size(("gy", "gz"))
    route = []
    for ia in range(size_a):
        for ib in range(size_b):
            target = ((ia + distance_a) % size_a) * size_b + (ib + distance_b) % size_b
            route.append((ia * size_b + ib, target))
    return route


def moved(block, distance_a, distance_b):
    return lax.ppermute(block, ("gx", "gy", "gz"), halo_route(distance_a, distance_b))


def shifted_block(both):
    from_a = moved(both[:, :SHIFT, SHIFT:], -1, 0)
    from_b = moved(both[:, SHIFT:, :SHIFT], 0, -1)
    from_ab = moved(both[:, :SHIFT, :SHIFT], -1, -1)
    upper = jnp.concatenate([both[:, SHIFT:, SHIFT:], from_b], axis=2)
    lower = jnp.concatenate([from_a, from_ab], axis=2)
    return jnp.concatenate([upper, lower], axis=1)


def unshifted_sum(grads_out, grad_shifted):
    narrow = grad_shifted.astype(jnp.bfloat16)
    to_a = moved(narrow[-SHIFT:, :-SHIFT], 1, 0).astype(jnp.float32)
    to_b = moved(narrow[:-SHIFT, -SHIFT:], 0, 1).astype(jnp.float32)
    to_ab = moved(narrow[-SHIFT:, -SHIFT:], 1, 1).astype(jnp.float32)
    upper = jnp.concatenate([to_ab, to_a], axis=1)
    lower = jnp.concatenate([to_b, grad_shifted[:-SHIFT, :-SHIFT]], axis=1)
    branch = jnp.concatenate([upper, lower], axis=0)
    return (grads_out.astype(jnp.float32) + branch.astype(jnp.float32)).astype(jnp.bfloat16)


def per_device(tokens, grads_out, labels, ln_gain, qkv_weight, proj_weight):
    brick_a, brick_b = (tokens.shape[0], tokens.shape[1])
    brick_c = NZ
    channels = C
    both = shifted_block(jnp.stack([tokens, grads_out]))
    extent_a = brick_a * lax.axis_size("gx")
    extent_b = brick_b * lax.axis_size(("gy", "gz"))
    first_index = lax.axis_index("gx") * brick_a + jnp.arange(brick_a, dtype=jnp.int32)
    second_index = lax.axis_index(("gy", "gz")) * brick_b + jnp.arange(brick_b, dtype=jnp.int32)
    wrap_first = (first_index >= extent_a - SHIFT).astype(jnp.int32)
    wrap_second = (second_index >= extent_b - SHIFT).astype(jnp.int32)
    wrap_third = (jnp.arange(brick_c, dtype=jnp.int32) >= brick_c - SHIFT).astype(jnp.int32)
    region = (
        wrap_first[:, None, None] * 4 + wrap_second[None, :, None] * 2 + wrap_third[None, None, :]
    )
    mask_key = to_windows_key(labels * 8 + region)

    grad_branch, qkv_grad_t, proj_grad, gain_grad = window_grads(
        both,
        mask_key[:, :, None],
        mask_key[:, None, :],
        ln_gain.reshape(channels, 1),
        qkv_weight.T,
        qkv_weight,
        proj_weight,
    )
    qkv_grad_t, proj_grad, gain_grad = summed_everywhere((qkv_grad_t, proj_grad, gain_grad))
    qkv_grad = qkv_grad_t.T
    grad_tokens = unshifted_sum(grads_out, grad_branch)
    return (grad_tokens, gain_grad.reshape(-1), qkv_grad.reshape(-1), proj_grad.reshape(-1))


def solution(mesh):
    return jax.shard_map(
        per_device,
        mesh=mesh,
        in_specs=(
            P("gx", ("gy", "gz"), None),
            P("gx", ("gy", "gz"), None),
            P("gx", ("gy", "gz"), None),
            P(),
            P(),
            P(),
        ),
        out_specs=(P("gx", ("gy", "gz"), None), P(), P(), P()),
        check_vma=False,
    )
```

```python
import jax
import jax.numpy as jnp
from jax import lax
from jax.experimental import pallas as pl
from jax.experimental.pallas import tpu as pltpu
from jax.sharding import PartitionSpec as P

HEADS = 6
C = 192
WIN = 8
SHIFT = 4
NZ = 16
CELLS = WIN**3
HEAD = C // HEADS
SCALE = HEAD ** (-0.5)


def passed_along(block, axis, distance):
    devices = range(lax.axis_size(axis))
    route = [((i - distance) % len(devices), i) for i in devices]
    return lax.ppermute(block, axis, route)


def to_windows_cm(values):
    extent_a, extent_b, extent_c, ch = values.shape
    shaped = values.reshape(extent_a // WIN, WIN, extent_b // WIN, WIN, extent_c // WIN, WIN, ch)
    return shaped.transpose(0, 2, 4, 6, 1, 3, 5).reshape(-1, ch, CELLS)


def from_windows_cm(values, extent_a, extent_b, extent_c):
    ch = values.shape[1]
    shaped = values.reshape(extent_a // WIN, extent_b // WIN, extent_c // WIN, ch, WIN, WIN, WIN)
    return shaped.transpose(0, 4, 1, 5, 2, 6, 3).reshape(extent_a, extent_b, extent_c, ch)


def to_windows_key(values):
    extent_a, extent_b, extent_c = values.shape
    shaped = values.reshape(extent_a // WIN, WIN, extent_b // WIN, WIN, extent_c // WIN, WIN)
    return shaped.transpose(0, 2, 4, 5, 1, 3).reshape(-1, CELLS)


def window_kernel(both_ref, kcol_ref, krow_ref, gain_ref, wqkvT_ref, wqkv_ref, wp_ref,
                  gs_ref, gqkvT_ref, gproj_ref, ggain_ref, qkv_s, ga_s, drow_s):
    f32 = jnp.float32
    bf16 = jnp.bfloat16
    gqkvT_ref[...] = jnp.zeros_like(gqkvT_ref)
    gproj_ref[...] = jnp.zeros_like(gproj_ref)
    ggain_ref[...] = jnp.zeros_like(ggain_ref)
    gain = gain_ref[...]
    nt = (((1,), (1,)), ((), ()))
    pair = 2 * C
    n_pairs = NZ // 2

    def gathered(which, i, j, l):
        pieces = []
        for q in range(WIN // 2):
            p = (WIN // 2 * l + SHIFT // 2 + q) % n_pairs
            block = both_ref[which, pl.ds(i * WIN, WIN), :, pl.ds(p * pair, pair)].astype(f32)
            block = jnp.where(j == 0, block[:, :WIN], block[:, WIN:]).reshape(WIN * WIN, pair)
            pieces.append(block[:, :C])
            pieces.append(block[:, C:])
        return jnp.concatenate(pieces, axis=0).T

    def scattered(values_t, i, j, l):
        rows = values_t.T
        for q in range(WIN // 2):
            p = (WIN // 2 * l + SHIFT // 2 + q) % n_pairs
            even = rows[2 * q * WIN * WIN:(2 * q + 1) * WIN * WIN]
            odd = rows[(2 * q + 1) * WIN * WIN:(2 * q + 2) * WIN * WIN]
            block = jnp.concatenate([even, odd], axis=1).reshape(WIN, WIN, pair)
            gs_ref[pl.ds(i * WIN, WIN), pl.ds(pl.multiple_of(j * WIN, WIN), WIN), pl.ds(p * pair, pair)] = block

    def window(ij, l):
        i = ij // 2
        j = ij % 2
        w = ij * 2 + l
        x = gathered(0, i, j, l)
        row_mean = jnp.mean(x, axis=0, keepdims=True)
        centred = x - row_mean
        inv_std = lax.rsqrt(jnp.mean(centred * centred, axis=0, keepdims=True) + 1e-05)
        x_hat = centred * inv_std
        normed = (x_hat * gain).astype(bf16)
        qkv_t = jnp.dot(wqkvT_ref[...], normed, preferred_element_type=f32)
        qkv_s[...] = qkv_t.astype(bf16).astype(f32)
        g = gathered(1, i, j, l).astype(bf16)
        ga_t = jnp.dot(wp_ref[...], g, preferred_element_type=f32)
        ga_s[...] = ga_t.astype(bf16).astype(f32)
        allowed = kcol_ref[w] == krow_ref[w]

        def head_step(h, carry):
            qo = pl.multiple_of(h * HEAD, HEAD)
            q_t = qkv_s[pl.ds(qo, HEAD), :]
            k_t = qkv_s[pl.ds(qo + C, HEAD), :]
            v_t = qkv_s[pl.ds(qo + 2 * C, HEAD), :]
            ga_th = ga_s[pl.ds(qo, HEAD), :]
            q = q_t.T.astype(bf16)
            scores = jnp.dot(q, k_t.astype(bf16), preferred_element_type=f32) * SCALE
            weights = jnp.where(allowed, jnp.exp(scores), 0.0)
            probs = weights / jnp.sum(weights, axis=1, keepdims=True)
            probs_bf = probs.astype(bf16)
            att_t = lax.dot_general(v_t.astype(bf16), probs_bf, nt, preferred_element_type=f32)
            att_t = att_t.astype(bf16)
            gproj_ref[pl.ds(qo, HEAD), :] += lax.dot_general(
                att_t, g, nt, preferred_element_type=f32
            )
            ga = ga_th.T.astype(bf16)
            grad_probs = jnp.dot(ga, v_t.astype(bf16), preferred_element_type=f32)
            dv_t = jnp.dot(ga_th.astype(bf16), probs_bf, preferred_element_type=f32)
            row_total = jnp.sum(probs * grad_probs, axis=1, keepdims=True)
            grad_scores = (probs * (grad_probs - row_total) * SCALE).astype(bf16)
            dq_t = lax.dot_general(k_t.astype(bf16), grad_scores, nt, preferred_element_type=f32)
            dk_t = jnp.dot(q_t.astype(bf16), grad_scores, preferred_element_type=f32)
            drow_s[pl.ds(qo, HEAD), :] = dq_t.astype(bf16).astype(f32)
            drow_s[pl.ds(qo + C, HEAD), :] = dk_t.astype(bf16).astype(f32)
            drow_s[pl.ds(qo + 2 * C, HEAD), :] = dv_t.astype(bf16).astype(f32)
            return carry

        lax.fori_loop(0, HEADS, head_step, 0)
        rows_t = drow_s[...].astype(bf16)
        gqkvT_ref[...] += lax.dot_general(rows_t, normed, nt, preferred_element_type=f32)
        grad_normed = jnp.dot(wqkv_ref[...], rows_t, preferred_element_type=f32)
        ggain_ref[...] += jnp.sum(grad_normed * x_hat, axis=1, keepdims=True)
        scaled = grad_normed * gain
        grad_shifted = inv_std * (
            scaled
            - jnp.mean(scaled, axis=0, keepdims=True)
            - x_hat * jnp.mean(scaled * x_hat, axis=0, keepdims=True)
        )
        scattered(grad_shifted.astype(bf16).astype(f32), i, j, l)

    def block_step(ij, carry):
        for l in range(2):
            window(ij, l)
        return carry

    lax.fori_loop(0, 4, block_step, 0)


def window_grads(both, kcol, krow, gain_col, wqkv_t, wqkv, wp):
    extent_a, extent_b, width = both.shape[1:]
    return pl.pallas_call(
        window_kernel,
        out_shape=[
            jax.ShapeDtypeStruct((extent_a, extent_b, width), jnp.float32),
            jax.ShapeDtypeStruct((3 * C, C), jnp.float32),
            jax.ShapeDtypeStruct((C, C), jnp.float32),
            jax.ShapeDtypeStruct((C, 1), jnp.float32),
        ],
        scratch_shapes=[
            pltpu.VMEM((3 * C, CELLS), jnp.float32),
            pltpu.VMEM((C, CELLS), jnp.float32),
            pltpu.VMEM((3 * C, CELLS), jnp.float32),
        ],
    )(both, kcol, krow, gain_col, wqkv_t, wqkv, wp)


SUM_AXES = ("gy", "gx", "gz")


def swapped(block, axis, distance):
    return lax.ppermute(block, axis, [(i, i ^ distance) for i in range(lax.axis_size(axis))])


def summed_everywhere(parts):
    sizes = [lax.axis_size(axis) for axis in SUM_AXES]
    if any(size & (size - 1) for size in sizes):
        return lax.psum(parts, SUM_AXES)
    flat = jnp.concatenate([part.reshape(-1) for part in parts])
    total = flat.shape[0]
    devices = 1
    for size in sizes:
        devices *= size
    padded = -(-total // devices) * devices
    values = jnp.pad(flat, (0, padded - total))
    steps = []
    for axis, size in zip(SUM_AXES, sizes):
        distance = 1
        while distance < size:
            bit = (lax.axis_index(axis) // distance) % 2
            half = values.shape[0] // 2
            keep = lax.dynamic_slice_in_dim(values, bit * half, half)
            send = lax.dynamic_slice_in_dim(values, (1 - bit) * half, half)
            values = keep + swapped(send, axis, distance)
            steps.append((axis, distance))
            distance *= 2
    for axis, distance in reversed(steps):
        bit = (lax.axis_index(axis) // distance) % 2
        other = swapped(values, axis, distance)
        values = jnp.where(
            bit == 0, jnp.concatenate([values, other]), jnp.concatenate([other, values])
        )
    out = []
    start = 0
    for part in parts:
        out.append(values[start : start + part.size].reshape(part.shape))
        start += part.size
    return tuple(out)


def halo_route(distance_a, distance_b):
    size_a = lax.axis_size("gx")
    size_b = lax.axis_size(("gy", "gz"))
    route = []
    for ia in range(size_a):
        for ib in range(size_b):
            target = ((ia + distance_a) % size_a) * size_b + (ib + distance_b) % size_b
            route.append((ia * size_b + ib, target))
    return route


def moved(block, distance_a, distance_b):
    return lax.ppermute(block, ("gx", "gy", "gz"), halo_route(distance_a, distance_b))


def shifted_block(both):
    from_a = moved(both[:, :SHIFT, SHIFT:], -1, 0)
    from_b = moved(both[:, SHIFT:, :SHIFT], 0, -1)
    from_ab = moved(both[:, :SHIFT, :SHIFT], -1, -1)
    upper = jnp.concatenate([both[:, SHIFT:, SHIFT:], from_b], axis=2)
    lower = jnp.concatenate([from_a, from_ab], axis=2)
    return jnp.concatenate([upper, lower], axis=1)


def sent_back(grad_shifted):
    narrow = grad_shifted.astype(jnp.bfloat16)
    to_a = moved(narrow[-SHIFT:, :-SHIFT], 1, 0)
    to_b = moved(narrow[:-SHIFT, -SHIFT:], 0, 1)
    to_ab = moved(narrow[-SHIFT:, -SHIFT:], 1, 1)
    return to_a, to_b, to_ab


def unshifted_sum(grads_out, grad_shifted, arrived):
    to_a, to_b, to_ab = (piece.astype(jnp.float32) for piece in arrived)
    upper = jnp.concatenate([to_ab, to_a], axis=1)
    lower = jnp.concatenate([to_b, grad_shifted[:-SHIFT, :-SHIFT]], axis=1)
    branch = jnp.concatenate([upper, lower], axis=0)
    return (grads_out.astype(jnp.float32) + branch.astype(jnp.float32)).astype(jnp.bfloat16)


def per_device(tokens, grads_out, labels, ln_gain, qkv_weight, proj_weight):
    brick_a, brick_b = (tokens.shape[0], tokens.shape[1])
    brick_c = NZ
    channels = C
    both = shifted_block(jnp.stack([tokens, grads_out]))
    extent_a = brick_a * lax.axis_size("gx")
    extent_b = brick_b * lax.axis_size(("gy", "gz"))
    first_index = lax.axis_index("gx") * brick_a + jnp.arange(brick_a, dtype=jnp.int32)
    second_index = lax.axis_index(("gy", "gz")) * brick_b + jnp.arange(brick_b, dtype=jnp.int32)
    wrap_first = (first_index >= extent_a - SHIFT).astype(jnp.int32)
    wrap_second = (second_index >= extent_b - SHIFT).astype(jnp.int32)
    wrap_third = (jnp.arange(brick_c, dtype=jnp.int32) >= brick_c - SHIFT).astype(jnp.int32)
    region = (
        wrap_first[:, None, None] * 4 + wrap_second[None, :, None] * 2 + wrap_third[None, None, :]
    )
    mask_key = to_windows_key(labels * 8 + region)

    grad_branch, qkv_grad_t, proj_grad, gain_grad = window_grads(
        both,
        mask_key[:, :, None],
        mask_key[:, None, :],
        ln_gain.reshape(channels, 1),
        qkv_weight.T,
        qkv_weight,
        proj_weight,
    )
    arrived = sent_back(grad_branch)
    arrived, qkv_grad_t, proj_grad, gain_grad = lax.optimization_barrier(
        (arrived, qkv_grad_t, proj_grad, gain_grad)
    )
    qkv_grad_t, proj_grad, gain_grad = summed_everywhere((qkv_grad_t, proj_grad, gain_grad))
    qkv_grad = qkv_grad_t.T
    grad_tokens = unshifted_sum(grads_out, grad_branch, arrived)
    return (grad_tokens, gain_grad.reshape(-1), qkv_grad.reshape(-1), proj_grad.reshape(-1))


def solution(mesh):
    return jax.shard_map(
        per_device,
        mesh=mesh,
        in_specs=(
            P("gx", ("gy", "gz"), None),
            P("gx", ("gy", "gz"), None),
            P("gx", ("gy", "gz"), None),
            P(),
            P(),
            P(),
        ),
        out_specs=(P("gx", ("gy", "gz"), None), P(), P(), P()),
        check_vma=False,
    )
```

```python
import jax
import jax.numpy as jnp
from jax import lax
from jax.experimental import pallas as pl
from jax.experimental.pallas import tpu as pltpu
from jax.sharding import PartitionSpec as P

HEADS = 6
C = 192
WIN = 8
SHIFT = 4
NZ = 16
CELLS = WIN**3
HEAD = C // HEADS
SCALE = HEAD ** (-0.5)


def passed_along(block, axis, distance):
    devices = range(lax.axis_size(axis))
    route = [((i - distance) % len(devices), i) for i in devices]
    return lax.ppermute(block, axis, route)


def to_windows_cm(values):
    extent_a, extent_b, extent_c, ch = values.shape
    shaped = values.reshape(extent_a // WIN, WIN, extent_b // WIN, WIN, extent_c // WIN, WIN, ch)
    return shaped.transpose(0, 2, 4, 6, 1, 3, 5).reshape(-1, ch, CELLS)


def from_windows_cm(values, extent_a, extent_b, extent_c):
    ch = values.shape[1]
    shaped = values.reshape(extent_a // WIN, extent_b // WIN, extent_c // WIN, ch, WIN, WIN, WIN)
    return shaped.transpose(0, 4, 1, 5, 2, 6, 3).reshape(extent_a, extent_b, extent_c, ch)


def to_windows_key(values):
    extent_a, extent_b, extent_c = values.shape
    shaped = values.reshape(extent_a // WIN, WIN, extent_b // WIN, WIN, extent_c // WIN, WIN)
    return shaped.transpose(0, 2, 4, 5, 1, 3).reshape(-1, CELLS)


def make_window_kernel(first):
    def window_kernel(*refs):
        if first:
            (tok_ref, grd_ref, kcol_ref, krow_ref, gain_ref, wqkvT_ref, wqkv_ref, wp_ref,
             gs_ref, gqkvT_ref, gproj_ref, ggain_ref, qkv_s, ga_s, drow_s) = refs
        else:
            (both_ref, kcol_ref, krow_ref, gain_ref, wqkvT_ref, wqkv_ref, wp_ref,
             gs0_ref, gqkvT0_ref, gproj0_ref, ggain0_ref,
             gs_ref, gqkvT_ref, gproj_ref, ggain_ref, qkv_s, ga_s, drow_s) = refs
        f32 = jnp.float32
        bf16 = jnp.bfloat16
        if first:
            gqkvT_ref[...] = jnp.zeros_like(gqkvT_ref)
            gproj_ref[...] = jnp.zeros_like(gproj_ref)
            ggain_ref[...] = jnp.zeros_like(ggain_ref)
        else:
            gqkvT_ref[...] = gqkvT0_ref[...]
            gproj_ref[...] = gproj0_ref[...]
            ggain_ref[...] = ggain0_ref[...]
            gs_ref[pl.ds(0, WIN), pl.ds(0, WIN), :] = gs0_ref[...]
        gain = gain_ref[...]
        nt = (((1,), (1,)), ((), ()))
        pair = 2 * C
        n_pairs = NZ // 2

        def gathered(which, i, j, l):
            pieces = []
            for q in range(WIN // 2):
                p = (WIN // 2 * l + SHIFT // 2 + q) % n_pairs
                if first:
                    source = (tok_ref, grd_ref)[which]
                    block = source[pl.ds(SHIFT, WIN), :, pl.ds(p * pair, pair)].astype(f32)
                    block = block[:, SHIFT:SHIFT + WIN]
                else:
                    block = both_ref[which, pl.ds(i * WIN, WIN), :, pl.ds(p * pair, pair)]
                    block = block.astype(f32)
                    block = jnp.where(j == 0, block[:, :WIN], block[:, WIN:])
                block = block.reshape(WIN * WIN, pair)
                pieces.append(block[:, :C])
                pieces.append(block[:, C:])
            return jnp.concatenate(pieces, axis=0).T

        def scattered(values_t, i, j, l):
            rows = values_t.T
            for q in range(WIN // 2):
                p = (WIN // 2 * l + SHIFT // 2 + q) % n_pairs
                even = rows[2 * q * WIN * WIN:(2 * q + 1) * WIN * WIN]
                odd = rows[(2 * q + 1) * WIN * WIN:(2 * q + 2) * WIN * WIN]
                block = jnp.concatenate([even, odd], axis=1).reshape(WIN, WIN, pair)
                if first:
                    gs_ref[:, :, pl.ds(p * pair, pair)] = block
                else:
                    gs_ref[
                        pl.ds(i * WIN, WIN),
                        pl.ds(pl.multiple_of(j * WIN, WIN), WIN),
                        pl.ds(p * pair, pair),
                    ] = block

        def window(ij, l):
            i = ij // 2
            j = ij % 2
            w = ij * 2 + l
            x = gathered(0, i, j, l)
            row_mean = jnp.mean(x, axis=0, keepdims=True)
            centred = x - row_mean
            inv_std = lax.rsqrt(jnp.mean(centred * centred, axis=0, keepdims=True) + 1e-05)
            x_hat = centred * inv_std
            normed = (x_hat * gain).astype(bf16)
            qkv_t = jnp.dot(wqkvT_ref[...], normed, preferred_element_type=f32)
            qkv_s[...] = qkv_t.astype(bf16).astype(f32)
            g = gathered(1, i, j, l).astype(bf16)
            ga_t = jnp.dot(wp_ref[...], g, preferred_element_type=f32)
            ga_s[...] = ga_t.astype(bf16).astype(f32)
            allowed = kcol_ref[w] == krow_ref[w]

            def head_step(h, carry):
                qo = pl.multiple_of(h * HEAD, HEAD)
                q_t = qkv_s[pl.ds(qo, HEAD), :]
                k_t = qkv_s[pl.ds(qo + C, HEAD), :]
                v_t = qkv_s[pl.ds(qo + 2 * C, HEAD), :]
                ga_th = ga_s[pl.ds(qo, HEAD), :]
                q = q_t.T.astype(bf16)
                scores = jnp.dot(q, k_t.astype(bf16), preferred_element_type=f32) * SCALE
                weights = jnp.where(allowed, jnp.exp(scores), 0.0)
                probs = weights / jnp.sum(weights, axis=1, keepdims=True)
                probs_bf = probs.astype(bf16)
                att_t = lax.dot_general(v_t.astype(bf16), probs_bf, nt, preferred_element_type=f32)
                att_t = att_t.astype(bf16)
                gproj_ref[pl.ds(qo, HEAD), :] += lax.dot_general(
                    att_t, g, nt, preferred_element_type=f32
                )
                ga = ga_th.T.astype(bf16)
                grad_probs = jnp.dot(ga, v_t.astype(bf16), preferred_element_type=f32)
                dv_t = jnp.dot(ga_th.astype(bf16), probs_bf, preferred_element_type=f32)
                row_total = jnp.sum(probs * grad_probs, axis=1, keepdims=True)
                grad_scores = (probs * (grad_probs - row_total) * SCALE).astype(bf16)
                dq_t = lax.dot_general(k_t.astype(bf16), grad_scores, nt, preferred_element_type=f32)
                dk_t = jnp.dot(q_t.astype(bf16), grad_scores, preferred_element_type=f32)
                drow_s[pl.ds(qo, HEAD), :] = dq_t.astype(bf16).astype(f32)
                drow_s[pl.ds(qo + C, HEAD), :] = dk_t.astype(bf16).astype(f32)
                drow_s[pl.ds(qo + 2 * C, HEAD), :] = dv_t.astype(bf16).astype(f32)
                return carry

            lax.fori_loop(0, HEADS, head_step, 0)
            rows_t = drow_s[...].astype(bf16)
            gqkvT_ref[...] += lax.dot_general(rows_t, normed, nt, preferred_element_type=f32)
            grad_normed = jnp.dot(wqkv_ref[...], rows_t, preferred_element_type=f32)
            ggain_ref[...] += jnp.sum(grad_normed * x_hat, axis=1, keepdims=True)
            scaled = grad_normed * gain
            grad_shifted = inv_std * (
                scaled
                - jnp.mean(scaled, axis=0, keepdims=True)
                - x_hat * jnp.mean(scaled * x_hat, axis=0, keepdims=True)
            )
            scattered(grad_shifted.astype(bf16).astype(f32), i, j, l)

        def block_step(ij, carry):
            for l in range(2):
                window(ij, l)
            return carry

        if first:
            block_step(0, 0)
        else:
            lax.fori_loop(1, 4, block_step, 0)

    return window_kernel


def window_grads(first, arrays, kcol, krow, gain_col, wqkv_t, wqkv, wp, partial=()):
    if first:
        extent_a, extent_b, width = WIN, WIN, arrays[0].shape[2]
    else:
        extent_a, extent_b, width = arrays[0].shape[1:]
    return pl.pallas_call(
        make_window_kernel(first),
        out_shape=[
            jax.ShapeDtypeStruct((extent_a, extent_b, width), jnp.float32),
            jax.ShapeDtypeStruct((3 * C, C), jnp.float32),
            jax.ShapeDtypeStruct((C, C), jnp.float32),
            jax.ShapeDtypeStruct((C, 1), jnp.float32),
        ],
        scratch_shapes=[
            pltpu.VMEM((3 * C, CELLS), jnp.float32),
            pltpu.VMEM((C, CELLS), jnp.float32),
            pltpu.VMEM((3 * C, CELLS), jnp.float32),
        ],
    )(*arrays, kcol, krow, gain_col, wqkv_t, wqkv, wp, *partial)


SUM_AXES = ("gy", "gx", "gz")


def swapped(block, axis, distance):
    return lax.ppermute(block, axis, [(i, i ^ distance) for i in range(lax.axis_size(axis))])


def summed_everywhere(parts):
    sizes = [lax.axis_size(axis) for axis in SUM_AXES]
    if any(size & (size - 1) for size in sizes):
        return lax.psum(parts, SUM_AXES)
    flat = jnp.concatenate([part.reshape(-1) for part in parts])
    total = flat.shape[0]
    devices = 1
    for size in sizes:
        devices *= size
    padded = -(-total // devices) * devices
    values = jnp.pad(flat, (0, padded - total))
    steps = []
    for axis, size in zip(SUM_AXES, sizes):
        distance = 1
        while distance < size:
            bit = (lax.axis_index(axis) // distance) % 2
            half = values.shape[0] // 2
            keep = lax.dynamic_slice_in_dim(values, bit * half, half)
            send = lax.dynamic_slice_in_dim(values, (1 - bit) * half, half)
            values = keep + swapped(send, axis, distance)
            steps.append((axis, distance))
            distance *= 2
    for axis, distance in reversed(steps):
        bit = (lax.axis_index(axis) // distance) % 2
        other = swapped(values, axis, distance)
        values = jnp.where(
            bit == 0, jnp.concatenate([values, other]), jnp.concatenate([other, values])
        )
    out = []
    start = 0
    for part in parts:
        out.append(values[start : start + part.size].reshape(part.shape))
        start += part.size
    return tuple(out)


def halo_route(distance_a, distance_b):
    size_a = lax.axis_size("gx")
    size_b = lax.axis_size(("gy", "gz"))
    route = []
    for ia in range(size_a):
        for ib in range(size_b):
            target = ((ia + distance_a) % size_a) * size_b + (ib + distance_b) % size_b
            route.append((ia * size_b + ib, target))
    return route


def moved(block, distance_a, distance_b):
    return lax.ppermute(block, ("gx", "gy", "gz"), halo_route(distance_a, distance_b))


def shifted_block(both):
    from_a = moved(both[:, :SHIFT, SHIFT:], -1, 0)
    from_b = moved(both[:, SHIFT:, :SHIFT], 0, -1)
    from_ab = moved(both[:, :SHIFT, :SHIFT], -1, -1)
    upper = jnp.concatenate([both[:, SHIFT:, SHIFT:], from_b], axis=2)
    lower = jnp.concatenate([from_a, from_ab], axis=2)
    return jnp.concatenate([upper, lower], axis=1)


def unshifted_sum(grads_out, grad_shifted):
    narrow = grad_shifted.astype(jnp.bfloat16)
    to_a = moved(narrow[-SHIFT:, :-SHIFT], 1, 0).astype(jnp.float32)
    to_b = moved(narrow[:-SHIFT, -SHIFT:], 0, 1).astype(jnp.float32)
    to_ab = moved(narrow[-SHIFT:, -SHIFT:], 1, 1).astype(jnp.float32)
    upper = jnp.concatenate([to_ab, to_a], axis=1)
    lower = jnp.concatenate([to_b, grad_shifted[:-SHIFT, :-SHIFT]], axis=1)
    branch = jnp.concatenate([upper, lower], axis=0)
    return (grads_out.astype(jnp.float32) + branch.astype(jnp.float32)).astype(jnp.bfloat16)


def per_device(tokens, grads_out, labels, ln_gain, qkv_weight, proj_weight):
    brick_a, brick_b = (tokens.shape[0], tokens.shape[1])
    brick_c = NZ
    channels = C
    both = shifted_block(jnp.stack([tokens, grads_out]))
    extent_a = brick_a * lax.axis_size("gx")
    extent_b = brick_b * lax.axis_size(("gy", "gz"))
    first_index = lax.axis_index("gx") * brick_a + jnp.arange(brick_a, dtype=jnp.int32)
    second_index = lax.axis_index(("gy", "gz")) * brick_b + jnp.arange(brick_b, dtype=jnp.int32)
    wrap_first = (first_index >= extent_a - SHIFT).astype(jnp.int32)
    wrap_second = (second_index >= extent_b - SHIFT).astype(jnp.int32)
    wrap_third = (jnp.arange(brick_c, dtype=jnp.int32) >= brick_c - SHIFT).astype(jnp.int32)
    region = (
        wrap_first[:, None, None] * 4 + wrap_second[None, :, None] * 2 + wrap_third[None, None, :]
    )
    mask_key = to_windows_key(labels * 8 + region)

    constants = (
        mask_key[:, :, None],
        mask_key[:, None, :],
        ln_gain.reshape(channels, 1),
        qkv_weight.T,
        qkv_weight,
        proj_weight,
    )
    partial = window_grads(True, (tokens, grads_out), *constants)
    grad_branch, qkv_grad_t, proj_grad, gain_grad = window_grads(
        False, (both,), *constants, partial=partial
    )
    qkv_grad_t, proj_grad, gain_grad = summed_everywhere((qkv_grad_t, proj_grad, gain_grad))
    qkv_grad = qkv_grad_t.T
    grad_tokens = unshifted_sum(grads_out, grad_branch)
    return (grad_tokens, gain_grad.reshape(-1), qkv_grad.reshape(-1), proj_grad.reshape(-1))


def solution(mesh):
    return jax.shard_map(
        per_device,
        mesh=mesh,
        in_specs=(
            P("gx", ("gy", "gz"), None),
            P("gx", ("gy", "gz"), None),
            P("gx", ("gy", "gz"), None),
            P(),
            P(),
            P(),
        ),
        out_specs=(P("gx", ("gy", "gz"), None), P(), P(), P()),
        check_vma=False,
    )
```

```python
import jax
import jax.numpy as jnp
from jax import lax
from jax.experimental import pallas as pl
from jax.experimental.pallas import tpu as pltpu
from jax.sharding import PartitionSpec as P

HEADS = 6
C = 192
WIN = 8
SHIFT = 4
NZ = 16
CELLS = WIN**3
HEAD = C // HEADS
SCALE = HEAD ** (-0.5)
ROWS = 128


def passed_along(block, axis, distance):
    devices = range(lax.axis_size(axis))
    route = [((i - distance) % len(devices), i) for i in devices]
    return lax.ppermute(block, axis, route)


def to_windows_cm(values):
    extent_a, extent_b, extent_c, ch = values.shape
    shaped = values.reshape(extent_a // WIN, WIN, extent_b // WIN, WIN, extent_c // WIN, WIN, ch)
    return shaped.transpose(0, 2, 4, 6, 1, 3, 5).reshape(-1, ch, CELLS)


def from_windows_cm(values, extent_a, extent_b, extent_c):
    ch = values.shape[1]
    shaped = values.reshape(extent_a // WIN, extent_b // WIN, extent_c // WIN, ch, WIN, WIN, WIN)
    return shaped.transpose(0, 4, 1, 5, 2, 6, 3).reshape(extent_a, extent_b, extent_c, ch)


def to_windows_key(values):
    extent_a, extent_b, extent_c = values.shape
    shaped = values.reshape(extent_a // WIN, WIN, extent_b // WIN, WIN, extent_c // WIN, WIN)
    return shaped.transpose(0, 2, 4, 5, 1, 3).reshape(-1, CELLS)


def make_window_kernel(first):
    def window_kernel(*refs):
        if first:
            (tok_ref, grd_ref, kcol_ref, krow_ref, gain_ref, wqkvT_ref, wqkv_ref, wp_ref,
             gs_ref, gqkvT_ref, gproj_ref, ggain_ref, qkv_s, ga_s, drow_s) = refs
        else:
            (both_ref, kcol_ref, krow_ref, gain_ref, wqkvT_ref, wqkv_ref, wp_ref,
             gs0_ref, gqkvT0_ref, gproj0_ref, ggain0_ref,
             gs_ref, gqkvT_ref, gproj_ref, ggain_ref, qkv_s, ga_s, drow_s) = refs
        f32 = jnp.float32
        bf16 = jnp.bfloat16
        if first:
            gqkvT_ref[...] = jnp.zeros_like(gqkvT_ref)
            gproj_ref[...] = jnp.zeros_like(gproj_ref)
            ggain_ref[...] = jnp.zeros_like(ggain_ref)
        else:
            gqkvT_ref[...] = gqkvT0_ref[...]
            gproj_ref[...] = gproj0_ref[...]
            ggain_ref[...] = ggain0_ref[...]
            gs_ref[pl.ds(0, WIN), pl.ds(0, WIN), :] = gs0_ref[...]
        gain = gain_ref[...]
        nt = (((1,), (1,)), ((), ()))
        pair = 2 * C
        n_pairs = NZ // 2

        def gathered(which, i, j, l):
            pieces = []
            for q in range(WIN // 2):
                p = (WIN // 2 * l + SHIFT // 2 + q) % n_pairs
                if first:
                    source = (tok_ref, grd_ref)[which]
                    block = source[pl.ds(SHIFT, WIN), :, pl.ds(p * pair, pair)].astype(f32)
                    block = block[:, SHIFT:SHIFT + WIN]
                else:
                    block = both_ref[which, pl.ds(i * WIN, WIN), :, pl.ds(p * pair, pair)]
                    block = block.astype(f32)
                    block = jnp.where(j == 0, block[:, :WIN], block[:, WIN:])
                block = block.reshape(WIN * WIN, pair)
                pieces.append(block[:, :C])
                pieces.append(block[:, C:])
            return jnp.concatenate(pieces, axis=0).T

        def scattered(values_t, i, j, l):
            rows = values_t.T
            for q in range(WIN // 2):
                p = (WIN // 2 * l + SHIFT // 2 + q) % n_pairs
                even = rows[2 * q * WIN * WIN:(2 * q + 1) * WIN * WIN]
                odd = rows[(2 * q + 1) * WIN * WIN:(2 * q + 2) * WIN * WIN]
                block = jnp.concatenate([even, odd], axis=1).reshape(WIN, WIN, pair)
                if first:
                    gs_ref[:, :, pl.ds(p * pair, pair)] = block
                else:
                    gs_ref[
                        pl.ds(i * WIN, WIN),
                        pl.ds(pl.multiple_of(j * WIN, WIN), WIN),
                        pl.ds(p * pair, pair),
                    ] = block

        def window(ij, l):
            i = ij // 2
            j = ij % 2
            w = ij * 2 + l
            x = gathered(0, i, j, l)
            row_mean = jnp.mean(x, axis=0, keepdims=True)
            centred = x - row_mean
            inv_std = lax.rsqrt(jnp.mean(centred * centred, axis=0, keepdims=True) + 1e-05)
            x_hat = centred * inv_std
            normed = (x_hat * gain).astype(bf16)
            qkv_t = jnp.dot(wqkvT_ref[...], normed, preferred_element_type=f32)
            qkv_s[...] = qkv_t.astype(bf16).astype(f32)
            g = gathered(1, i, j, l).astype(bf16)
            ga_t = jnp.dot(wp_ref[...], g, preferred_element_type=f32)
            ga_s[...] = ga_t.astype(bf16).astype(f32)
            allowed = kcol_ref[w] == krow_ref[w]

            def head_step(h, carry):
                qo = pl.multiple_of(h * HEAD, HEAD)
                q_t = qkv_s[pl.ds(qo, HEAD), :]
                k_t = qkv_s[pl.ds(qo + C, HEAD), :]
                v_t = qkv_s[pl.ds(qo + 2 * C, HEAD), :]
                ga_th = ga_s[pl.ds(qo, HEAD), :]
                q = q_t.T.astype(bf16)
                ga = ga_th.T.astype(bf16)
                q_tb = q_t.astype(bf16)
                k_tb = k_t.astype(bf16)
                v_tb = v_t.astype(bf16)
                ga_tb = ga_th.astype(bf16)
                att_parts = []
                dq_parts = []
                dv_t = jnp.zeros((HEAD, CELLS), f32)
                dk_t = jnp.zeros((HEAD, CELLS), f32)
                for r in range(CELLS // ROWS):
                    rows = slice(r * ROWS, (r + 1) * ROWS)
                    scores = jnp.dot(q[rows], k_tb, preferred_element_type=f32) * SCALE
                    weights = jnp.where(allowed[rows], jnp.exp(scores), 0.0)
                    probs = weights / jnp.sum(weights, axis=1, keepdims=True)
                    probs_bf = probs.astype(bf16)
                    att_parts.append(
                        lax.dot_general(v_tb, probs_bf, nt, preferred_element_type=f32)
                    )
                    grad_probs = jnp.dot(ga[rows], v_tb, preferred_element_type=f32)
                    dv_t = dv_t + jnp.dot(ga_tb[:, rows], probs_bf, preferred_element_type=f32)
                    row_total = jnp.sum(probs * grad_probs, axis=1, keepdims=True)
                    grad_scores = (probs * (grad_probs - row_total) * SCALE).astype(bf16)
                    dq_parts.append(
                        lax.dot_general(k_tb, grad_scores, nt, preferred_element_type=f32)
                    )
                    dk_t = dk_t + jnp.dot(q_tb[:, rows], grad_scores, preferred_element_type=f32)
                att_t = jnp.concatenate(att_parts, axis=1).astype(bf16)
                gproj_ref[pl.ds(qo, HEAD), :] += lax.dot_general(
                    att_t, g, nt, preferred_element_type=f32
                )
                dq_t = jnp.concatenate(dq_parts, axis=1)
                drow_s[pl.ds(qo, HEAD), :] = dq_t.astype(bf16).astype(f32)
                drow_s[pl.ds(qo + C, HEAD), :] = dk_t.astype(bf16).astype(f32)
                drow_s[pl.ds(qo + 2 * C, HEAD), :] = dv_t.astype(bf16).astype(f32)
                return carry

            lax.fori_loop(0, HEADS, head_step, 0)
            rows_t = drow_s[...].astype(bf16)
            gqkvT_ref[...] += lax.dot_general(rows_t, normed, nt, preferred_element_type=f32)
            grad_normed = jnp.dot(wqkv_ref[...], rows_t, preferred_element_type=f32)
            ggain_ref[...] += jnp.sum(grad_normed * x_hat, axis=1, keepdims=True)
            scaled = grad_normed * gain
            grad_shifted = inv_std * (
                scaled
                - jnp.mean(scaled, axis=0, keepdims=True)
                - x_hat * jnp.mean(scaled * x_hat, axis=0, keepdims=True)
            )
            scattered(grad_shifted.astype(bf16).astype(f32), i, j, l)

        def block_step(ij, carry):
            for l in range(2):
                window(ij, l)
            return carry

        if first:
            block_step(0, 0)
        else:
            lax.fori_loop(1, 4, block_step, 0)

    return window_kernel


def window_grads(first, arrays, kcol, krow, gain_col, wqkv_t, wqkv, wp, partial=()):
    if first:
        extent_a, extent_b, width = WIN, WIN, arrays[0].shape[2]
    else:
        extent_a, extent_b, width = arrays[0].shape[1:]
    return pl.pallas_call(
        make_window_kernel(first),
        out_shape=[
            jax.ShapeDtypeStruct((extent_a, extent_b, width), jnp.float32),
            jax.ShapeDtypeStruct((3 * C, C), jnp.float32),
            jax.ShapeDtypeStruct((C, C), jnp.float32),
            jax.ShapeDtypeStruct((C, 1), jnp.float32),
        ],
        scratch_shapes=[
            pltpu.VMEM((3 * C, CELLS), jnp.float32),
            pltpu.VMEM((C, CELLS), jnp.float32),
            pltpu.VMEM((3 * C, CELLS), jnp.float32),
        ],
    )(*arrays, kcol, krow, gain_col, wqkv_t, wqkv, wp, *partial)


SUM_AXES = ("gy", "gx", "gz")


def swapped(block, axis, distance):
    return lax.ppermute(block, axis, [(i, i ^ distance) for i in range(lax.axis_size(axis))])


def summed_everywhere(parts):
    sizes = [lax.axis_size(axis) for axis in SUM_AXES]
    if any(size & (size - 1) for size in sizes):
        return lax.psum(parts, SUM_AXES)
    flat = jnp.concatenate([part.reshape(-1) for part in parts])
    total = flat.shape[0]
    devices = 1
    for size in sizes:
        devices *= size
    padded = -(-total // devices) * devices
    values = jnp.pad(flat, (0, padded - total))
    steps = []
    for axis, size in zip(SUM_AXES, sizes):
        distance = 1
        while distance < size:
            bit = (lax.axis_index(axis) // distance) % 2
            half = values.shape[0] // 2
            keep = lax.dynamic_slice_in_dim(values, bit * half, half)
            send = lax.dynamic_slice_in_dim(values, (1 - bit) * half, half)
            values = keep + swapped(send, axis, distance)
            steps.append((axis, distance))
            distance *= 2
    for axis, distance in reversed(steps):
        bit = (lax.axis_index(axis) // distance) % 2
        other = swapped(values, axis, distance)
        values = jnp.where(
            bit == 0, jnp.concatenate([values, other]), jnp.concatenate([other, values])
        )
    out = []
    start = 0
    for part in parts:
        out.append(values[start : start + part.size].reshape(part.shape))
        start += part.size
    return tuple(out)


def halo_route(distance_a, distance_b):
    size_a = lax.axis_size("gx")
    size_b = lax.axis_size(("gy", "gz"))
    route = []
    for ia in range(size_a):
        for ib in range(size_b):
            target = ((ia + distance_a) % size_a) * size_b + (ib + distance_b) % size_b
            route.append((ia * size_b + ib, target))
    return route


def moved(block, distance_a, distance_b):
    return lax.ppermute(block, ("gx", "gy", "gz"), halo_route(distance_a, distance_b))


def shifted_block(both):
    from_a = moved(both[:, :SHIFT, SHIFT:], -1, 0)
    from_b = moved(both[:, SHIFT:, :SHIFT], 0, -1)
    from_ab = moved(both[:, :SHIFT, :SHIFT], -1, -1)
    upper = jnp.concatenate([both[:, SHIFT:, SHIFT:], from_b], axis=2)
    lower = jnp.concatenate([from_a, from_ab], axis=2)
    return jnp.concatenate([upper, lower], axis=1)


def unshifted_sum(grads_out, grad_shifted):
    narrow = grad_shifted.astype(jnp.bfloat16)
    to_a = moved(narrow[-SHIFT:, :-SHIFT], 1, 0).astype(jnp.float32)
    to_b = moved(narrow[:-SHIFT, -SHIFT:], 0, 1).astype(jnp.float32)
    to_ab = moved(narrow[-SHIFT:, -SHIFT:], 1, 1).astype(jnp.float32)
    upper = jnp.concatenate([to_ab, to_a], axis=1)
    lower = jnp.concatenate([to_b, grad_shifted[:-SHIFT, :-SHIFT]], axis=1)
    branch = jnp.concatenate([upper, lower], axis=0)
    return (grads_out.astype(jnp.float32) + branch.astype(jnp.float32)).astype(jnp.bfloat16)


def per_device(tokens, grads_out, labels, ln_gain, qkv_weight, proj_weight):
    brick_a, brick_b = (tokens.shape[0], tokens.shape[1])
    brick_c = NZ
    channels = C
    both = shifted_block(jnp.stack([tokens, grads_out]))
    extent_a = brick_a * lax.axis_size("gx")
    extent_b = brick_b * lax.axis_size(("gy", "gz"))
    first_index = lax.axis_index("gx") * brick_a + jnp.arange(brick_a, dtype=jnp.int32)
    second_index = lax.axis_index(("gy", "gz")) * brick_b + jnp.arange(brick_b, dtype=jnp.int32)
    wrap_first = (first_index >= extent_a - SHIFT).astype(jnp.int32)
    wrap_second = (second_index >= extent_b - SHIFT).astype(jnp.int32)
    wrap_third = (jnp.arange(brick_c, dtype=jnp.int32) >= brick_c - SHIFT).astype(jnp.int32)
    region = (
        wrap_first[:, None, None] * 4 + wrap_second[None, :, None] * 2 + wrap_third[None, None, :]
    )
    mask_key = to_windows_key(labels * 8 + region)

    constants = (
        mask_key[:, :, None],
        mask_key[:, None, :],
        ln_gain.reshape(channels, 1),
        qkv_weight.T,
        qkv_weight,
        proj_weight,
    )
    partial = window_grads(True, (tokens, grads_out), *constants)
    grad_branch, qkv_grad_t, proj_grad, gain_grad = window_grads(
        False, (both,), *constants, partial=partial
    )
    qkv_grad_t, proj_grad, gain_grad = summed_everywhere((qkv_grad_t, proj_grad, gain_grad))
    qkv_grad = qkv_grad_t.T
    grad_tokens = unshifted_sum(grads_out, grad_branch)
    return (grad_tokens, gain_grad.reshape(-1), qkv_grad.reshape(-1), proj_grad.reshape(-1))


def solution(mesh):
    return jax.shard_map(
        per_device,
        mesh=mesh,
        in_specs=(
            P("gx", ("gy", "gz"), None),
            P("gx", ("gy", "gz"), None),
            P("gx", ("gy", "gz"), None),
            P(),
            P(),
            P(),
        ),
        out_specs=(P("gx", ("gy", "gz"), None), P(), P(), P()),
        check_vma=False,
    )
```

```python
import jax
import jax.numpy as jnp
from jax import lax
from jax.experimental import pallas as pl
from jax.experimental.pallas import tpu as pltpu
from jax.sharding import PartitionSpec as P

HEADS = 6
C = 192
WIN = 8
SHIFT = 4
NZ = 16
CELLS = WIN**3
HEAD = C // HEADS
SCALE = HEAD ** (-0.5)


def passed_along(block, axis, distance):
    devices = range(lax.axis_size(axis))
    route = [((i - distance) % len(devices), i) for i in devices]
    return lax.ppermute(block, axis, route)


def to_windows_cm(values):
    extent_a, extent_b, extent_c, ch = values.shape
    shaped = values.reshape(extent_a // WIN, WIN, extent_b // WIN, WIN, extent_c // WIN, WIN, ch)
    return shaped.transpose(0, 2, 4, 6, 1, 3, 5).reshape(-1, ch, CELLS)


def from_windows_cm(values, extent_a, extent_b, extent_c):
    ch = values.shape[1]
    shaped = values.reshape(extent_a // WIN, extent_b // WIN, extent_c // WIN, ch, WIN, WIN, WIN)
    return shaped.transpose(0, 4, 1, 5, 2, 6, 3).reshape(extent_a, extent_b, extent_c, ch)


def to_windows_key(values):
    extent_a, extent_b, extent_c = values.shape
    shaped = values.reshape(extent_a // WIN, WIN, extent_b // WIN, WIN, extent_c // WIN, WIN)
    return shaped.transpose(0, 2, 4, 5, 1, 3).reshape(-1, CELLS)


def make_window_kernel(first):
    def window_kernel(*refs):
        if first:
            (tok_ref, grd_ref, kcol_ref, krow_ref, gain_ref, wqkvT_ref, wqkv_ref, wp_ref,
             gs_ref, gqkvT_ref, gproj_ref, ggain_ref, qkv_s, ga_s, drow_s) = refs
        else:
            (both_ref, kcol_ref, krow_ref, gain_ref, wqkvT_ref, wqkv_ref, wp_ref,
             gs0_ref, gqkvT0_ref, gproj0_ref, ggain0_ref,
             gs_ref, gqkvT_ref, gproj_ref, ggain_ref, qkv_s, ga_s, drow_s) = refs
        f32 = jnp.float32
        bf16 = jnp.bfloat16
        if first:
            gqkvT_ref[...] = jnp.zeros_like(gqkvT_ref)
            gproj_ref[...] = jnp.zeros_like(gproj_ref)
            ggain_ref[...] = jnp.zeros_like(ggain_ref)
        else:
            gqkvT_ref[...] = gqkvT0_ref[...]
            gproj_ref[...] = gproj0_ref[...]
            ggain_ref[...] = ggain0_ref[...]
            gs_ref[pl.ds(0, WIN), pl.ds(0, WIN), :] = gs0_ref[...]
        gain = gain_ref[...]
        nt = (((1,), (1,)), ((), ()))
        pair = 2 * C
        n_pairs = NZ // 2

        def gathered(which, i, j, l):
            pieces = []
            for q in range(WIN // 2):
                p = (WIN // 2 * l + SHIFT // 2 + q) % n_pairs
                if first:
                    source = (tok_ref, grd_ref)[which]
                    block = source[pl.ds(SHIFT, WIN), :, pl.ds(p * pair, pair)].astype(f32)
                    block = block[:, SHIFT:SHIFT + WIN]
                else:
                    block = both_ref[which, pl.ds(i * WIN, WIN), :, pl.ds(p * pair, pair)]
                    block = block.astype(f32)
                    block = jnp.where(j == 0, block[:, :WIN], block[:, WIN:])
                block = block.reshape(WIN * WIN, pair)
                pieces.append(block[:, :C])
                pieces.append(block[:, C:])
            return jnp.concatenate(pieces, axis=0).T

        def scattered(values_t, i, j, l):
            rows = values_t.T
            for q in range(WIN // 2):
                p = (WIN // 2 * l + SHIFT // 2 + q) % n_pairs
                even = rows[2 * q * WIN * WIN:(2 * q + 1) * WIN * WIN]
                odd = rows[(2 * q + 1) * WIN * WIN:(2 * q + 2) * WIN * WIN]
                block = jnp.concatenate([even, odd], axis=1).reshape(WIN, WIN, pair)
                if first:
                    gs_ref[:, :, pl.ds(p * pair, pair)] = block
                else:
                    gs_ref[
                        pl.ds(i * WIN, WIN),
                        pl.ds(pl.multiple_of(j * WIN, WIN), WIN),
                        pl.ds(p * pair, pair),
                    ] = block

        def window(ij, l):
            i = ij // 2
            j = ij % 2
            w = ij * 2 + l
            x = gathered(0, i, j, l)
            row_mean = jnp.mean(x, axis=0, keepdims=True)
            centred = x - row_mean
            inv_std = lax.rsqrt(jnp.mean(centred * centred, axis=0, keepdims=True) + 1e-05)
            x_hat = centred * inv_std
            normed = (x_hat * gain).astype(bf16)
            qkv_t = jnp.dot(wqkvT_ref[...], normed, preferred_element_type=f32)
            qkv_s[...] = qkv_t.astype(bf16).astype(f32)
            g = gathered(1, i, j, l).astype(bf16)
            ga_t = jnp.dot(wp_ref[...], g, preferred_element_type=f32)
            ga_s[...] = ga_t.astype(bf16).astype(f32)
            allowed = kcol_ref[w] == krow_ref[w]

            def head_step(h, carry):
                qo = pl.multiple_of(h * HEAD, HEAD)
                q_t = qkv_s[pl.ds(qo, HEAD), :]
                k_t = qkv_s[pl.ds(qo + C, HEAD), :]
                v_t = qkv_s[pl.ds(qo + 2 * C, HEAD), :]
                ga_th = ga_s[pl.ds(qo, HEAD), :]
                q = q_t.T.astype(bf16)
                scores = jnp.dot(q, k_t.astype(bf16), preferred_element_type=f32) * SCALE
                weights = jnp.where(allowed, jnp.exp(scores), 0.0)
                probs = weights / jnp.sum(weights, axis=1, keepdims=True)
                probs_bf = probs.astype(bf16)
                attended = jnp.dot(probs_bf, v_t.T.astype(bf16), preferred_element_type=f32)
                att_t = attended.T.astype(bf16)
                gproj_ref[pl.ds(qo, HEAD), :] += lax.dot_general(
                    att_t, g, nt, preferred_element_type=f32
                )
                ga = ga_th.T.astype(bf16)
                grad_probs = jnp.dot(ga, v_t.astype(bf16), preferred_element_type=f32)
                dv_t = jnp.dot(ga_th.astype(bf16), probs_bf, preferred_element_type=f32)
                row_total = jnp.sum(probs * grad_probs, axis=1, keepdims=True)
                grad_scores = (probs * (grad_probs - row_total) * SCALE).astype(bf16)
                dq_t = jnp.dot(grad_scores, k_t.T.astype(bf16), preferred_element_type=f32).T
                dk_t = jnp.dot(q_t.astype(bf16), grad_scores, preferred_element_type=f32)
                drow_s[pl.ds(qo, HEAD), :] = dq_t.astype(bf16).astype(f32)
                drow_s[pl.ds(qo + C, HEAD), :] = dk_t.astype(bf16).astype(f32)
                drow_s[pl.ds(qo + 2 * C, HEAD), :] = dv_t.astype(bf16).astype(f32)
                return carry

            lax.fori_loop(0, HEADS, head_step, 0)
            rows_t = drow_s[...].astype(bf16)
            gqkvT_ref[...] += lax.dot_general(rows_t, normed, nt, preferred_element_type=f32)
            grad_normed = jnp.dot(wqkv_ref[...], rows_t, preferred_element_type=f32)
            ggain_ref[...] += jnp.sum(grad_normed * x_hat, axis=1, keepdims=True)
            scaled = grad_normed * gain
            grad_shifted = inv_std * (
                scaled
                - jnp.mean(scaled, axis=0, keepdims=True)
                - x_hat * jnp.mean(scaled * x_hat, axis=0, keepdims=True)
            )
            scattered(grad_shifted.astype(bf16).astype(f32), i, j, l)

        def block_step(ij, carry):
            for l in range(2):
                window(ij, l)
            return carry

        if first:
            block_step(0, 0)
        else:
            lax.fori_loop(1, 4, block_step, 0)

    return window_kernel


def window_grads(first, arrays, kcol, krow, gain_col, wqkv_t, wqkv, wp, partial=()):
    if first:
        extent_a, extent_b, width = WIN, WIN, arrays[0].shape[2]
    else:
        extent_a, extent_b, width = arrays[0].shape[1:]
    return pl.pallas_call(
        make_window_kernel(first),
        out_shape=[
            jax.ShapeDtypeStruct((extent_a, extent_b, width), jnp.float32),
            jax.ShapeDtypeStruct((3 * C, C), jnp.float32),
            jax.ShapeDtypeStruct((C, C), jnp.float32),
            jax.ShapeDtypeStruct((C, 1), jnp.float32),
        ],
        scratch_shapes=[
            pltpu.VMEM((3 * C, CELLS), jnp.float32),
            pltpu.VMEM((C, CELLS), jnp.float32),
            pltpu.VMEM((3 * C, CELLS), jnp.float32),
        ],
    )(*arrays, kcol, krow, gain_col, wqkv_t, wqkv, wp, *partial)


SUM_AXES = ("gy", "gx", "gz")


def swapped(block, axis, distance):
    return lax.ppermute(block, axis, [(i, i ^ distance) for i in range(lax.axis_size(axis))])


def summed_everywhere(parts):
    sizes = [lax.axis_size(axis) for axis in SUM_AXES]
    if any(size & (size - 1) for size in sizes):
        return lax.psum(parts, SUM_AXES)
    flat = jnp.concatenate([part.reshape(-1) for part in parts])
    total = flat.shape[0]
    devices = 1
    for size in sizes:
        devices *= size
    padded = -(-total // devices) * devices
    values = jnp.pad(flat, (0, padded - total))
    steps = []
    for axis, size in zip(SUM_AXES, sizes):
        distance = 1
        while distance < size:
            bit = (lax.axis_index(axis) // distance) % 2
            half = values.shape[0] // 2
            keep = lax.dynamic_slice_in_dim(values, bit * half, half)
            send = lax.dynamic_slice_in_dim(values, (1 - bit) * half, half)
            values = keep + swapped(send, axis, distance)
            steps.append((axis, distance))
            distance *= 2
    for axis, distance in reversed(steps):
        bit = (lax.axis_index(axis) // distance) % 2
        other = swapped(values, axis, distance)
        values = jnp.where(
            bit == 0, jnp.concatenate([values, other]), jnp.concatenate([other, values])
        )
    out = []
    start = 0
    for part in parts:
        out.append(values[start : start + part.size].reshape(part.shape))
        start += part.size
    return tuple(out)


def halo_route(distance_a, distance_b):
    size_a = lax.axis_size("gx")
    size_b = lax.axis_size(("gy", "gz"))
    route = []
    for ia in range(size_a):
        for ib in range(size_b):
            target = ((ia + distance_a) % size_a) * size_b + (ib + distance_b) % size_b
            route.append((ia * size_b + ib, target))
    return route


def moved(block, distance_a, distance_b):
    return lax.ppermute(block, ("gx", "gy", "gz"), halo_route(distance_a, distance_b))


def shifted_block(both):
    from_a = moved(both[:, :SHIFT, SHIFT:], -1, 0)
    from_b = moved(both[:, SHIFT:, :SHIFT], 0, -1)
    from_ab = moved(both[:, :SHIFT, :SHIFT], -1, -1)
    upper = jnp.concatenate([both[:, SHIFT:, SHIFT:], from_b], axis=2)
    lower = jnp.concatenate([from_a, from_ab], axis=2)
    return jnp.concatenate([upper, lower], axis=1)


def unshifted_sum(grads_out, grad_shifted):
    narrow = grad_shifted.astype(jnp.bfloat16)
    to_a = moved(narrow[-SHIFT:, :-SHIFT], 1, 0).astype(jnp.float32)
    to_b = moved(narrow[:-SHIFT, -SHIFT:], 0, 1).astype(jnp.float32)
    to_ab = moved(narrow[-SHIFT:, -SHIFT:], 1, 1).astype(jnp.float32)
    upper = jnp.concatenate([to_ab, to_a], axis=1)
    lower = jnp.concatenate([to_b, grad_shifted[:-SHIFT, :-SHIFT]], axis=1)
    branch = jnp.concatenate([upper, lower], axis=0)
    return (grads_out.astype(jnp.float32) + branch.astype(jnp.float32)).astype(jnp.bfloat16)


def per_device(tokens, grads_out, labels, ln_gain, qkv_weight, proj_weight):
    brick_a, brick_b = (tokens.shape[0], tokens.shape[1])
    brick_c = NZ
    channels = C
    both = shifted_block(jnp.stack([tokens, grads_out]))
    extent_a = brick_a * lax.axis_size("gx")
    extent_b = brick_b * lax.axis_size(("gy", "gz"))
    first_index = lax.axis_index("gx") * brick_a + jnp.arange(brick_a, dtype=jnp.int32)
    second_index = lax.axis_index(("gy", "gz")) * brick_b + jnp.arange(brick_b, dtype=jnp.int32)
    wrap_first = (first_index >= extent_a - SHIFT).astype(jnp.int32)
    wrap_second = (second_index >= extent_b - SHIFT).astype(jnp.int32)
    wrap_third = (jnp.arange(brick_c, dtype=jnp.int32) >= brick_c - SHIFT).astype(jnp.int32)
    region = (
        wrap_first[:, None, None] * 4 + wrap_second[None, :, None] * 2 + wrap_third[None, None, :]
    )
    mask_key = to_windows_key(labels * 8 + region)

    constants = (
        mask_key[:, :, None],
        mask_key[:, None, :],
        ln_gain.reshape(channels, 1),
        qkv_weight.T,
        qkv_weight,
        proj_weight,
    )
    partial = window_grads(True, (tokens, grads_out), *constants)
    grad_branch, qkv_grad_t, proj_grad, gain_grad = window_grads(
        False, (both,), *constants, partial=partial
    )
    qkv_grad_t, proj_grad, gain_grad = summed_everywhere((qkv_grad_t, proj_grad, gain_grad))
    qkv_grad = qkv_grad_t.T
    grad_tokens = unshifted_sum(grads_out, grad_branch)
    return (grad_tokens, gain_grad.reshape(-1), qkv_grad.reshape(-1), proj_grad.reshape(-1))


def solution(mesh):
    return jax.shard_map(
        per_device,
        mesh=mesh,
        in_specs=(
            P("gx", ("gy", "gz"), None),
            P("gx", ("gy", "gz"), None),
            P("gx", ("gy", "gz"), None),
            P(),
            P(),
            P(),
        ),
        out_specs=(P("gx", ("gy", "gz"), None), P(), P(), P()),
        check_vma=False,
    )
```

```python
import jax
import jax.numpy as jnp
from jax import lax
from jax.experimental import pallas as pl
from jax.experimental.pallas import tpu as pltpu
from jax.sharding import PartitionSpec as P

HEADS = 6
C = 192
WIN = 8
SHIFT = 4
NZ = 16
CELLS = WIN**3
HEAD = C // HEADS
SCALE = HEAD ** (-0.5)


def passed_along(block, axis, distance):
    devices = range(lax.axis_size(axis))
    route = [((i - distance) % len(devices), i) for i in devices]
    return lax.ppermute(block, axis, route)


def to_windows_cm(values):
    extent_a, extent_b, extent_c, ch = values.shape
    shaped = values.reshape(extent_a // WIN, WIN, extent_b // WIN, WIN, extent_c // WIN, WIN, ch)
    return shaped.transpose(0, 2, 4, 6, 1, 3, 5).reshape(-1, ch, CELLS)


def from_windows_cm(values, extent_a, extent_b, extent_c):
    ch = values.shape[1]
    shaped = values.reshape(extent_a // WIN, extent_b // WIN, extent_c // WIN, ch, WIN, WIN, WIN)
    return shaped.transpose(0, 4, 1, 5, 2, 6, 3).reshape(extent_a, extent_b, extent_c, ch)


def to_windows_key(values):
    extent_a, extent_b, extent_c = values.shape
    shaped = values.reshape(extent_a // WIN, WIN, extent_b // WIN, WIN, extent_c // WIN, WIN)
    return shaped.transpose(0, 2, 4, 5, 1, 3).reshape(-1, CELLS)


def make_window_kernel(first):
    def window_kernel(*refs):
        if first:
            (tok_ref, grd_ref, kcol_ref, krow_ref, gain_ref, wqkvT_ref, wqkv_ref, wp_ref,
             gs_ref, gqkvT_ref, gproj_ref, ggain_ref, qkv_s, ga_s, drow_s) = refs
        else:
            (both_ref, kcol_ref, krow_ref, gain_ref, wqkvT_ref, wqkv_ref, wp_ref,
             gs0_ref, gqkvT0_ref, gproj0_ref, ggain0_ref,
             gs_ref, gqkvT_ref, gproj_ref, ggain_ref, qkv_s, ga_s, drow_s) = refs
        f32 = jnp.float32
        bf16 = jnp.bfloat16
        if first:
            gqkvT_ref[...] = jnp.zeros_like(gqkvT_ref)
            gproj_ref[...] = jnp.zeros_like(gproj_ref)
            ggain_ref[...] = jnp.zeros_like(ggain_ref)
        else:
            gqkvT_ref[...] = gqkvT0_ref[...]
            gproj_ref[...] = gproj0_ref[...]
            ggain_ref[...] = ggain0_ref[...]
            gs_ref[pl.ds(0, WIN), pl.ds(0, WIN), :] = gs0_ref[...]
        gain = gain_ref[...]
        nt = (((1,), (1,)), ((), ()))
        pair = 2 * C
        n_pairs = NZ // 2

        def gathered(which, i, j, l):
            pieces = []
            for q in range(WIN // 2):
                p = (WIN // 2 * l + SHIFT // 2 + q) % n_pairs
                if first:
                    source = (tok_ref, grd_ref)[which]
                    block = source[pl.ds(SHIFT, WIN), :, pl.ds(p * pair, pair)].astype(f32)
                    block = block[:, SHIFT:SHIFT + WIN]
                else:
                    block = both_ref[which, pl.ds(i * WIN, WIN), :, pl.ds(p * pair, pair)]
                    block = block.astype(f32)
                    block = jnp.where(j == 0, block[:, :WIN], block[:, WIN:])
                block = block.reshape(WIN * WIN, pair)
                pieces.append(block[:, :C])
                pieces.append(block[:, C:])
            return jnp.concatenate(pieces, axis=0).T

        def scattered(values_t, i, j, l):
            rows = values_t.T
            for q in range(WIN // 2):
                p = (WIN // 2 * l + SHIFT // 2 + q) % n_pairs
                even = rows[2 * q * WIN * WIN:(2 * q + 1) * WIN * WIN]
                odd = rows[(2 * q + 1) * WIN * WIN:(2 * q + 2) * WIN * WIN]
                block = jnp.concatenate([even, odd], axis=1).reshape(WIN, WIN, pair)
                if first:
                    gs_ref[:, :, pl.ds(p * pair, pair)] = block
                else:
                    gs_ref[
                        pl.ds(i * WIN, WIN),
                        pl.ds(pl.multiple_of(j * WIN, WIN), WIN),
                        pl.ds(p * pair, pair),
                    ] = block

        def window(ij, l):
            i = ij // 2
            j = ij % 2
            w = ij * 2 + l
            x = gathered(0, i, j, l)
            row_mean = jnp.mean(x, axis=0, keepdims=True)
            centred = x - row_mean
            inv_std = lax.rsqrt(jnp.mean(centred * centred, axis=0, keepdims=True) + 1e-05)
            x_hat = centred * inv_std
            normed = (x_hat * gain).astype(bf16)
            qkv_t = jnp.dot(wqkvT_ref[...], normed, preferred_element_type=f32)
            qkv_s[...] = qkv_t.astype(bf16).astype(f32)
            g = gathered(1, i, j, l).astype(bf16)
            ga_t = jnp.dot(wp_ref[...], g, preferred_element_type=f32)
            ga_s[...] = ga_t.astype(bf16).astype(f32)
            allowed = kcol_ref[w] == krow_ref[w]

            def head_step(h, carry):
                qo = pl.multiple_of(h * HEAD, HEAD)
                q_t = qkv_s[pl.ds(qo, HEAD), :]
                k_t = qkv_s[pl.ds(qo + C, HEAD), :]
                v_t = qkv_s[pl.ds(qo + 2 * C, HEAD), :]
                ga_th = ga_s[pl.ds(qo, HEAD), :]
                q = q_t.T.astype(bf16)
                scores = jnp.dot(q, k_t.astype(bf16), preferred_element_type=f32) * SCALE
                weights = jnp.where(allowed, jnp.exp(scores), 0.0)
                probs = weights / jnp.sum(weights, axis=1, keepdims=True)
                probs_bf = probs.astype(bf16)
                att_t = lax.dot_general(v_t.astype(bf16), probs_bf, nt, preferred_element_type=f32)
                att_t = att_t.astype(bf16)
                gproj_ref[pl.ds(qo, HEAD), :] += lax.dot_general(
                    att_t, g, nt, preferred_element_type=f32
                )
                ga = ga_th.T.astype(bf16)
                grad_probs = jnp.dot(ga, v_t.astype(bf16), preferred_element_type=f32)
                dv_t = jnp.dot(ga_th.astype(bf16), probs_bf, preferred_element_type=f32)
                row_total = jnp.sum(probs * grad_probs, axis=1, keepdims=True)
                grad_scores = (probs * (grad_probs - row_total) * SCALE).astype(bf16)
                dq_t = lax.dot_general(k_t.astype(bf16), grad_scores, nt, preferred_element_type=f32)
                dk_t = jnp.dot(q_t.astype(bf16), grad_scores, preferred_element_type=f32)
                drow_s[pl.ds(qo, HEAD), :] = dq_t.astype(bf16).astype(f32)
                drow_s[pl.ds(qo + C, HEAD), :] = dk_t.astype(bf16).astype(f32)
                drow_s[pl.ds(qo + 2 * C, HEAD), :] = dv_t.astype(bf16).astype(f32)
                return carry

            lax.fori_loop(0, HEADS, head_step, 0, unroll=2)
            rows_t = drow_s[...].astype(bf16)
            gqkvT_ref[...] += lax.dot_general(rows_t, normed, nt, preferred_element_type=f32)
            grad_normed = jnp.dot(wqkv_ref[...], rows_t, preferred_element_type=f32)
            ggain_ref[...] += jnp.sum(grad_normed * x_hat, axis=1, keepdims=True)
            scaled = grad_normed * gain
            grad_shifted = inv_std * (
                scaled
                - jnp.mean(scaled, axis=0, keepdims=True)
                - x_hat * jnp.mean(scaled * x_hat, axis=0, keepdims=True)
            )
            scattered(grad_shifted.astype(bf16).astype(f32), i, j, l)

        def block_step(ij, carry):
            for l in range(2):
                window(ij, l)
            return carry

        if first:
            block_step(0, 0)
        else:
            lax.fori_loop(1, 4, block_step, 0)

    return window_kernel


def window_grads(first, arrays, kcol, krow, gain_col, wqkv_t, wqkv, wp, partial=()):
    if first:
        extent_a, extent_b, width = WIN, WIN, arrays[0].shape[2]
    else:
        extent_a, extent_b, width = arrays[0].shape[1:]
    return pl.pallas_call(
        make_window_kernel(first),
        out_shape=[
            jax.ShapeDtypeStruct((extent_a, extent_b, width), jnp.float32),
            jax.ShapeDtypeStruct((3 * C, C), jnp.float32),
            jax.ShapeDtypeStruct((C, C), jnp.float32),
            jax.ShapeDtypeStruct((C, 1), jnp.float32),
        ],
        scratch_shapes=[
            pltpu.VMEM((3 * C, CELLS), jnp.float32),
            pltpu.VMEM((C, CELLS), jnp.float32),
            pltpu.VMEM((3 * C, CELLS), jnp.float32),
        ],
    )(*arrays, kcol, krow, gain_col, wqkv_t, wqkv, wp, *partial)


SUM_AXES = ("gy", "gx", "gz")


def swapped(block, axis, distance):
    return lax.ppermute(block, axis, [(i, i ^ distance) for i in range(lax.axis_size(axis))])


def summed_everywhere(parts):
    sizes = [lax.axis_size(axis) for axis in SUM_AXES]
    if any(size & (size - 1) for size in sizes):
        return lax.psum(parts, SUM_AXES)
    flat = jnp.concatenate([part.reshape(-1) for part in parts])
    total = flat.shape[0]
    devices = 1
    for size in sizes:
        devices *= size
    padded = -(-total // devices) * devices
    values = jnp.pad(flat, (0, padded - total))
    steps = []
    for axis, size in zip(SUM_AXES, sizes):
        distance = 1
        while distance < size:
            bit = (lax.axis_index(axis) // distance) % 2
            half = values.shape[0] // 2
            keep = lax.dynamic_slice_in_dim(values, bit * half, half)
            send = lax.dynamic_slice_in_dim(values, (1 - bit) * half, half)
            values = keep + swapped(send, axis, distance)
            steps.append((axis, distance))
            distance *= 2
    for axis, distance in reversed(steps):
        bit = (lax.axis_index(axis) // distance) % 2
        other = swapped(values, axis, distance)
        values = jnp.where(
            bit == 0, jnp.concatenate([values, other]), jnp.concatenate([other, values])
        )
    out = []
    start = 0
    for part in parts:
        out.append(values[start : start + part.size].reshape(part.shape))
        start += part.size
    return tuple(out)


def halo_route(distance_a, distance_b):
    size_a = lax.axis_size("gx")
    size_b = lax.axis_size(("gy", "gz"))
    route = []
    for ia in range(size_a):
        for ib in range(size_b):
            target = ((ia + distance_a) % size_a) * size_b + (ib + distance_b) % size_b
            route.append((ia * size_b + ib, target))
    return route


def moved(block, distance_a, distance_b):
    return lax.ppermute(block, ("gx", "gy", "gz"), halo_route(distance_a, distance_b))


def shifted_block(both):
    from_a = moved(both[:, :SHIFT, SHIFT:], -1, 0)
    from_b = moved(both[:, SHIFT:, :SHIFT], 0, -1)
    from_ab = moved(both[:, :SHIFT, :SHIFT], -1, -1)
    upper = jnp.concatenate([both[:, SHIFT:, SHIFT:], from_b], axis=2)
    lower = jnp.concatenate([from_a, from_ab], axis=2)
    return jnp.concatenate([upper, lower], axis=1)


def unshifted_sum(grads_out, grad_shifted):
    narrow = grad_shifted.astype(jnp.bfloat16)
    to_a = moved(narrow[-SHIFT:, :-SHIFT], 1, 0).astype(jnp.float32)
    to_b = moved(narrow[:-SHIFT, -SHIFT:], 0, 1).astype(jnp.float32)
    to_ab = moved(narrow[-SHIFT:, -SHIFT:], 1, 1).astype(jnp.float32)
    upper = jnp.concatenate([to_ab, to_a], axis=1)
    lower = jnp.concatenate([to_b, grad_shifted[:-SHIFT, :-SHIFT]], axis=1)
    branch = jnp.concatenate([upper, lower], axis=0)
    return (grads_out.astype(jnp.float32) + branch.astype(jnp.float32)).astype(jnp.bfloat16)


def per_device(tokens, grads_out, labels, ln_gain, qkv_weight, proj_weight):
    brick_a, brick_b = (tokens.shape[0], tokens.shape[1])
    brick_c = NZ
    channels = C
    both = shifted_block(jnp.stack([tokens, grads_out]))
    extent_a = brick_a * lax.axis_size("gx")
    extent_b = brick_b * lax.axis_size(("gy", "gz"))
    first_index = lax.axis_index("gx") * brick_a + jnp.arange(brick_a, dtype=jnp.int32)
    second_index = lax.axis_index(("gy", "gz")) * brick_b + jnp.arange(brick_b, dtype=jnp.int32)
    wrap_first = (first_index >= extent_a - SHIFT).astype(jnp.int32)
    wrap_second = (second_index >= extent_b - SHIFT).astype(jnp.int32)
    wrap_third = (jnp.arange(brick_c, dtype=jnp.int32) >= brick_c - SHIFT).astype(jnp.int32)
    region = (
        wrap_first[:, None, None] * 4 + wrap_second[None, :, None] * 2 + wrap_third[None, None, :]
    )
    mask_key = to_windows_key(labels * 8 + region)

    constants = (
        mask_key[:, :, None],
        mask_key[:, None, :],
        ln_gain.reshape(channels, 1),
        qkv_weight.T,
        qkv_weight,
        proj_weight,
    )
    partial = window_grads(True, (tokens, grads_out), *constants)
    grad_branch, qkv_grad_t, proj_grad, gain_grad = window_grads(
        False, (both,), *constants, partial=partial
    )
    qkv_grad_t, proj_grad, gain_grad = summed_everywhere((qkv_grad_t, proj_grad, gain_grad))
    qkv_grad = qkv_grad_t.T
    grad_tokens = unshifted_sum(grads_out, grad_branch)
    return (grad_tokens, gain_grad.reshape(-1), qkv_grad.reshape(-1), proj_grad.reshape(-1))


def solution(mesh):
    return jax.shard_map(
        per_device,
        mesh=mesh,
        in_specs=(
            P("gx", ("gy", "gz"), None),
            P("gx", ("gy", "gz"), None),
            P("gx", ("gy", "gz"), None),
            P(),
            P(),
            P(),
        ),
        out_specs=(P("gx", ("gy", "gz"), None), P(), P(), P()),
        check_vma=False,
    )
```

```python
import jax
import jax.numpy as jnp
from jax import lax
from jax.experimental import pallas as pl
from jax.experimental.pallas import tpu as pltpu
from jax.sharding import PartitionSpec as P

HEADS = 6
C = 192
WIN = 8
SHIFT = 4
NZ = 16
CELLS = WIN**3
HEAD = C // HEADS
SCALE = HEAD ** (-0.5)


def passed_along(block, axis, distance):
    devices = range(lax.axis_size(axis))
    route = [((i - distance) % len(devices), i) for i in devices]
    return lax.ppermute(block, axis, route)


def to_windows_cm(values):
    extent_a, extent_b, extent_c, ch = values.shape
    shaped = values.reshape(extent_a // WIN, WIN, extent_b // WIN, WIN, extent_c // WIN, WIN, ch)
    return shaped.transpose(0, 2, 4, 6, 1, 3, 5).reshape(-1, ch, CELLS)


def from_windows_cm(values, extent_a, extent_b, extent_c):
    ch = values.shape[1]
    shaped = values.reshape(extent_a // WIN, extent_b // WIN, extent_c // WIN, ch, WIN, WIN, WIN)
    return shaped.transpose(0, 4, 1, 5, 2, 6, 3).reshape(extent_a, extent_b, extent_c, ch)


def to_windows_key(values):
    extent_a, extent_b, extent_c = values.shape
    shaped = values.reshape(extent_a // WIN, WIN, extent_b // WIN, WIN, extent_c // WIN, WIN)
    return shaped.transpose(0, 2, 4, 5, 1, 3).reshape(-1, CELLS)


def make_window_kernel(first):
    def window_kernel(*refs):
        if first:
            (tok_ref, grd_ref, kcol_ref, krow_ref, gain_ref, wqkvT_ref, wqkv_ref, wp_ref,
             gs_ref, gqkvT_ref, gproj_ref, ggain_ref, qkv_s, ga_s, drow_s) = refs
        else:
            (both_ref, kcol_ref, krow_ref, gain_ref, wqkvT_ref, wqkv_ref, wp_ref,
             gs0_ref, gqkvT0_ref, gproj0_ref, ggain0_ref,
             gs_ref, gqkvT_ref, gproj_ref, ggain_ref, qkv_s, ga_s, drow_s) = refs
        f32 = jnp.float32
        bf16 = jnp.bfloat16
        if first:
            gqkvT_ref[...] = jnp.zeros_like(gqkvT_ref)
            gproj_ref[...] = jnp.zeros_like(gproj_ref)
            ggain_ref[...] = jnp.zeros_like(ggain_ref)
        else:
            gqkvT_ref[...] = gqkvT0_ref[...]
            gproj_ref[...] = gproj0_ref[...]
            ggain_ref[...] = ggain0_ref[...]
            gs_ref[pl.ds(0, WIN), pl.ds(0, WIN), :] = gs0_ref[...]
        gain = gain_ref[...]
        nt = (((1,), (1,)), ((), ()))
        pair = 2 * C
        n_pairs = NZ // 2

        def gathered(which, i, j, l):
            pieces = []
            for q in range(WIN // 2):
                p = (WIN // 2 * l + SHIFT // 2 + q) % n_pairs
                if first:
                    source = (tok_ref, grd_ref)[which]
                    block = source[pl.ds(SHIFT, WIN), :, pl.ds(p * pair, pair)].astype(f32)
                    block = block[:, SHIFT:SHIFT + WIN]
                else:
                    block = both_ref[which, pl.ds(i * WIN, WIN), :, pl.ds(p * pair, pair)]
                    block = block.astype(f32)
                    block = jnp.where(j == 0, block[:, :WIN], block[:, WIN:])
                block = block.reshape(WIN * WIN, pair)
                pieces.append(block[:, :C])
                pieces.append(block[:, C:])
            return jnp.concatenate(pieces, axis=0).T

        def scattered(values_t, i, j, l):
            rows = values_t.T
            for q in range(WIN // 2):
                p = (WIN // 2 * l + SHIFT // 2 + q) % n_pairs
                even = rows[2 * q * WIN * WIN:(2 * q + 1) * WIN * WIN]
                odd = rows[(2 * q + 1) * WIN * WIN:(2 * q + 2) * WIN * WIN]
                block = jnp.concatenate([even, odd], axis=1).reshape(WIN, WIN, pair)
                if first:
                    gs_ref[:, :, pl.ds(p * pair, pair)] = block
                else:
                    gs_ref[
                        pl.ds(i * WIN, WIN),
                        pl.ds(pl.multiple_of(j * WIN, WIN), WIN),
                        pl.ds(p * pair, pair),
                    ] = block

        def window(ij, l):
            i = ij // 2
            j = ij % 2
            w = ij * 2 + l
            x = gathered(0, i, j, l)
            row_mean = jnp.mean(x, axis=0, keepdims=True)
            centred = x - row_mean
            inv_std = lax.rsqrt(jnp.mean(centred * centred, axis=0, keepdims=True) + 1e-05)
            x_hat = centred * inv_std
            normed = (x_hat * gain).astype(bf16)
            qkv_t = jnp.dot(wqkvT_ref[...], normed, preferred_element_type=f32)
            qkv_s[...] = qkv_t.astype(bf16).astype(f32)
            g = gathered(1, i, j, l).astype(bf16)
            ga_t = jnp.dot(wp_ref[...], g, preferred_element_type=f32)
            ga_s[...] = ga_t.astype(bf16).astype(f32)
            allowed = kcol_ref[w] == krow_ref[w]

            def head_step(h, carry):
                qo = pl.multiple_of(h * HEAD, HEAD)
                q_t = qkv_s[pl.ds(qo, HEAD), :]
                k_t = qkv_s[pl.ds(qo + C, HEAD), :]
                v_t = qkv_s[pl.ds(qo + 2 * C, HEAD), :]
                ga_th = ga_s[pl.ds(qo, HEAD), :]
                q = q_t.T.astype(bf16)
                scores = jnp.dot(q, k_t.astype(bf16), preferred_element_type=f32) * SCALE
                weights = jnp.where(allowed, jnp.exp(scores), 0.0)
                probs = weights / jnp.sum(weights, axis=1, keepdims=True)
                probs_bf = probs.astype(bf16)
                att_t = lax.dot_general(v_t.astype(bf16), probs_bf, nt, preferred_element_type=f32)
                att_t = att_t.astype(bf16)
                gproj_ref[pl.ds(qo, HEAD), :] += lax.dot_general(
                    att_t, g, nt, preferred_element_type=f32
                )
                ga = ga_th.T.astype(bf16)
                grad_probs = jnp.dot(ga, v_t.astype(bf16), preferred_element_type=f32)
                dv_t = jnp.dot(ga_th.astype(bf16), probs_bf, preferred_element_type=f32)
                row_total = jnp.sum(probs * grad_probs, axis=1, keepdims=True)
                grad_scores = (probs * (grad_probs - row_total) * SCALE).astype(bf16)
                dq_t = lax.dot_general(k_t.astype(bf16), grad_scores, nt, preferred_element_type=f32)
                dk_t = jnp.dot(q_t.astype(bf16), grad_scores, preferred_element_type=f32)
                drow_s[pl.ds(qo, HEAD), :] = dq_t.astype(bf16).astype(f32)
                drow_s[pl.ds(qo + C, HEAD), :] = dk_t.astype(bf16).astype(f32)
                drow_s[pl.ds(qo + 2 * C, HEAD), :] = dv_t.astype(bf16).astype(f32)
                return carry

            lax.fori_loop(0, HEADS, head_step, 0, unroll=3)
            rows_t = drow_s[...].astype(bf16)
            gqkvT_ref[...] += lax.dot_general(rows_t, normed, nt, preferred_element_type=f32)
            grad_normed = jnp.dot(wqkv_ref[...], rows_t, preferred_element_type=f32)
            ggain_ref[...] += jnp.sum(grad_normed * x_hat, axis=1, keepdims=True)
            scaled = grad_normed * gain
            grad_shifted = inv_std * (
                scaled
                - jnp.mean(scaled, axis=0, keepdims=True)
                - x_hat * jnp.mean(scaled * x_hat, axis=0, keepdims=True)
            )
            scattered(grad_shifted.astype(bf16).astype(f32), i, j, l)

        def block_step(ij, carry):
            for l in range(2):
                window(ij, l)
            return carry

        if first:
            block_step(0, 0)
        else:
            lax.fori_loop(1, 4, block_step, 0)

    return window_kernel


def window_grads(first, arrays, kcol, krow, gain_col, wqkv_t, wqkv, wp, partial=()):
    if first:
        extent_a, extent_b, width = WIN, WIN, arrays[0].shape[2]
    else:
        extent_a, extent_b, width = arrays[0].shape[1:]
    return pl.pallas_call(
        make_window_kernel(first),
        out_shape=[
            jax.ShapeDtypeStruct((extent_a, extent_b, width), jnp.float32),
            jax.ShapeDtypeStruct((3 * C, C), jnp.float32),
            jax.ShapeDtypeStruct((C, C), jnp.float32),
            jax.ShapeDtypeStruct((C, 1), jnp.float32),
        ],
        scratch_shapes=[
            pltpu.VMEM((3 * C, CELLS), jnp.float32),
            pltpu.VMEM((C, CELLS), jnp.float32),
            pltpu.VMEM((3 * C, CELLS), jnp.float32),
        ],
    )(*arrays, kcol, krow, gain_col, wqkv_t, wqkv, wp, *partial)


SUM_AXES = ("gy", "gx", "gz")


def swapped(block, axis, distance):
    return lax.ppermute(block, axis, [(i, i ^ distance) for i in range(lax.axis_size(axis))])


def summed_everywhere(parts):
    sizes = [lax.axis_size(axis) for axis in SUM_AXES]
    if any(size & (size - 1) for size in sizes):
        return lax.psum(parts, SUM_AXES)
    flat = jnp.concatenate([part.reshape(-1) for part in parts])
    total = flat.shape[0]
    devices = 1
    for size in sizes:
        devices *= size
    padded = -(-total // devices) * devices
    values = jnp.pad(flat, (0, padded - total))
    steps = []
    for axis, size in zip(SUM_AXES, sizes):
        distance = 1
        while distance < size:
            bit = (lax.axis_index(axis) // distance) % 2
            half = values.shape[0] // 2
            keep = lax.dynamic_slice_in_dim(values, bit * half, half)
            send = lax.dynamic_slice_in_dim(values, (1 - bit) * half, half)
            values = keep + swapped(send, axis, distance)
            steps.append((axis, distance))
            distance *= 2
    for axis, distance in reversed(steps):
        bit = (lax.axis_index(axis) // distance) % 2
        other = swapped(values, axis, distance)
        values = jnp.where(
            bit == 0, jnp.concatenate([values, other]), jnp.concatenate([other, values])
        )
    out = []
    start = 0
    for part in parts:
        out.append(values[start : start + part.size].reshape(part.shape))
        start += part.size
    return tuple(out)


def halo_route(distance_a, distance_b):
    size_a = lax.axis_size("gx")
    size_b = lax.axis_size(("gy", "gz"))
    route = []
    for ia in range(size_a):
        for ib in range(size_b):
            target = ((ia + distance_a) % size_a) * size_b + (ib + distance_b) % size_b
            route.append((ia * size_b + ib, target))
    return route


def moved(block, distance_a, distance_b):
    return lax.ppermute(block, ("gx", "gy", "gz"), halo_route(distance_a, distance_b))


def shifted_block(both):
    from_a = moved(both[:, :SHIFT, SHIFT:], -1, 0)
    from_b = moved(both[:, SHIFT:, :SHIFT], 0, -1)
    from_ab = moved(both[:, :SHIFT, :SHIFT], -1, -1)
    upper = jnp.concatenate([both[:, SHIFT:, SHIFT:], from_b], axis=2)
    lower = jnp.concatenate([from_a, from_ab], axis=2)
    return jnp.concatenate([upper, lower], axis=1)


def unshifted_sum(grads_out, grad_shifted):
    narrow = grad_shifted.astype(jnp.bfloat16)
    to_a = moved(narrow[-SHIFT:, :-SHIFT], 1, 0).astype(jnp.float32)
    to_b = moved(narrow[:-SHIFT, -SHIFT:], 0, 1).astype(jnp.float32)
    to_ab = moved(narrow[-SHIFT:, -SHIFT:], 1, 1).astype(jnp.float32)
    upper = jnp.concatenate([to_ab, to_a], axis=1)
    lower = jnp.concatenate([to_b, grad_shifted[:-SHIFT, :-SHIFT]], axis=1)
    branch = jnp.concatenate([upper, lower], axis=0)
    return (grads_out.astype(jnp.float32) + branch.astype(jnp.float32)).astype(jnp.bfloat16)


def per_device(tokens, grads_out, labels, ln_gain, qkv_weight, proj_weight):
    brick_a, brick_b = (tokens.shape[0], tokens.shape[1])
    brick_c = NZ
    channels = C
    both = shifted_block(jnp.stack([tokens, grads_out]))
    extent_a = brick_a * lax.axis_size("gx")
    extent_b = brick_b * lax.axis_size(("gy", "gz"))
    first_index = lax.axis_index("gx") * brick_a + jnp.arange(brick_a, dtype=jnp.int32)
    second_index = lax.axis_index(("gy", "gz")) * brick_b + jnp.arange(brick_b, dtype=jnp.int32)
    wrap_first = (first_index >= extent_a - SHIFT).astype(jnp.int32)
    wrap_second = (second_index >= extent_b - SHIFT).astype(jnp.int32)
    wrap_third = (jnp.arange(brick_c, dtype=jnp.int32) >= brick_c - SHIFT).astype(jnp.int32)
    region = (
        wrap_first[:, None, None] * 4 + wrap_second[None, :, None] * 2 + wrap_third[None, None, :]
    )
    mask_key = to_windows_key(labels * 8 + region)

    constants = (
        mask_key[:, :, None],
        mask_key[:, None, :],
        ln_gain.reshape(channels, 1),
        qkv_weight.T,
        qkv_weight,
        proj_weight,
    )
    partial = window_grads(True, (tokens, grads_out), *constants)
    grad_branch, qkv_grad_t, proj_grad, gain_grad = window_grads(
        False, (both,), *constants, partial=partial
    )
    qkv_grad_t, proj_grad, gain_grad = summed_everywhere((qkv_grad_t, proj_grad, gain_grad))
    qkv_grad = qkv_grad_t.T
    grad_tokens = unshifted_sum(grads_out, grad_branch)
    return (grad_tokens, gain_grad.reshape(-1), qkv_grad.reshape(-1), proj_grad.reshape(-1))


def solution(mesh):
    return jax.shard_map(
        per_device,
        mesh=mesh,
        in_specs=(
            P("gx", ("gy", "gz"), None),
            P("gx", ("gy", "gz"), None),
            P("gx", ("gy", "gz"), None),
            P(),
            P(),
            P(),
        ),
        out_specs=(P("gx", ("gy", "gz"), None), P(), P(), P()),
        check_vma=False,
    )
```

```python
import jax
import jax.numpy as jnp
from jax import lax
from jax.experimental import pallas as pl
from jax.experimental.pallas import tpu as pltpu
from jax.sharding import PartitionSpec as P

HEADS = 6
C = 192
WIN = 8
SHIFT = 4
NZ = 16
CELLS = WIN**3
HEAD = C // HEADS
SCALE = HEAD ** (-0.5)


def passed_along(block, axis, distance):
    devices = range(lax.axis_size(axis))
    route = [((i - distance) % len(devices), i) for i in devices]
    return lax.ppermute(block, axis, route)


def to_windows_cm(values):
    extent_a, extent_b, extent_c, ch = values.shape
    shaped = values.reshape(extent_a // WIN, WIN, extent_b // WIN, WIN, extent_c // WIN, WIN, ch)
    return shaped.transpose(0, 2, 4, 6, 1, 3, 5).reshape(-1, ch, CELLS)


def from_windows_cm(values, extent_a, extent_b, extent_c):
    ch = values.shape[1]
    shaped = values.reshape(extent_a // WIN, extent_b // WIN, extent_c // WIN, ch, WIN, WIN, WIN)
    return shaped.transpose(0, 4, 1, 5, 2, 6, 3).reshape(extent_a, extent_b, extent_c, ch)


def to_windows_key(values):
    extent_a, extent_b, extent_c = values.shape
    shaped = values.reshape(extent_a // WIN, WIN, extent_b // WIN, WIN, extent_c // WIN, WIN)
    return shaped.transpose(0, 2, 4, 5, 1, 3).reshape(-1, CELLS)


def make_window_kernel(first):
    def window_kernel(*refs):
        if first:
            (tok_ref, grd_ref, kcol_ref, krow_ref, gain_ref, wqkvT_ref, wqkv_ref, wp_ref,
             gs_ref, gqkvT_ref, gproj_ref, ggain_ref, qkv_s, ga_s, drow_s) = refs
        else:
            (both_ref, kcol_ref, krow_ref, gain_ref, wqkvT_ref, wqkv_ref, wp_ref,
             gs0_ref, gqkvT0_ref, gproj0_ref, ggain0_ref,
             gs_ref, gqkvT_ref, gproj_ref, ggain_ref, qkv_s, ga_s, drow_s) = refs
        f32 = jnp.float32
        bf16 = jnp.bfloat16
        if first:
            gqkvT_ref[...] = jnp.zeros_like(gqkvT_ref)
            gproj_ref[...] = jnp.zeros_like(gproj_ref)
            ggain_ref[...] = jnp.zeros_like(ggain_ref)
        else:
            gqkvT_ref[...] = gqkvT0_ref[...]
            gproj_ref[...] = gproj0_ref[...]
            ggain_ref[...] = ggain0_ref[...]
            gs_ref[pl.ds(0, WIN), pl.ds(0, WIN), :] = gs0_ref[...]
        gain = gain_ref[...]
        nt = (((1,), (1,)), ((), ()))
        pair = 2 * C
        n_pairs = NZ // 2

        def gathered(which, i, j, l):
            pieces = []
            for q in range(WIN // 2):
                p = (WIN // 2 * l + SHIFT // 2 + q) % n_pairs
                if first:
                    source = (tok_ref, grd_ref)[which]
                    block = source[pl.ds(SHIFT, WIN), :, pl.ds(p * pair, pair)].astype(f32)
                    block = block[:, SHIFT:SHIFT + WIN]
                else:
                    block = both_ref[which, pl.ds(i * WIN, WIN), :, pl.ds(p * pair, pair)]
                    block = block.astype(f32)
                    block = jnp.where(j == 0, block[:, :WIN], block[:, WIN:])
                block = block.reshape(WIN * WIN, pair)
                pieces.append(block[:, :C])
                pieces.append(block[:, C:])
            return jnp.concatenate(pieces, axis=0).T

        def scattered(values_t, i, j, l):
            rows = values_t.T
            for q in range(WIN // 2):
                p = (WIN // 2 * l + SHIFT // 2 + q) % n_pairs
                even = rows[2 * q * WIN * WIN:(2 * q + 1) * WIN * WIN]
                odd = rows[(2 * q + 1) * WIN * WIN:(2 * q + 2) * WIN * WIN]
                block = jnp.concatenate([even, odd], axis=1).reshape(WIN, WIN, pair)
                if first:
                    gs_ref[:, :, pl.ds(p * pair, pair)] = block
                else:
                    gs_ref[
                        pl.ds(i * WIN, WIN),
                        pl.ds(pl.multiple_of(j * WIN, WIN), WIN),
                        pl.ds(p * pair, pair),
                    ] = block

        def window(ij, l):
            i = ij // 2
            j = ij % 2
            w = ij * 2 + l
            x = gathered(0, i, j, l)
            row_mean = jnp.mean(x, axis=0, keepdims=True)
            centred = x - row_mean
            inv_std = lax.rsqrt(jnp.mean(centred * centred, axis=0, keepdims=True) + 1e-05)
            x_hat = centred * inv_std
            normed = (x_hat * gain).astype(bf16)
            qkv_t = jnp.dot(wqkvT_ref[...], normed, preferred_element_type=f32)
            qkv_s[...] = qkv_t.astype(bf16).astype(f32)
            g = gathered(1, i, j, l).astype(bf16)
            ga_t = jnp.dot(wp_ref[...], g, preferred_element_type=f32)
            ga_s[...] = ga_t.astype(bf16).astype(f32)
            allowed = kcol_ref[w] == krow_ref[w]

            def head_step(h, carry):
                qo = pl.multiple_of(h * HEAD, HEAD)
                q_t = qkv_s[pl.ds(qo, HEAD), :]
                k_t = qkv_s[pl.ds(qo + C, HEAD), :]
                v_t = qkv_s[pl.ds(qo + 2 * C, HEAD), :]
                ga_th = ga_s[pl.ds(qo, HEAD), :]
                q = q_t.T.astype(bf16)
                scores = jnp.dot(q, k_t.astype(bf16), preferred_element_type=f32) * SCALE
                weights = jnp.where(allowed, jnp.exp(scores), 0.0)
                probs = weights / jnp.sum(weights, axis=1, keepdims=True)
                probs_bf = probs.astype(bf16)
                att_t = lax.dot_general(v_t.astype(bf16), probs_bf, nt, preferred_element_type=f32)
                att_t = att_t.astype(bf16)
                gproj_ref[pl.ds(qo, HEAD), :] += lax.dot_general(
                    att_t, g, nt, preferred_element_type=f32
                )
                ga = ga_th.T.astype(bf16)
                grad_probs = jnp.dot(ga, v_t.astype(bf16), preferred_element_type=f32)
                dv_t = jnp.dot(ga_th.astype(bf16), probs_bf, preferred_element_type=f32)
                row_total = jnp.sum(probs * grad_probs, axis=1, keepdims=True)
                grad_scores = (probs * (grad_probs - row_total) * SCALE).astype(bf16)
                dq_t = lax.dot_general(k_t.astype(bf16), grad_scores, nt, preferred_element_type=f32)
                dk_t = jnp.dot(q_t.astype(bf16), grad_scores, preferred_element_type=f32)
                drow_s[pl.ds(qo, HEAD), :] = dq_t.astype(bf16).astype(f32)
                drow_s[pl.ds(qo + C, HEAD), :] = dk_t.astype(bf16).astype(f32)
                drow_s[pl.ds(qo + 2 * C, HEAD), :] = dv_t.astype(bf16).astype(f32)
                return carry

            lax.fori_loop(0, HEADS, head_step, 0, unroll=3)
            rows_t = drow_s[...].astype(bf16)
            gqkvT_ref[...] += lax.dot_general(normed, rows_t, nt, preferred_element_type=f32)
            grad_normed = jnp.dot(wqkv_ref[...], rows_t, preferred_element_type=f32)
            ggain_ref[...] += jnp.sum(grad_normed * x_hat, axis=1, keepdims=True)
            scaled = grad_normed * gain
            grad_shifted = inv_std * (
                scaled
                - jnp.mean(scaled, axis=0, keepdims=True)
                - x_hat * jnp.mean(scaled * x_hat, axis=0, keepdims=True)
            )
            scattered(grad_shifted.astype(bf16).astype(f32), i, j, l)

        def block_step(ij, carry):
            for l in range(2):
                window(ij, l)
            return carry

        if first:
            block_step(0, 0)
        else:
            lax.fori_loop(1, 4, block_step, 0)

    return window_kernel


def window_grads(first, arrays, kcol, krow, gain_col, wqkv_t, wqkv, wp, partial=()):
    if first:
        extent_a, extent_b, width = WIN, WIN, arrays[0].shape[2]
    else:
        extent_a, extent_b, width = arrays[0].shape[1:]
    return pl.pallas_call(
        make_window_kernel(first),
        out_shape=[
            jax.ShapeDtypeStruct((extent_a, extent_b, width), jnp.float32),
            jax.ShapeDtypeStruct((C, 3 * C), jnp.float32),
            jax.ShapeDtypeStruct((C, C), jnp.float32),
            jax.ShapeDtypeStruct((C, 1), jnp.float32),
        ],
        scratch_shapes=[
            pltpu.VMEM((3 * C, CELLS), jnp.float32),
            pltpu.VMEM((C, CELLS), jnp.float32),
            pltpu.VMEM((3 * C, CELLS), jnp.float32),
        ],
    )(*arrays, kcol, krow, gain_col, wqkv_t, wqkv, wp, *partial)


SUM_AXES = ("gy", "gx", "gz")


def swapped(block, axis, distance):
    return lax.ppermute(block, axis, [(i, i ^ distance) for i in range(lax.axis_size(axis))])


def summed_everywhere(matrix):
    sizes = [lax.axis_size(axis) for axis in SUM_AXES]
    if any(size & (size - 1) for size in sizes):
        return lax.psum(matrix, SUM_AXES)
    devices = 1
    for size in sizes:
        devices *= size
    unit = devices * 8 if devices * 8 <= 2 * matrix.shape[0] else devices
    padded = -(-matrix.shape[0] // unit) * unit
    values = jnp.pad(matrix, ((0, padded - matrix.shape[0]), (0, 0)))
    steps = []
    for axis, size in zip(SUM_AXES, sizes):
        distance = 1
        while distance < size:
            bit = (lax.axis_index(axis) // distance) % 2
            half = values.shape[0] // 2
            keep = lax.dynamic_slice_in_dim(values, bit * half, half)
            send = lax.dynamic_slice_in_dim(values, (1 - bit) * half, half)
            values = keep + swapped(send, axis, distance)
            steps.append((axis, distance))
            distance *= 2
    for axis, distance in reversed(steps):
        bit = (lax.axis_index(axis) // distance) % 2
        other = swapped(values, axis, distance)
        values = jnp.where(
            bit == 0, jnp.concatenate([values, other]), jnp.concatenate([other, values])
        )
    return values[: matrix.shape[0]]


def halo_route(distance_a, distance_b):
    size_a = lax.axis_size("gx")
    size_b = lax.axis_size(("gy", "gz"))
    route = []
    for ia in range(size_a):
        for ib in range(size_b):
            target = ((ia + distance_a) % size_a) * size_b + (ib + distance_b) % size_b
            route.append((ia * size_b + ib, target))
    return route


def moved(block, distance_a, distance_b):
    return lax.ppermute(block, ("gx", "gy", "gz"), halo_route(distance_a, distance_b))


def shifted_block(both):
    from_a = moved(both[:, :SHIFT, SHIFT:], -1, 0)
    from_b = moved(both[:, SHIFT:, :SHIFT], 0, -1)
    from_ab = moved(both[:, :SHIFT, :SHIFT], -1, -1)
    upper = jnp.concatenate([both[:, SHIFT:, SHIFT:], from_b], axis=2)
    lower = jnp.concatenate([from_a, from_ab], axis=2)
    return jnp.concatenate([upper, lower], axis=1)


def unshifted_sum(grads_out, grad_shifted):
    narrow = grad_shifted.astype(jnp.bfloat16)
    to_a = moved(narrow[-SHIFT:, :-SHIFT], 1, 0).astype(jnp.float32)
    to_b = moved(narrow[:-SHIFT, -SHIFT:], 0, 1).astype(jnp.float32)
    to_ab = moved(narrow[-SHIFT:, -SHIFT:], 1, 1).astype(jnp.float32)
    upper = jnp.concatenate([to_ab, to_a], axis=1)
    lower = jnp.concatenate([to_b, grad_shifted[:-SHIFT, :-SHIFT]], axis=1)
    branch = jnp.concatenate([upper, lower], axis=0)
    return (grads_out.astype(jnp.float32) + branch.astype(jnp.float32)).astype(jnp.bfloat16)


def per_device(tokens, grads_out, labels, ln_gain, qkv_weight, proj_weight):
    brick_a, brick_b = (tokens.shape[0], tokens.shape[1])
    brick_c = NZ
    channels = C
    both = shifted_block(jnp.stack([tokens, grads_out]))
    extent_a = brick_a * lax.axis_size("gx")
    extent_b = brick_b * lax.axis_size(("gy", "gz"))
    first_index = lax.axis_index("gx") * brick_a + jnp.arange(brick_a, dtype=jnp.int32)
    second_index = lax.axis_index(("gy", "gz")) * brick_b + jnp.arange(brick_b, dtype=jnp.int32)
    wrap_first = (first_index >= extent_a - SHIFT).astype(jnp.int32)
    wrap_second = (second_index >= extent_b - SHIFT).astype(jnp.int32)
    wrap_third = (jnp.arange(brick_c, dtype=jnp.int32) >= brick_c - SHIFT).astype(jnp.int32)
    region = (
        wrap_first[:, None, None] * 4 + wrap_second[None, :, None] * 2 + wrap_third[None, None, :]
    )
    mask_key = to_windows_key(labels * 8 + region)

    constants = (
        mask_key[:, :, None],
        mask_key[:, None, :],
        ln_gain.reshape(channels, 1),
        qkv_weight.T,
        qkv_weight,
        proj_weight,
    )
    partial = window_grads(True, (tokens, grads_out), *constants)
    grad_branch, qkv_part, proj_grad, gain_grad = window_grads(
        False, (both,), *constants, partial=partial
    )
    width = 4 * channels
    gain_row = jnp.pad(gain_grad.reshape(1, channels), ((0, 0), (0, width - channels)))
    summed = summed_everywhere(
        jnp.concatenate([jnp.concatenate([qkv_part, proj_grad], axis=1), gain_row], axis=0)
    )
    qkv_grad = summed[:channels, : 3 * channels]
    proj_grad = summed[:channels, 3 * channels :]
    gain_grad = summed[channels, :channels]
    grad_tokens = unshifted_sum(grads_out, grad_branch)
    return (grad_tokens, gain_grad.reshape(-1), qkv_grad.reshape(-1), proj_grad.reshape(-1))


def solution(mesh):
    return jax.shard_map(
        per_device,
        mesh=mesh,
        in_specs=(
            P("gx", ("gy", "gz"), None),
            P("gx", ("gy", "gz"), None),
            P("gx", ("gy", "gz"), None),
            P(),
            P(),
            P(),
        ),
        out_specs=(P("gx", ("gy", "gz"), None), P(), P(), P()),
        check_vma=False,
    )
```

```python
import jax
import jax.numpy as jnp
from jax import lax
from jax.experimental import pallas as pl
from jax.experimental.pallas import tpu as pltpu
from jax.sharding import PartitionSpec as P

HEADS = 6
C = 192
WIN = 8
SHIFT = 4
NZ = 16
CELLS = WIN**3
HEAD = C // HEADS
SCALE = HEAD ** (-0.5)


def passed_along(block, axis, distance):
    devices = range(lax.axis_size(axis))
    route = [((i - distance) % len(devices), i) for i in devices]
    return lax.ppermute(block, axis, route)


def to_windows_cm(values):
    extent_a, extent_b, extent_c, ch = values.shape
    shaped = values.reshape(extent_a // WIN, WIN, extent_b // WIN, WIN, extent_c // WIN, WIN, ch)
    return shaped.transpose(0, 2, 4, 6, 1, 3, 5).reshape(-1, ch, CELLS)


def from_windows_cm(values, extent_a, extent_b, extent_c):
    ch = values.shape[1]
    shaped = values.reshape(extent_a // WIN, extent_b // WIN, extent_c // WIN, ch, WIN, WIN, WIN)
    return shaped.transpose(0, 4, 1, 5, 2, 6, 3).reshape(extent_a, extent_b, extent_c, ch)


def to_windows_key(values):
    extent_a, extent_b, extent_c = values.shape
    shaped = values.reshape(extent_a // WIN, WIN, extent_b // WIN, WIN, extent_c // WIN, WIN)
    return shaped.transpose(0, 2, 4, 5, 1, 3).reshape(-1, CELLS)


def make_window_kernel(first):
    def window_kernel(*refs):
        if first:
            (tok_ref, grd_ref, krow_ref, gain_ref, wqkv_ref, wp_ref,
             gs_ref, gqkvT_ref, gproj_ref, ggain_ref, qkv_s, ga_s, drow_s) = refs
        else:
            (both_ref, krow_ref, gain_ref, wqkv_ref, wp_ref,
             gs0_ref, gqkvT0_ref, gproj0_ref, ggain0_ref,
             gs_ref, gqkvT_ref, gproj_ref, ggain_ref, qkv_s, ga_s, drow_s) = refs
        f32 = jnp.float32
        bf16 = jnp.bfloat16
        if first:
            gqkvT_ref[...] = jnp.zeros_like(gqkvT_ref)
            gproj_ref[...] = jnp.zeros_like(gproj_ref)
            ggain_ref[...] = jnp.zeros_like(ggain_ref)
        else:
            gqkvT_ref[...] = gqkvT0_ref[...]
            gproj_ref[...] = gproj0_ref[...]
            ggain_ref[...] = ggain0_ref[...]
            gs_ref[pl.ds(0, WIN), pl.ds(0, WIN), :] = gs0_ref[...]
        gain = jnp.broadcast_to(gain_ref[...], (8, C)).T[:, 0:1]
        wqkv_t = wqkv_ref[...].astype(f32).T.astype(bf16)
        nt = (((1,), (1,)), ((), ()))
        pair = 2 * C
        n_pairs = NZ // 2

        def gathered(which, i, j, l):
            pieces = []
            for q in range(WIN // 2):
                p = (WIN // 2 * l + SHIFT // 2 + q) % n_pairs
                if first:
                    source = (tok_ref, grd_ref)[which]
                    block = source[pl.ds(SHIFT, WIN), :, pl.ds(p * pair, pair)].astype(f32)
                    block = block[:, SHIFT:SHIFT + WIN]
                else:
                    block = both_ref[which, pl.ds(i * WIN, WIN), :, pl.ds(p * pair, pair)]
                    block = block.astype(f32)
                    block = jnp.where(j == 0, block[:, :WIN], block[:, WIN:])
                block = block.reshape(WIN * WIN, pair)
                pieces.append(block[:, :C])
                pieces.append(block[:, C:])
            return jnp.concatenate(pieces, axis=0).T

        def scattered(values_t, i, j, l):
            rows = values_t.T
            for q in range(WIN // 2):
                p = (WIN // 2 * l + SHIFT // 2 + q) % n_pairs
                even = rows[2 * q * WIN * WIN:(2 * q + 1) * WIN * WIN]
                odd = rows[(2 * q + 1) * WIN * WIN:(2 * q + 2) * WIN * WIN]
                block = jnp.concatenate([even, odd], axis=1).reshape(WIN, WIN, pair)
                if first:
                    gs_ref[:, :, pl.ds(p * pair, pair)] = block
                else:
                    gs_ref[
                        pl.ds(i * WIN, WIN),
                        pl.ds(pl.multiple_of(j * WIN, WIN), WIN),
                        pl.ds(p * pair, pair),
                    ] = block

        def window(ij, l):
            i = ij // 2
            j = ij % 2
            w = ij * 2 + l
            x = gathered(0, i, j, l)
            row_mean = jnp.mean(x, axis=0, keepdims=True)
            centred = x - row_mean
            inv_std = lax.rsqrt(jnp.mean(centred * centred, axis=0, keepdims=True) + 1e-05)
            x_hat = centred * inv_std
            normed = (x_hat * gain).astype(bf16)
            qkv_t = jnp.dot(wqkv_t, normed, preferred_element_type=f32)
            qkv_s[...] = qkv_t.astype(bf16).astype(f32)
            g = gathered(1, i, j, l).astype(bf16)
            ga_t = jnp.dot(wp_ref[...], g, preferred_element_type=f32)
            ga_s[...] = ga_t.astype(bf16).astype(f32)
            key_row = krow_ref[w].astype(f32)
            key_col = jnp.broadcast_to(key_row, (8, CELLS)).T[:, 0:1]
            allowed = key_col == key_row

            def head_step(h, carry):
                qo = pl.multiple_of(h * HEAD, HEAD)
                q_t = qkv_s[pl.ds(qo, HEAD), :]
                k_t = qkv_s[pl.ds(qo + C, HEAD), :]
                v_t = qkv_s[pl.ds(qo + 2 * C, HEAD), :]
                ga_th = ga_s[pl.ds(qo, HEAD), :]
                q = q_t.T.astype(bf16)
                scores = jnp.dot(q, k_t.astype(bf16), preferred_element_type=f32) * SCALE
                weights = jnp.where(allowed, jnp.exp(scores), 0.0)
                probs = weights / jnp.sum(weights, axis=1, keepdims=True)
                probs_bf = probs.astype(bf16)
                att_t = lax.dot_general(v_t.astype(bf16), probs_bf, nt, preferred_element_type=f32)
                att_t = att_t.astype(bf16)
                gproj_ref[pl.ds(qo, HEAD), :] += lax.dot_general(
                    att_t, g, nt, preferred_element_type=f32
                )
                ga = ga_th.T.astype(bf16)
                grad_probs = jnp.dot(ga, v_t.astype(bf16), preferred_element_type=f32)
                dv_t = jnp.dot(ga_th.astype(bf16), probs_bf, preferred_element_type=f32)
                row_total = jnp.sum(probs * grad_probs, axis=1, keepdims=True)
                grad_scores = (probs * (grad_probs - row_total) * SCALE).astype(bf16)
                dq_t = lax.dot_general(k_t.astype(bf16), grad_scores, nt, preferred_element_type=f32)
                dk_t = jnp.dot(q_t.astype(bf16), grad_scores, preferred_element_type=f32)
                drow_s[pl.ds(qo, HEAD), :] = dq_t.astype(bf16).astype(f32)
                drow_s[pl.ds(qo + C, HEAD), :] = dk_t.astype(bf16).astype(f32)
                drow_s[pl.ds(qo + 2 * C, HEAD), :] = dv_t.astype(bf16).astype(f32)
                return carry

            lax.fori_loop(0, HEADS, head_step, 0, unroll=3)
            rows_t = drow_s[...].astype(bf16)
            gqkvT_ref[...] += lax.dot_general(normed, rows_t, nt, preferred_element_type=f32)
            grad_normed = jnp.dot(wqkv_ref[...], rows_t, preferred_element_type=f32)
            ggain_ref[...] += jnp.sum(grad_normed * x_hat, axis=1, keepdims=True)
            scaled = grad_normed * gain
            grad_shifted = inv_std * (
                scaled
                - jnp.mean(scaled, axis=0, keepdims=True)
                - x_hat * jnp.mean(scaled * x_hat, axis=0, keepdims=True)
            )
            scattered(grad_shifted.astype(bf16).astype(f32), i, j, l)

        def block_step(ij, carry):
            for l in range(2):
                window(ij, l)
            return carry

        if first:
            block_step(0, 0)
        else:
            lax.fori_loop(1, 4, block_step, 0)

    return window_kernel


def window_grads(first, arrays, krow, gain_row, wqkv, wp, partial=()):
    if first:
        extent_a, extent_b, width = WIN, WIN, arrays[0].shape[2]
    else:
        extent_a, extent_b, width = arrays[0].shape[1:]
    return pl.pallas_call(
        make_window_kernel(first),
        out_shape=[
            jax.ShapeDtypeStruct((extent_a, extent_b, width), jnp.float32),
            jax.ShapeDtypeStruct((C, 3 * C), jnp.float32),
            jax.ShapeDtypeStruct((C, C), jnp.float32),
            jax.ShapeDtypeStruct((C, 1), jnp.float32),
        ],
        scratch_shapes=[
            pltpu.VMEM((3 * C, CELLS), jnp.float32),
            pltpu.VMEM((C, CELLS), jnp.float32),
            pltpu.VMEM((3 * C, CELLS), jnp.float32),
        ],
    )(*arrays, krow, gain_row, wqkv, wp, *partial)


SUM_AXES = ("gy", "gx", "gz")


def swapped(block, axis, distance):
    return lax.ppermute(block, axis, [(i, i ^ distance) for i in range(lax.axis_size(axis))])


def summed_everywhere(matrix):
    sizes = [lax.axis_size(axis) for axis in SUM_AXES]
    if any(size & (size - 1) for size in sizes):
        return lax.psum(matrix, SUM_AXES)
    devices = 1
    for size in sizes:
        devices *= size
    unit = devices * 8 if devices * 8 <= 2 * matrix.shape[0] else devices
    padded = -(-matrix.shape[0] // unit) * unit
    values = jnp.pad(matrix, ((0, padded - matrix.shape[0]), (0, 0)))
    steps = []
    for axis, size in zip(SUM_AXES, sizes):
        distance = 1
        while distance < size:
            bit = (lax.axis_index(axis) // distance) % 2
            half = values.shape[0] // 2
            keep = lax.dynamic_slice_in_dim(values, bit * half, half)
            send = lax.dynamic_slice_in_dim(values, (1 - bit) * half, half)
            values = keep + swapped(send, axis, distance)
            steps.append((axis, distance))
            distance *= 2
    for axis, distance in reversed(steps):
        bit = (lax.axis_index(axis) // distance) % 2
        other = swapped(values, axis, distance)
        values = jnp.where(
            bit == 0, jnp.concatenate([values, other]), jnp.concatenate([other, values])
        )
    return values[: matrix.shape[0]]


def halo_route(distance_a, distance_b):
    size_a = lax.axis_size("gx")
    size_b = lax.axis_size(("gy", "gz"))
    route = []
    for ia in range(size_a):
        for ib in range(size_b):
            target = ((ia + distance_a) % size_a) * size_b + (ib + distance_b) % size_b
            route.append((ia * size_b + ib, target))
    return route


def moved(block, distance_a, distance_b):
    return lax.ppermute(block, ("gx", "gy", "gz"), halo_route(distance_a, distance_b))


def shifted_block(both):
    from_a = moved(both[:, :SHIFT, SHIFT:], -1, 0)
    from_b = moved(both[:, SHIFT:, :SHIFT], 0, -1)
    from_ab = moved(both[:, :SHIFT, :SHIFT], -1, -1)
    upper = jnp.concatenate([both[:, SHIFT:, SHIFT:], from_b], axis=2)
    lower = jnp.concatenate([from_a, from_ab], axis=2)
    return jnp.concatenate([upper, lower], axis=1)


def unshifted_sum(grads_out, grad_shifted):
    narrow = grad_shifted.astype(jnp.bfloat16)
    to_a = moved(narrow[-SHIFT:, :-SHIFT], 1, 0).astype(jnp.float32)
    to_b = moved(narrow[:-SHIFT, -SHIFT:], 0, 1).astype(jnp.float32)
    to_ab = moved(narrow[-SHIFT:, -SHIFT:], 1, 1).astype(jnp.float32)
    upper = jnp.concatenate([to_ab, to_a], axis=1)
    lower = jnp.concatenate([to_b, grad_shifted[:-SHIFT, :-SHIFT]], axis=1)
    branch = jnp.concatenate([upper, lower], axis=0)
    return (grads_out.astype(jnp.float32) + branch.astype(jnp.float32)).astype(jnp.bfloat16)


def per_device(tokens, grads_out, labels, ln_gain, qkv_weight, proj_weight):
    brick_a, brick_b = (tokens.shape[0], tokens.shape[1])
    brick_c = NZ
    channels = C
    both = shifted_block(jnp.stack([tokens, grads_out]))
    extent_a = brick_a * lax.axis_size("gx")
    extent_b = brick_b * lax.axis_size(("gy", "gz"))
    first_index = lax.axis_index("gx") * brick_a + jnp.arange(brick_a, dtype=jnp.int32)
    second_index = lax.axis_index(("gy", "gz")) * brick_b + jnp.arange(brick_b, dtype=jnp.int32)
    wrap_first = (first_index >= extent_a - SHIFT).astype(jnp.int32)
    wrap_second = (second_index >= extent_b - SHIFT).astype(jnp.int32)
    wrap_third = (jnp.arange(brick_c, dtype=jnp.int32) >= brick_c - SHIFT).astype(jnp.int32)
    region = (
        wrap_first[:, None, None] * 4 + wrap_second[None, :, None] * 2 + wrap_third[None, None, :]
    )
    mask_key = to_windows_key(labels * 8 + region)

    constants = (
        mask_key[:, None, :],
        ln_gain.reshape(1, channels),
        qkv_weight,
        proj_weight,
    )
    partial = window_grads(True, (tokens, grads_out), *constants)
    grad_branch, qkv_part, proj_grad, gain_grad = window_grads(
        False, (both,), *constants, partial=partial
    )
    width = 4 * channels
    gain_row = jnp.pad(gain_grad.reshape(1, channels), ((0, 0), (0, width - channels)))
    summed = summed_everywhere(
        jnp.concatenate([jnp.concatenate([qkv_part, proj_grad], axis=1), gain_row], axis=0)
    )
    qkv_grad = summed[:channels, : 3 * channels]
    proj_grad = summed[:channels, 3 * channels :]
    gain_grad = summed[channels, :channels]
    grad_tokens = unshifted_sum(grads_out, grad_branch)
    return (grad_tokens, gain_grad.reshape(-1), qkv_grad.reshape(-1), proj_grad.reshape(-1))


def solution(mesh):
    return jax.shard_map(
        per_device,
        mesh=mesh,
        in_specs=(
            P("gx", ("gy", "gz"), None),
            P("gx", ("gy", "gz"), None),
            P("gx", ("gy", "gz"), None),
            P(),
            P(),
            P(),
        ),
        out_specs=(P("gx", ("gy", "gz"), None), P(), P(), P()),
        check_vma=False,
    )
```

```python
import jax
import jax.numpy as jnp
from jax import lax
from jax.experimental import pallas as pl
from jax.experimental.pallas import tpu as pltpu
from jax.sharding import PartitionSpec as P

HEADS = 6
C = 192
WIN = 8
SHIFT = 4
NZ = 16
CELLS = WIN**3
HEAD = C // HEADS
SCALE = HEAD ** (-0.5)
EXP2_SCALE = SCALE * 1.4426950408889634


def passed_along(block, axis, distance):
    devices = range(lax.axis_size(axis))
    route = [((i - distance) % len(devices), i) for i in devices]
    return lax.ppermute(block, axis, route)


def to_windows_cm(values):
    extent_a, extent_b, extent_c, ch = values.shape
    shaped = values.reshape(extent_a // WIN, WIN, extent_b // WIN, WIN, extent_c // WIN, WIN, ch)
    return shaped.transpose(0, 2, 4, 6, 1, 3, 5).reshape(-1, ch, CELLS)


def from_windows_cm(values, extent_a, extent_b, extent_c):
    ch = values.shape[1]
    shaped = values.reshape(extent_a // WIN, extent_b // WIN, extent_c // WIN, ch, WIN, WIN, WIN)
    return shaped.transpose(0, 4, 1, 5, 2, 6, 3).reshape(extent_a, extent_b, extent_c, ch)


def to_windows_key(values):
    extent_a, extent_b, extent_c = values.shape
    shaped = values.reshape(extent_a // WIN, WIN, extent_b // WIN, WIN, extent_c // WIN, WIN)
    return shaped.transpose(0, 2, 4, 5, 1, 3).reshape(-1, CELLS)


def make_window_kernel(first):
    def window_kernel(*refs):
        if first:
            (tok_ref, grd_ref, krow_ref, gain_ref, wqkv_ref, wp_ref,
             gs_ref, gqkvT_ref, gproj_ref, ggain_ref, qkv_s, ga_s, drow_s) = refs
        else:
            (both_ref, krow_ref, gain_ref, wqkv_ref, wp_ref,
             gs0_ref, gqkvT0_ref, gproj0_ref, ggain0_ref,
             gs_ref, gqkvT_ref, gproj_ref, ggain_ref, qkv_s, ga_s, drow_s) = refs
        f32 = jnp.float32
        bf16 = jnp.bfloat16
        if first:
            gqkvT_ref[...] = jnp.zeros_like(gqkvT_ref)
            gproj_ref[...] = jnp.zeros_like(gproj_ref)
            ggain_ref[...] = jnp.zeros_like(ggain_ref)
        else:
            gqkvT_ref[...] = gqkvT0_ref[...]
            gproj_ref[...] = gproj0_ref[...]
            ggain_ref[...] = ggain0_ref[...]
            gs_ref[pl.ds(0, WIN), pl.ds(0, WIN), :] = gs0_ref[...]
        gain = jnp.broadcast_to(gain_ref[...], (8, C)).T[:, 0:1]
        wqkv_t = wqkv_ref[...].astype(f32).T.astype(bf16)
        nt = (((1,), (1,)), ((), ()))
        pair = 2 * C
        n_pairs = NZ // 2

        def gathered(which, i, j, l):
            pieces = []
            for q in range(WIN // 2):
                p = (WIN // 2 * l + SHIFT // 2 + q) % n_pairs
                if first:
                    source = (tok_ref, grd_ref)[which]
                    block = source[pl.ds(SHIFT, WIN), :, pl.ds(p * pair, pair)].astype(f32)
                    block = block[:, SHIFT:SHIFT + WIN]
                else:
                    block = both_ref[which, pl.ds(i * WIN, WIN), :, pl.ds(p * pair, pair)]
                    block = block.astype(f32)
                    block = jnp.where(j == 0, block[:, :WIN], block[:, WIN:])
                block = block.reshape(WIN * WIN, pair)
                pieces.append(block[:, :C])
                pieces.append(block[:, C:])
            return jnp.concatenate(pieces, axis=0).T

        def scattered(values_t, i, j, l):
            rows = values_t.T
            for q in range(WIN // 2):
                p = (WIN // 2 * l + SHIFT // 2 + q) % n_pairs
                even = rows[2 * q * WIN * WIN:(2 * q + 1) * WIN * WIN]
                odd = rows[(2 * q + 1) * WIN * WIN:(2 * q + 2) * WIN * WIN]
                block = jnp.concatenate([even, odd], axis=1).reshape(WIN, WIN, pair)
                if first:
                    gs_ref[:, :, pl.ds(p * pair, pair)] = block
                else:
                    gs_ref[
                        pl.ds(i * WIN, WIN),
                        pl.ds(pl.multiple_of(j * WIN, WIN), WIN),
                        pl.ds(p * pair, pair),
                    ] = block

        def window(ij, l):
            i = ij // 2
            j = ij % 2
            w = ij * 2 + l
            x = gathered(0, i, j, l)
            row_mean = jnp.mean(x, axis=0, keepdims=True)
            centred = x - row_mean
            inv_std = lax.rsqrt(jnp.mean(centred * centred, axis=0, keepdims=True) + 1e-05)
            x_hat = centred * inv_std
            normed = (x_hat * gain).astype(bf16)
            qkv_t = jnp.dot(wqkv_t, normed, preferred_element_type=f32)
            qkv_s[...] = qkv_t.astype(bf16).astype(f32)
            g = gathered(1, i, j, l).astype(bf16)
            ga_t = jnp.dot(wp_ref[...], g, preferred_element_type=f32)
            ga_s[...] = ga_t.astype(bf16).astype(f32)
            key_row = krow_ref[w].astype(f32)
            key_col = jnp.broadcast_to(key_row, (8, CELLS)).T[:, 0:1]
            allowed = key_col == key_row

            def head_step(h, carry):
                qo = pl.multiple_of(h * HEAD, HEAD)
                q_t = qkv_s[pl.ds(qo, HEAD), :]
                k_t = qkv_s[pl.ds(qo + C, HEAD), :]
                v_t = qkv_s[pl.ds(qo + 2 * C, HEAD), :]
                ga_th = ga_s[pl.ds(qo, HEAD), :]
                q = q_t.T.astype(bf16)
                scores = jnp.dot(q, k_t.astype(bf16), preferred_element_type=f32)
                weights = jnp.where(allowed, jnp.exp2(scores * EXP2_SCALE), 0.0)
                probs = weights / jnp.sum(weights, axis=1, keepdims=True)
                probs_bf = probs.astype(bf16)
                att_t = lax.dot_general(v_t.astype(bf16), probs_bf, nt, preferred_element_type=f32)
                att_t = att_t.astype(bf16)
                gproj_ref[pl.ds(qo, HEAD), :] += lax.dot_general(
                    att_t, g, nt, preferred_element_type=f32
                )
                ga = ga_th.T.astype(bf16)
                grad_probs = jnp.dot(ga, v_t.astype(bf16), preferred_element_type=f32)
                dv_t = jnp.dot(ga_th.astype(bf16), probs_bf, preferred_element_type=f32)
                row_total = jnp.sum(probs * grad_probs, axis=1, keepdims=True)
                grad_scores = (probs * (grad_probs - row_total) * SCALE).astype(bf16)
                dq_t = lax.dot_general(k_t.astype(bf16), grad_scores, nt, preferred_element_type=f32)
                dk_t = jnp.dot(q_t.astype(bf16), grad_scores, preferred_element_type=f32)
                drow_s[pl.ds(qo, HEAD), :] = dq_t.astype(bf16).astype(f32)
                drow_s[pl.ds(qo + C, HEAD), :] = dk_t.astype(bf16).astype(f32)
                drow_s[pl.ds(qo + 2 * C, HEAD), :] = dv_t.astype(bf16).astype(f32)
                return carry

            lax.fori_loop(0, HEADS, head_step, 0, unroll=3)
            rows_t = drow_s[...].astype(bf16)
            gqkvT_ref[...] += lax.dot_general(normed, rows_t, nt, preferred_element_type=f32)
            grad_normed = jnp.dot(wqkv_ref[...], rows_t, preferred_element_type=f32)
            ggain_ref[...] += jnp.sum(grad_normed * x_hat, axis=1, keepdims=True)
            scaled = grad_normed * gain
            grad_shifted = inv_std * (
                scaled
                - jnp.mean(scaled, axis=0, keepdims=True)
                - x_hat * jnp.mean(scaled * x_hat, axis=0, keepdims=True)
            )
            scattered(grad_shifted.astype(bf16).astype(f32), i, j, l)

        def block_step(ij, carry):
            for l in range(2):
                window(ij, l)
            return carry

        if first:
            block_step(0, 0)
        else:
            lax.fori_loop(1, 4, block_step, 0)

    return window_kernel


def window_grads(first, arrays, krow, gain_row, wqkv, wp, partial=()):
    if first:
        extent_a, extent_b, width = WIN, WIN, arrays[0].shape[2]
    else:
        extent_a, extent_b, width = arrays[0].shape[1:]
    return pl.pallas_call(
        make_window_kernel(first),
        out_shape=[
            jax.ShapeDtypeStruct((extent_a, extent_b, width), jnp.float32),
            jax.ShapeDtypeStruct((C, 3 * C), jnp.float32),
            jax.ShapeDtypeStruct((C, C), jnp.float32),
            jax.ShapeDtypeStruct((C, 1), jnp.float32),
        ],
        scratch_shapes=[
            pltpu.VMEM((3 * C, CELLS), jnp.float32),
            pltpu.VMEM((C, CELLS), jnp.float32),
            pltpu.VMEM((3 * C, CELLS), jnp.float32),
        ],
    )(*arrays, krow, gain_row, wqkv, wp, *partial)


SUM_AXES = ("gy", "gx", "gz")


def swapped(block, axis, distance):
    return lax.ppermute(block, axis, [(i, i ^ distance) for i in range(lax.axis_size(axis))])


def summed_everywhere(matrix):
    sizes = [lax.axis_size(axis) for axis in SUM_AXES]
    if any(size & (size - 1) for size in sizes):
        return lax.psum(matrix, SUM_AXES)
    devices = 1
    for size in sizes:
        devices *= size
    unit = devices * 8 if devices * 8 <= 2 * matrix.shape[0] else devices
    padded = -(-matrix.shape[0] // unit) * unit
    values = jnp.pad(matrix, ((0, padded - matrix.shape[0]), (0, 0)))
    steps = []
    for axis, size in zip(SUM_AXES, sizes):
        distance = 1
        while distance < size:
            bit = (lax.axis_index(axis) // distance) % 2
            half = values.shape[0] // 2
            keep = lax.dynamic_slice_in_dim(values, bit * half, half)
            send = lax.dynamic_slice_in_dim(values, (1 - bit) * half, half)
            values = keep + swapped(send, axis, distance)
            steps.append((axis, distance))
            distance *= 2
    for axis, distance in reversed(steps):
        bit = (lax.axis_index(axis) // distance) % 2
        other = swapped(values, axis, distance)
        values = jnp.where(
            bit == 0, jnp.concatenate([values, other]), jnp.concatenate([other, values])
        )
    return values[: matrix.shape[0]]


def halo_route(distance_a, distance_b):
    size_a = lax.axis_size("gx")
    size_b = lax.axis_size(("gy", "gz"))
    route = []
    for ia in range(size_a):
        for ib in range(size_b):
            target = ((ia + distance_a) % size_a) * size_b + (ib + distance_b) % size_b
            route.append((ia * size_b + ib, target))
    return route


def moved(block, distance_a, distance_b):
    return lax.ppermute(block, ("gx", "gy", "gz"), halo_route(distance_a, distance_b))


def shifted_block(both):
    from_a = moved(both[:, :SHIFT, SHIFT:], -1, 0)
    from_b = moved(both[:, SHIFT:, :SHIFT], 0, -1)
    from_ab = moved(both[:, :SHIFT, :SHIFT], -1, -1)
    upper = jnp.concatenate([both[:, SHIFT:, SHIFT:], from_b], axis=2)
    lower = jnp.concatenate([from_a, from_ab], axis=2)
    return jnp.concatenate([upper, lower], axis=1)


def unshifted_sum(grads_out, grad_shifted):
    narrow = grad_shifted.astype(jnp.bfloat16)
    to_a = moved(narrow[-SHIFT:, :-SHIFT], 1, 0).astype(jnp.float32)
    to_b = moved(narrow[:-SHIFT, -SHIFT:], 0, 1).astype(jnp.float32)
    to_ab = moved(narrow[-SHIFT:, -SHIFT:], 1, 1).astype(jnp.float32)
    upper = jnp.concatenate([to_ab, to_a], axis=1)
    lower = jnp.concatenate([to_b, grad_shifted[:-SHIFT, :-SHIFT]], axis=1)
    branch = jnp.concatenate([upper, lower], axis=0)
    return (grads_out.astype(jnp.float32) + branch.astype(jnp.float32)).astype(jnp.bfloat16)


def per_device(tokens, grads_out, labels, ln_gain, qkv_weight, proj_weight):
    brick_a, brick_b = (tokens.shape[0], tokens.shape[1])
    brick_c = NZ
    channels = C
    both = shifted_block(jnp.stack([tokens, grads_out]))
    extent_a = brick_a * lax.axis_size("gx")
    extent_b = brick_b * lax.axis_size(("gy", "gz"))
    first_index = lax.axis_index("gx") * brick_a + jnp.arange(brick_a, dtype=jnp.int32)
    second_index = lax.axis_index(("gy", "gz")) * brick_b + jnp.arange(brick_b, dtype=jnp.int32)
    wrap_first = (first_index >= extent_a - SHIFT).astype(jnp.int32)
    wrap_second = (second_index >= extent_b - SHIFT).astype(jnp.int32)
    wrap_third = (jnp.arange(brick_c, dtype=jnp.int32) >= brick_c - SHIFT).astype(jnp.int32)
    region = (
        wrap_first[:, None, None] * 4 + wrap_second[None, :, None] * 2 + wrap_third[None, None, :]
    )
    mask_key = to_windows_key(labels * 8 + region)

    constants = (
        mask_key[:, None, :],
        ln_gain.reshape(1, channels),
        qkv_weight,
        proj_weight,
    )
    partial = window_grads(True, (tokens, grads_out), *constants)
    grad_branch, qkv_part, proj_grad, gain_grad = window_grads(
        False, (both,), *constants, partial=partial
    )
    width = 4 * channels
    gain_row = jnp.pad(gain_grad.reshape(1, channels), ((0, 0), (0, width - channels)))
    summed = summed_everywhere(
        jnp.concatenate([jnp.concatenate([qkv_part, proj_grad], axis=1), gain_row], axis=0)
    )
    qkv_grad = summed[:channels, : 3 * channels]
    proj_grad = summed[:channels, 3 * channels :]
    gain_grad = summed[channels, :channels]
    grad_tokens = unshifted_sum(grads_out, grad_branch)
    return (grad_tokens, gain_grad.reshape(-1), qkv_grad.reshape(-1), proj_grad.reshape(-1))


def solution(mesh):
    return jax.shard_map(
        per_device,
        mesh=mesh,
        in_specs=(
            P("gx", ("gy", "gz"), None),
            P("gx", ("gy", "gz"), None),
            P("gx", ("gy", "gz"), None),
            P(),
            P(),
            P(),
        ),
        out_specs=(P("gx", ("gy", "gz"), None), P(), P(), P()),
        check_vma=False,
    )
```

```python
import jax
import jax.numpy as jnp
from jax import lax
from jax.experimental import pallas as pl
from jax.experimental.pallas import tpu as pltpu
from jax.sharding import PartitionSpec as P

HEADS = 6
C = 192
WIN = 8
SHIFT = 4
NZ = 16
CELLS = WIN**3
HEAD = C // HEADS
SCALE = HEAD ** (-0.5)
EXP2_SCALE = SCALE * 1.4426950408889634


def passed_along(block, axis, distance):
    devices = range(lax.axis_size(axis))
    route = [((i - distance) % len(devices), i) for i in devices]
    return lax.ppermute(block, axis, route)


def to_windows_cm(values):
    extent_a, extent_b, extent_c, ch = values.shape
    shaped = values.reshape(extent_a // WIN, WIN, extent_b // WIN, WIN, extent_c // WIN, WIN, ch)
    return shaped.transpose(0, 2, 4, 6, 1, 3, 5).reshape(-1, ch, CELLS)


def from_windows_cm(values, extent_a, extent_b, extent_c):
    ch = values.shape[1]
    shaped = values.reshape(extent_a // WIN, extent_b // WIN, extent_c // WIN, ch, WIN, WIN, WIN)
    return shaped.transpose(0, 4, 1, 5, 2, 6, 3).reshape(extent_a, extent_b, extent_c, ch)


def to_windows_key(values):
    extent_a, extent_b, extent_c = values.shape
    shaped = values.reshape(extent_a // WIN, WIN, extent_b // WIN, WIN, extent_c // WIN, WIN)
    return shaped.transpose(0, 2, 4, 5, 1, 3).reshape(-1, CELLS)


def make_window_kernel(first):
    def window_kernel(*refs):
        if first:
            (tok_ref, grd_ref, krow_ref, gain_ref, wqkv_ref, wp_ref,
             gs_ref, gqkvT_ref, gproj_ref, ggain_ref, qkv_s, ga_s, drow_s) = refs
        else:
            (both_ref, krow_ref, gain_ref, wqkv_ref, wp_ref,
             gs0_ref, gqkvT0_ref, gproj0_ref, ggain0_ref,
             gs_ref, gqkvT_ref, gproj_ref, ggain_ref, qkv_s, ga_s, drow_s) = refs
        f32 = jnp.float32
        bf16 = jnp.bfloat16
        if first:
            gqkvT_ref[...] = jnp.zeros_like(gqkvT_ref)
            gproj_ref[...] = jnp.zeros_like(gproj_ref)
            ggain_ref[...] = jnp.zeros_like(ggain_ref)
        else:
            gqkvT_ref[...] = gqkvT0_ref[...]
            gproj_ref[...] = gproj0_ref[...]
            ggain_ref[...] = ggain0_ref[...]
            gs_ref[pl.ds(0, WIN), pl.ds(0, WIN), :] = gs0_ref[...]
        gain = jnp.broadcast_to(gain_ref[...], (8, C)).T[:, 0:1]
        wqkv_t = wqkv_ref[...].astype(f32).T.astype(bf16)
        nt = (((1,), (1,)), ((), ()))
        pair = 2 * C
        n_pairs = NZ // 2

        def gathered(which, i, j, l):
            pieces = []
            for q in range(WIN // 2):
                p = (WIN // 2 * l + SHIFT // 2 + q) % n_pairs
                if first:
                    source = (tok_ref, grd_ref)[which]
                    block = source[pl.ds(SHIFT, WIN), :, pl.ds(p * pair, pair)].astype(f32)
                    block = block[:, SHIFT:SHIFT + WIN]
                else:
                    block = both_ref[which, pl.ds(i * WIN, WIN), :, pl.ds(p * pair, pair)]
                    block = block.astype(f32)
                    block = jnp.where(j == 0, block[:, :WIN], block[:, WIN:])
                block = block.reshape(WIN * WIN, pair)
                pieces.append(block[:, :C])
                pieces.append(block[:, C:])
            return jnp.concatenate(pieces, axis=0).T

        def scattered(values_t, i, j, l):
            rows = values_t.T
            for q in range(WIN // 2):
                p = (WIN // 2 * l + SHIFT // 2 + q) % n_pairs
                even = rows[2 * q * WIN * WIN:(2 * q + 1) * WIN * WIN]
                odd = rows[(2 * q + 1) * WIN * WIN:(2 * q + 2) * WIN * WIN]
                block = jnp.concatenate([even, odd], axis=1).reshape(WIN, WIN, pair)
                if first:
                    gs_ref[:, :, pl.ds(p * pair, pair)] = block
                else:
                    gs_ref[
                        pl.ds(i * WIN, WIN),
                        pl.ds(pl.multiple_of(j * WIN, WIN), WIN),
                        pl.ds(p * pair, pair),
                    ] = block

        def window(ij, l):
            i = ij // 2
            j = ij % 2
            w = ij * 2 + l
            x = gathered(0, i, j, l)
            row_mean = jnp.mean(x, axis=0, keepdims=True)
            centred = x - row_mean
            inv_std = lax.rsqrt(jnp.mean(centred * centred, axis=0, keepdims=True) + 1e-05)
            x_hat = centred * inv_std
            normed = (x_hat * gain).astype(bf16)
            qkv_t = jnp.dot(wqkv_t, normed, preferred_element_type=f32)
            qkv_s[...] = qkv_t.astype(bf16).astype(f32)
            g = gathered(1, i, j, l).astype(bf16)
            ga_t = jnp.dot(wp_ref[...], g, preferred_element_type=f32)
            ga_s[...] = ga_t.astype(bf16).astype(f32)
            key_row = krow_ref[w].astype(f32)
            key_col = jnp.broadcast_to(key_row, (8, CELLS)).T[:, 0:1]
            allowed = key_col == key_row

            def head_step(h, carry):
                qo = pl.multiple_of(h * HEAD, HEAD)
                q_t = qkv_s[pl.ds(qo, HEAD), :]
                k_t = qkv_s[pl.ds(qo + C, HEAD), :]
                v_t = qkv_s[pl.ds(qo + 2 * C, HEAD), :]
                ga_th = ga_s[pl.ds(qo, HEAD), :]
                q = q_t.T.astype(bf16)
                scores = jnp.dot(q, k_t.astype(bf16), preferred_element_type=f32)
                weights = jnp.where(allowed, jnp.exp2(scores * EXP2_SCALE), 0.0)
                probs = weights / jnp.sum(weights, axis=1, keepdims=True)
                probs_bf = probs.astype(bf16)
                att_t = lax.dot_general(v_t.astype(bf16), probs_bf, nt, preferred_element_type=f32)
                att_t = att_t.astype(bf16)
                gproj_ref[pl.ds(qo, HEAD), :] += lax.dot_general(
                    att_t, g, nt, preferred_element_type=f32
                )
                ga = ga_th.T.astype(bf16)
                grad_probs = jnp.dot(ga, v_t.astype(bf16), preferred_element_type=f32)
                dv_t = jnp.dot(ga_th.astype(bf16), probs_bf, preferred_element_type=f32)
                row_total = jnp.sum(probs * grad_probs, axis=1, keepdims=True)
                grad_scores = (probs * (grad_probs - row_total) * SCALE).astype(bf16)
                dq_t = lax.dot_general(k_t.astype(bf16), grad_scores, nt, preferred_element_type=f32)
                dk_t = jnp.dot(q_t.astype(bf16), grad_scores, preferred_element_type=f32)
                drow_s[pl.ds(qo, HEAD), :] = dq_t.astype(bf16).astype(f32)
                drow_s[pl.ds(qo + C, HEAD), :] = dk_t.astype(bf16).astype(f32)
                drow_s[pl.ds(qo + 2 * C, HEAD), :] = dv_t.astype(bf16).astype(f32)
                return carry

            lax.fori_loop(0, HEADS, head_step, 0, unroll=3)
            rows_t = drow_s[...].astype(bf16)
            gqkvT_ref[...] += lax.dot_general(normed, rows_t, nt, preferred_element_type=f32)
            grad_normed = jnp.dot(wqkv_ref[...], rows_t, preferred_element_type=f32)
            ggain_ref[...] += jnp.sum(grad_normed * x_hat, axis=1, keepdims=True)
            scaled = grad_normed * gain
            grad_shifted = inv_std * (
                scaled
                - jnp.mean(scaled, axis=0, keepdims=True)
                - x_hat * jnp.mean(scaled * x_hat, axis=0, keepdims=True)
            )
            scattered(grad_shifted.astype(bf16).astype(f32), i, j, l)

        def block_step(ij, carry):
            for l in range(2):
                window(ij, l)
            return carry

        if first:
            block_step(0, 0)
        else:
            lax.fori_loop(1, 4, block_step, 0)

    return window_kernel


def window_grads(first, arrays, krow, gain_row, wqkv, wp, partial=()):
    if first:
        extent_a, extent_b, width = WIN, WIN, arrays[0].shape[2]
    else:
        extent_a, extent_b, width = arrays[0].shape[1:]
    return pl.pallas_call(
        make_window_kernel(first),
        out_shape=[
            jax.ShapeDtypeStruct((extent_a, extent_b, width), jnp.float32),
            jax.ShapeDtypeStruct((C, 3 * C), jnp.float32),
            jax.ShapeDtypeStruct((C, C), jnp.float32),
            jax.ShapeDtypeStruct((C, 1), jnp.float32),
        ],
        scratch_shapes=[
            pltpu.VMEM((3 * C, CELLS), jnp.float32),
            pltpu.VMEM((C, CELLS), jnp.float32),
            pltpu.VMEM((3 * C, CELLS), jnp.float32),
        ],
    )(*arrays, krow, gain_row, wqkv, wp, *partial)


SUM_AXES = ("gy", "gx", "gz")


def swapped(block, axis, distance):
    return lax.ppermute(block, axis, [(i, i ^ distance) for i in range(lax.axis_size(axis))])


def summed_everywhere(matrix):
    sizes = [lax.axis_size(axis) for axis in SUM_AXES]
    if any(size & (size - 1) for size in sizes):
        return lax.psum(matrix, SUM_AXES)
    devices = 1
    for size in sizes:
        devices *= size
    unit = devices * 8 if devices * 8 <= 2 * matrix.shape[0] else devices
    padded = -(-matrix.shape[0] // unit) * unit
    values = jnp.pad(matrix, ((0, padded - matrix.shape[0]), (0, 0)))
    steps = []
    for axis, size in zip(SUM_AXES, sizes):
        distance = 1
        while distance < size:
            bit = (lax.axis_index(axis) // distance) % 2
            half = values.shape[0] // 2
            keep = lax.dynamic_slice_in_dim(values, bit * half, half)
            send = lax.dynamic_slice_in_dim(values, (1 - bit) * half, half)
            values = keep + swapped(send, axis, distance)
            steps.append((axis, distance))
            distance *= 2
    for axis, distance in reversed(steps):
        bit = (lax.axis_index(axis) // distance) % 2
        other = swapped(values, axis, distance)
        half = values.shape[0]
        joined = jnp.zeros((2 * half,) + values.shape[1:], values.dtype)
        joined = lax.dynamic_update_slice_in_dim(joined, values, bit * half, 0)
        values = lax.dynamic_update_slice_in_dim(joined, other, (1 - bit) * half, 0)
    return values[: matrix.shape[0]]


def halo_route(distance_a, distance_b):
    size_a = lax.axis_size("gx")
    size_b = lax.axis_size(("gy", "gz"))
    route = []
    for ia in range(size_a):
        for ib in range(size_b):
            target = ((ia + distance_a) % size_a) * size_b + (ib + distance_b) % size_b
            route.append((ia * size_b + ib, target))
    return route


def moved(block, distance_a, distance_b):
    return lax.ppermute(block, ("gx", "gy", "gz"), halo_route(distance_a, distance_b))


def shifted_block(both):
    from_a = moved(both[:, :SHIFT, SHIFT:], -1, 0)
    from_b = moved(both[:, SHIFT:, :SHIFT], 0, -1)
    from_ab = moved(both[:, :SHIFT, :SHIFT], -1, -1)
    upper = jnp.concatenate([both[:, SHIFT:, SHIFT:], from_b], axis=2)
    lower = jnp.concatenate([from_a, from_ab], axis=2)
    return jnp.concatenate([upper, lower], axis=1)


def unshifted_sum(grads_out, grad_shifted):
    narrow = grad_shifted.astype(jnp.bfloat16)
    to_a = moved(narrow[-SHIFT:, :-SHIFT], 1, 0).astype(jnp.float32)
    to_b = moved(narrow[:-SHIFT, -SHIFT:], 0, 1).astype(jnp.float32)
    to_ab = moved(narrow[-SHIFT:, -SHIFT:], 1, 1).astype(jnp.float32)
    upper = jnp.concatenate([to_ab, to_a], axis=1)
    lower = jnp.concatenate([to_b, grad_shifted[:-SHIFT, :-SHIFT]], axis=1)
    branch = jnp.concatenate([upper, lower], axis=0)
    return (grads_out.astype(jnp.float32) + branch.astype(jnp.float32)).astype(jnp.bfloat16)


def per_device(tokens, grads_out, labels, ln_gain, qkv_weight, proj_weight):
    brick_a, brick_b = (tokens.shape[0], tokens.shape[1])
    brick_c = NZ
    channels = C
    both = shifted_block(jnp.stack([tokens, grads_out]))
    extent_a = brick_a * lax.axis_size("gx")
    extent_b = brick_b * lax.axis_size(("gy", "gz"))
    first_index = lax.axis_index("gx") * brick_a + jnp.arange(brick_a, dtype=jnp.int32)
    second_index = lax.axis_index(("gy", "gz")) * brick_b + jnp.arange(brick_b, dtype=jnp.int32)
    wrap_first = (first_index >= extent_a - SHIFT).astype(jnp.int32)
    wrap_second = (second_index >= extent_b - SHIFT).astype(jnp.int32)
    wrap_third = (jnp.arange(brick_c, dtype=jnp.int32) >= brick_c - SHIFT).astype(jnp.int32)
    region = (
        wrap_first[:, None, None] * 4 + wrap_second[None, :, None] * 2 + wrap_third[None, None, :]
    )
    mask_key = to_windows_key(labels * 8 + region)

    constants = (
        mask_key[:, None, :],
        ln_gain.reshape(1, channels),
        qkv_weight,
        proj_weight,
    )
    partial = window_grads(True, (tokens, grads_out), *constants)
    grad_branch, qkv_part, proj_grad, gain_grad = window_grads(
        False, (both,), *constants, partial=partial
    )
    width = 4 * channels
    gain_row = jnp.pad(gain_grad.reshape(1, channels), ((0, 0), (0, width - channels)))
    summed = summed_everywhere(
        jnp.concatenate([jnp.concatenate([qkv_part, proj_grad], axis=1), gain_row], axis=0)
    )
    qkv_grad = summed[:channels, : 3 * channels]
    proj_grad = summed[:channels, 3 * channels :]
    gain_grad = summed[channels, :channels]
    grad_tokens = unshifted_sum(grads_out, grad_branch)
    return (grad_tokens, gain_grad.reshape(-1), qkv_grad.reshape(-1), proj_grad.reshape(-1))


def solution(mesh):
    return jax.shard_map(
        per_device,
        mesh=mesh,
        in_specs=(
            P("gx", ("gy", "gz"), None),
            P("gx", ("gy", "gz"), None),
            P("gx", ("gy", "gz"), None),
            P(),
            P(),
            P(),
        ),
        out_specs=(P("gx", ("gy", "gz"), None), P(), P(), P()),
        check_vma=False,
    )
```

```python
import jax
import jax.numpy as jnp
from jax import lax
from jax.experimental import pallas as pl
from jax.experimental.pallas import tpu as pltpu
from jax.sharding import PartitionSpec as P

HEADS = 6
C = 192
WIN = 8
SHIFT = 4
NZ = 16
CELLS = WIN**3
HEAD = C // HEADS
SCALE = HEAD ** (-0.5)
EXP2_SCALE = SCALE * 1.4426950408889634


def passed_along(block, axis, distance):
    devices = range(lax.axis_size(axis))
    route = [((i - distance) % len(devices), i) for i in devices]
    return lax.ppermute(block, axis, route)


def to_windows_cm(values):
    extent_a, extent_b, extent_c, ch = values.shape
    shaped = values.reshape(extent_a // WIN, WIN, extent_b // WIN, WIN, extent_c // WIN, WIN, ch)
    return shaped.transpose(0, 2, 4, 6, 1, 3, 5).reshape(-1, ch, CELLS)


def from_windows_cm(values, extent_a, extent_b, extent_c):
    ch = values.shape[1]
    shaped = values.reshape(extent_a // WIN, extent_b // WIN, extent_c // WIN, ch, WIN, WIN, WIN)
    return shaped.transpose(0, 4, 1, 5, 2, 6, 3).reshape(extent_a, extent_b, extent_c, ch)


def to_windows_key(values):
    extent_a, extent_b, extent_c = values.shape
    shaped = values.reshape(extent_a // WIN, WIN, extent_b // WIN, WIN, extent_c // WIN, WIN)
    return shaped.transpose(0, 2, 4, 5, 1, 3).reshape(-1, CELLS)


def make_window_kernel(first):
    def window_kernel(*refs):
        if first:
            (tok_ref, grd_ref, krow_ref, gain_ref, wqkv_ref, wp_ref,
             gs_ref, gqkvT_ref, gproj_ref, ggain_ref, qkv_s, ga_s, drow_s, bias_s) = refs
        else:
            (both_ref, krow_ref, gain_ref, wqkv_ref, wp_ref,
             gs0_ref, gqkvT0_ref, gproj0_ref, ggain0_ref,
             gs_ref, gqkvT_ref, gproj_ref, ggain_ref, qkv_s, ga_s, drow_s, bias_s) = refs
        f32 = jnp.float32
        bf16 = jnp.bfloat16
        if first:
            gqkvT_ref[...] = jnp.zeros_like(gqkvT_ref)
            gproj_ref[...] = jnp.zeros_like(gproj_ref)
            ggain_ref[...] = jnp.zeros_like(ggain_ref)
        else:
            gqkvT_ref[...] = gqkvT0_ref[...]
            gproj_ref[...] = gproj0_ref[...]
            ggain_ref[...] = ggain0_ref[...]
            gs_ref[pl.ds(0, WIN), pl.ds(0, WIN), :] = gs0_ref[...]
        gain = jnp.broadcast_to(gain_ref[...], (8, C)).T[:, 0:1]
        wqkv_t = wqkv_ref[...].astype(f32).T.astype(bf16)
        nt = (((1,), (1,)), ((), ()))
        pair = 2 * C
        n_pairs = NZ // 2

        def gathered(which, i, j, l):
            pieces = []
            for q in range(WIN // 2):
                p = (WIN // 2 * l + SHIFT // 2 + q) % n_pairs
                if first:
                    source = (tok_ref, grd_ref)[which]
                    block = source[pl.ds(SHIFT, WIN), :, pl.ds(p * pair, pair)].astype(f32)
                    block = block[:, SHIFT:SHIFT + WIN]
                else:
                    block = both_ref[which, pl.ds(i * WIN, WIN), :, pl.ds(p * pair, pair)]
                    block = block.astype(f32)
                    block = jnp.where(j == 0, block[:, :WIN], block[:, WIN:])
                block = block.reshape(WIN * WIN, pair)
                pieces.append(block[:, :C])
                pieces.append(block[:, C:])
            return jnp.concatenate(pieces, axis=0).T

        def scattered(values_t, i, j, l):
            rows = values_t.T
            for q in range(WIN // 2):
                p = (WIN // 2 * l + SHIFT // 2 + q) % n_pairs
                even = rows[2 * q * WIN * WIN:(2 * q + 1) * WIN * WIN]
                odd = rows[(2 * q + 1) * WIN * WIN:(2 * q + 2) * WIN * WIN]
                block = jnp.concatenate([even, odd], axis=1).reshape(WIN, WIN, pair)
                if first:
                    gs_ref[:, :, pl.ds(p * pair, pair)] = block
                else:
                    gs_ref[
                        pl.ds(i * WIN, WIN),
                        pl.ds(pl.multiple_of(j * WIN, WIN), WIN),
                        pl.ds(p * pair, pair),
                    ] = block

        def window(ij, l):
            i = ij // 2
            j = ij % 2
            w = ij * 2 + l
            x = gathered(0, i, j, l)
            row_mean = jnp.mean(x, axis=0, keepdims=True)
            centred = x - row_mean
            inv_std = lax.rsqrt(jnp.mean(centred * centred, axis=0, keepdims=True) + 1e-05)
            x_hat = centred * inv_std
            normed = (x_hat * gain).astype(bf16)
            qkv_t = jnp.dot(wqkv_t, normed, preferred_element_type=f32)
            qkv_s[...] = qkv_t.astype(bf16).astype(f32)
            g = gathered(1, i, j, l).astype(bf16)
            ga_t = jnp.dot(wp_ref[...], g, preferred_element_type=f32)
            ga_s[...] = ga_t.astype(bf16).astype(f32)
            key_row = krow_ref[w].astype(f32)
            key_col = jnp.broadcast_to(key_row, (8, CELLS)).T[:, 0:1]
            bias_s[...] = jnp.where(key_col == key_row, 0.0, -jnp.inf)

            def head_step(h, carry):
                qo = pl.multiple_of(h * HEAD, HEAD)
                q_t = qkv_s[pl.ds(qo, HEAD), :]
                k_t = qkv_s[pl.ds(qo + C, HEAD), :]
                v_t = qkv_s[pl.ds(qo + 2 * C, HEAD), :]
                ga_th = ga_s[pl.ds(qo, HEAD), :]
                q = q_t.T.astype(bf16)
                scores = jnp.dot(q, k_t.astype(bf16), preferred_element_type=f32)
                weights = jnp.exp2(scores * EXP2_SCALE + bias_s[...])
                probs = weights / jnp.sum(weights, axis=1, keepdims=True)
                probs_bf = probs.astype(bf16)
                att_t = lax.dot_general(v_t.astype(bf16), probs_bf, nt, preferred_element_type=f32)
                att_t = att_t.astype(bf16)
                gproj_ref[pl.ds(qo, HEAD), :] += lax.dot_general(
                    att_t, g, nt, preferred_element_type=f32
                )
                ga = ga_th.T.astype(bf16)
                grad_probs = jnp.dot(ga, v_t.astype(bf16), preferred_element_type=f32)
                dv_t = jnp.dot(ga_th.astype(bf16), probs_bf, preferred_element_type=f32)
                row_total = jnp.sum(probs * grad_probs, axis=1, keepdims=True)
                grad_scores = (probs * (grad_probs - row_total) * SCALE).astype(bf16)
                dq_t = lax.dot_general(k_t.astype(bf16), grad_scores, nt, preferred_element_type=f32)
                dk_t = jnp.dot(q_t.astype(bf16), grad_scores, preferred_element_type=f32)
                drow_s[pl.ds(qo, HEAD), :] = dq_t.astype(bf16).astype(f32)
                drow_s[pl.ds(qo + C, HEAD), :] = dk_t.astype(bf16).astype(f32)
                drow_s[pl.ds(qo + 2 * C, HEAD), :] = dv_t.astype(bf16).astype(f32)
                return carry

            lax.fori_loop(0, HEADS, head_step, 0, unroll=3)
            rows_t = drow_s[...].astype(bf16)
            gqkvT_ref[...] += lax.dot_general(normed, rows_t, nt, preferred_element_type=f32)
            grad_normed = jnp.dot(wqkv_ref[...], rows_t, preferred_element_type=f32)
            ggain_ref[...] += jnp.sum(grad_normed * x_hat, axis=1, keepdims=True)
            scaled = grad_normed * gain
            grad_shifted = inv_std * (
                scaled
                - jnp.mean(scaled, axis=0, keepdims=True)
                - x_hat * jnp.mean(scaled * x_hat, axis=0, keepdims=True)
            )
            scattered(grad_shifted.astype(bf16).astype(f32), i, j, l)

        def block_step(ij, carry):
            for l in range(2):
                window(ij, l)
            return carry

        if first:
            block_step(0, 0)
        else:
            lax.fori_loop(1, 4, block_step, 0)

    return window_kernel


def window_grads(first, arrays, krow, gain_row, wqkv, wp, partial=()):
    if first:
        extent_a, extent_b, width = WIN, WIN, arrays[0].shape[2]
    else:
        extent_a, extent_b, width = arrays[0].shape[1:]
    return pl.pallas_call(
        make_window_kernel(first),
        out_shape=[
            jax.ShapeDtypeStruct((extent_a, extent_b, width), jnp.float32),
            jax.ShapeDtypeStruct((C, 3 * C), jnp.float32),
            jax.ShapeDtypeStruct((C, C), jnp.float32),
            jax.ShapeDtypeStruct((C, 1), jnp.float32),
        ],
        scratch_shapes=[
            pltpu.VMEM((3 * C, CELLS), jnp.float32),
            pltpu.VMEM((C, CELLS), jnp.float32),
            pltpu.VMEM((3 * C, CELLS), jnp.float32),
            pltpu.VMEM((CELLS, CELLS), jnp.float32),
        ],
    )(*arrays, krow, gain_row, wqkv, wp, *partial)


SUM_AXES = ("gy", "gx", "gz")


def swapped(block, axis, distance):
    return lax.ppermute(block, axis, [(i, i ^ distance) for i in range(lax.axis_size(axis))])


def summed_everywhere(matrix):
    sizes = [lax.axis_size(axis) for axis in SUM_AXES]
    if any(size & (size - 1) for size in sizes):
        return lax.psum(matrix, SUM_AXES)
    devices = 1
    for size in sizes:
        devices *= size
    unit = devices * 8 if devices * 8 <= 2 * matrix.shape[0] else devices
    padded = -(-matrix.shape[0] // unit) * unit
    values = jnp.pad(matrix, ((0, padded - matrix.shape[0]), (0, 0)))
    steps = []
    for axis, size in zip(SUM_AXES, sizes):
        distance = 1
        while distance < size:
            bit = (lax.axis_index(axis) // distance) % 2
            half = values.shape[0] // 2
            keep = lax.dynamic_slice_in_dim(values, bit * half, half)
            send = lax.dynamic_slice_in_dim(values, (1 - bit) * half, half)
            values = keep + swapped(send, axis, distance)
            steps.append((axis, distance))
            distance *= 2
    for axis, distance in reversed(steps):
        bit = (lax.axis_index(axis) // distance) % 2
        other = swapped(values, axis, distance)
        half = values.shape[0]
        joined = jnp.zeros((2 * half,) + values.shape[1:], values.dtype)
        joined = lax.dynamic_update_slice_in_dim(joined, values, bit * half, 0)
        values = lax.dynamic_update_slice_in_dim(joined, other, (1 - bit) * half, 0)
    return values[: matrix.shape[0]]


def halo_route(distance_a, distance_b):
    size_a = lax.axis_size("gx")
    size_b = lax.axis_size(("gy", "gz"))
    route = []
    for ia in range(size_a):
        for ib in range(size_b):
            target = ((ia + distance_a) % size_a) * size_b + (ib + distance_b) % size_b
            route.append((ia * size_b + ib, target))
    return route


def moved(block, distance_a, distance_b):
    return lax.ppermute(block, ("gx", "gy", "gz"), halo_route(distance_a, distance_b))


def shifted_block(both):
    from_a = moved(both[:, :SHIFT, SHIFT:], -1, 0)
    from_b = moved(both[:, SHIFT:, :SHIFT], 0, -1)
    from_ab = moved(both[:, :SHIFT, :SHIFT], -1, -1)
    upper = jnp.concatenate([both[:, SHIFT:, SHIFT:], from_b], axis=2)
    lower = jnp.concatenate([from_a, from_ab], axis=2)
    return jnp.concatenate([upper, lower], axis=1)


def unshifted_sum(grads_out, grad_shifted):
    narrow = grad_shifted.astype(jnp.bfloat16)
    to_a = moved(narrow[-SHIFT:, :-SHIFT], 1, 0).astype(jnp.float32)
    to_b = moved(narrow[:-SHIFT, -SHIFT:], 0, 1).astype(jnp.float32)
    to_ab = moved(narrow[-SHIFT:, -SHIFT:], 1, 1).astype(jnp.float32)
    upper = jnp.concatenate([to_ab, to_a], axis=1)
    lower = jnp.concatenate([to_b, grad_shifted[:-SHIFT, :-SHIFT]], axis=1)
    branch = jnp.concatenate([upper, lower], axis=0)
    return (grads_out.astype(jnp.float32) + branch.astype(jnp.float32)).astype(jnp.bfloat16)


def per_device(tokens, grads_out, labels, ln_gain, qkv_weight, proj_weight):
    brick_a, brick_b = (tokens.shape[0], tokens.shape[1])
    brick_c = NZ
    channels = C
    both = shifted_block(jnp.stack([tokens, grads_out]))
    extent_a = brick_a * lax.axis_size("gx")
    extent_b = brick_b * lax.axis_size(("gy", "gz"))
    first_index = lax.axis_index("gx") * brick_a + jnp.arange(brick_a, dtype=jnp.int32)
    second_index = lax.axis_index(("gy", "gz")) * brick_b + jnp.arange(brick_b, dtype=jnp.int32)
    wrap_first = (first_index >= extent_a - SHIFT).astype(jnp.int32)
    wrap_second = (second_index >= extent_b - SHIFT).astype(jnp.int32)
    wrap_third = (jnp.arange(brick_c, dtype=jnp.int32) >= brick_c - SHIFT).astype(jnp.int32)
    region = (
        wrap_first[:, None, None] * 4 + wrap_second[None, :, None] * 2 + wrap_third[None, None, :]
    )
    mask_key = to_windows_key(labels * 8 + region)

    constants = (
        mask_key[:, None, :],
        ln_gain.reshape(1, channels),
        qkv_weight,
        proj_weight,
    )
    partial = window_grads(True, (tokens, grads_out), *constants)
    grad_branch, qkv_part, proj_grad, gain_grad = window_grads(
        False, (both,), *constants, partial=partial
    )
    width = 4 * channels
    gain_row = jnp.pad(gain_grad.reshape(1, channels), ((0, 0), (0, width - channels)))
    summed = summed_everywhere(
        jnp.concatenate([jnp.concatenate([qkv_part, proj_grad], axis=1), gain_row], axis=0)
    )
    qkv_grad = summed[:channels, : 3 * channels]
    proj_grad = summed[:channels, 3 * channels :]
    gain_grad = summed[channels, :channels]
    grad_tokens = unshifted_sum(grads_out, grad_branch)
    return (grad_tokens, gain_grad.reshape(-1), qkv_grad.reshape(-1), proj_grad.reshape(-1))


def solution(mesh):
    return jax.shard_map(
        per_device,
        mesh=mesh,
        in_specs=(
            P("gx", ("gy", "gz"), None),
            P("gx", ("gy", "gz"), None),
            P("gx", ("gy", "gz"), None),
            P(),
            P(),
            P(),
        ),
        out_specs=(P("gx", ("gy", "gz"), None), P(), P(), P()),
        check_vma=False,
    )
```

```python
import jax
import jax.numpy as jnp
from jax import lax
from jax.experimental import pallas as pl
from jax.experimental.pallas import tpu as pltpu
from jax.sharding import PartitionSpec as P

HEADS = 6
C = 192
WIN = 8
SHIFT = 4
NZ = 16
CELLS = WIN**3
HEAD = C // HEADS
SCALE = HEAD ** (-0.5)
EXP2_SCALE = SCALE * 1.4426950408889634
PACKED_ROWS = 256


def passed_along(block, axis, distance):
    devices = range(lax.axis_size(axis))
    route = [((i - distance) % len(devices), i) for i in devices]
    return lax.ppermute(block, axis, route)


def to_windows_cm(values):
    extent_a, extent_b, extent_c, ch = values.shape
    shaped = values.reshape(extent_a // WIN, WIN, extent_b // WIN, WIN, extent_c // WIN, WIN, ch)
    return shaped.transpose(0, 2, 4, 6, 1, 3, 5).reshape(-1, ch, CELLS)


def from_windows_cm(values, extent_a, extent_b, extent_c):
    ch = values.shape[1]
    shaped = values.reshape(extent_a // WIN, extent_b // WIN, extent_c // WIN, ch, WIN, WIN, WIN)
    return shaped.transpose(0, 4, 1, 5, 2, 6, 3).reshape(extent_a, extent_b, extent_c, ch)


def to_windows_key(values):
    extent_a, extent_b, extent_c = values.shape
    shaped = values.reshape(extent_a // WIN, WIN, extent_b // WIN, WIN, extent_c // WIN, WIN)
    return shaped.transpose(0, 2, 4, 5, 1, 3).reshape(-1, CELLS)


def make_window_kernel(first):
    def window_kernel(*refs):
        if first:
            (tok_ref, grd_ref, krow_ref, gain_ref, wqkv_ref, wp_ref,
             gs_ref, gqkvT_ref, gproj_ref, ggain_ref, qkv_s, ga_s, drow_s, bias_s) = refs
        else:
            (both_ref, krow_ref, gain_ref, wqkv_ref, wp_ref,
             gs0_ref, gqkvT0_ref, gproj0_ref, ggain0_ref,
             gs_ref, gqkvT_ref, gproj_ref, ggain_ref, packed_ref, qkv_s, ga_s, drow_s, bias_s) = refs
        f32 = jnp.float32
        bf16 = jnp.bfloat16
        if first:
            gqkvT_ref[...] = jnp.zeros_like(gqkvT_ref)
            gproj_ref[...] = jnp.zeros_like(gproj_ref)
            ggain_ref[...] = jnp.zeros_like(ggain_ref)
        else:
            gqkvT_ref[...] = gqkvT0_ref[...]
            gproj_ref[...] = gproj0_ref[...]
            ggain_ref[...] = ggain0_ref[...]
            gs_ref[pl.ds(0, WIN), pl.ds(0, WIN), :] = gs0_ref[...]
        gain = jnp.broadcast_to(gain_ref[...], (8, C)).T[:, 0:1]
        wqkv_t = wqkv_ref[...].astype(f32).T.astype(bf16)
        nt = (((1,), (1,)), ((), ()))
        pair = 2 * C
        n_pairs = NZ // 2

        def gathered(which, i, j, l):
            pieces = []
            for q in range(WIN // 2):
                p = (WIN // 2 * l + SHIFT // 2 + q) % n_pairs
                if first:
                    source = (tok_ref, grd_ref)[which]
                    block = source[pl.ds(SHIFT, WIN), :, pl.ds(p * pair, pair)].astype(f32)
                    block = block[:, SHIFT:SHIFT + WIN]
                else:
                    block = both_ref[which, pl.ds(i * WIN, WIN), :, pl.ds(p * pair, pair)]
                    block = block.astype(f32)
                    block = jnp.where(j == 0, block[:, :WIN], block[:, WIN:])
                block = block.reshape(WIN * WIN, pair)
                pieces.append(block[:, :C])
                pieces.append(block[:, C:])
            return jnp.concatenate(pieces, axis=0).T

        def scattered(values_t, i, j, l):
            rows = values_t.T
            for q in range(WIN // 2):
                p = (WIN // 2 * l + SHIFT // 2 + q) % n_pairs
                even = rows[2 * q * WIN * WIN:(2 * q + 1) * WIN * WIN]
                odd = rows[(2 * q + 1) * WIN * WIN:(2 * q + 2) * WIN * WIN]
                block = jnp.concatenate([even, odd], axis=1).reshape(WIN, WIN, pair)
                if first:
                    gs_ref[:, :, pl.ds(p * pair, pair)] = block
                else:
                    gs_ref[
                        pl.ds(i * WIN, WIN),
                        pl.ds(pl.multiple_of(j * WIN, WIN), WIN),
                        pl.ds(p * pair, pair),
                    ] = block

        def window(ij, l):
            i = ij // 2
            j = ij % 2
            w = ij * 2 + l
            x = gathered(0, i, j, l)
            row_mean = jnp.mean(x, axis=0, keepdims=True)
            centred = x - row_mean
            inv_std = lax.rsqrt(jnp.mean(centred * centred, axis=0, keepdims=True) + 1e-05)
            x_hat = centred * inv_std
            normed = (x_hat * gain).astype(bf16)
            qkv_t = jnp.dot(wqkv_t, normed, preferred_element_type=f32)
            qkv_s[...] = qkv_t.astype(bf16).astype(f32)
            g = gathered(1, i, j, l).astype(bf16)
            ga_t = jnp.dot(wp_ref[...], g, preferred_element_type=f32)
            ga_s[...] = ga_t.astype(bf16).astype(f32)
            key_row = krow_ref[w].astype(f32)
            key_col = jnp.broadcast_to(key_row, (8, CELLS)).T[:, 0:1]
            bias_s[...] = jnp.where(key_col == key_row, 0.0, -jnp.inf)

            def head_step(h, carry):
                qo = pl.multiple_of(h * HEAD, HEAD)
                q_t = qkv_s[pl.ds(qo, HEAD), :]
                k_t = qkv_s[pl.ds(qo + C, HEAD), :]
                v_t = qkv_s[pl.ds(qo + 2 * C, HEAD), :]
                ga_th = ga_s[pl.ds(qo, HEAD), :]
                q = q_t.T.astype(bf16)
                scores = jnp.dot(q, k_t.astype(bf16), preferred_element_type=f32)
                weights = jnp.exp2(scores * EXP2_SCALE + bias_s[...])
                probs = weights / jnp.sum(weights, axis=1, keepdims=True)
                probs_bf = probs.astype(bf16)
                att_t = lax.dot_general(v_t.astype(bf16), probs_bf, nt, preferred_element_type=f32)
                att_t = att_t.astype(bf16)
                gproj_ref[pl.ds(qo, HEAD), :] += lax.dot_general(
                    att_t, g, nt, preferred_element_type=f32
                )
                ga = ga_th.T.astype(bf16)
                grad_probs = jnp.dot(ga, v_t.astype(bf16), preferred_element_type=f32)
                dv_t = jnp.dot(ga_th.astype(bf16), probs_bf, preferred_element_type=f32)
                row_total = jnp.sum(probs * grad_probs, axis=1, keepdims=True)
                grad_scores = (probs * (grad_probs - row_total) * SCALE).astype(bf16)
                dq_t = lax.dot_general(k_t.astype(bf16), grad_scores, nt, preferred_element_type=f32)
                dk_t = jnp.dot(q_t.astype(bf16), grad_scores, preferred_element_type=f32)
                drow_s[pl.ds(qo, HEAD), :] = dq_t.astype(bf16).astype(f32)
                drow_s[pl.ds(qo + C, HEAD), :] = dk_t.astype(bf16).astype(f32)
                drow_s[pl.ds(qo + 2 * C, HEAD), :] = dv_t.astype(bf16).astype(f32)
                return carry

            lax.fori_loop(0, HEADS, head_step, 0, unroll=3)
            rows_t = drow_s[...].astype(bf16)
            gqkvT_ref[...] += lax.dot_general(normed, rows_t, nt, preferred_element_type=f32)
            grad_normed = jnp.dot(wqkv_ref[...], rows_t, preferred_element_type=f32)
            ggain_ref[...] += jnp.sum(grad_normed * x_hat, axis=1, keepdims=True)
            scaled = grad_normed * gain
            grad_shifted = inv_std * (
                scaled
                - jnp.mean(scaled, axis=0, keepdims=True)
                - x_hat * jnp.mean(scaled * x_hat, axis=0, keepdims=True)
            )
            scattered(grad_shifted.astype(bf16).astype(f32), i, j, l)

        def block_step(ij, carry):
            for l in range(2):
                window(ij, l)
            return carry

        if first:
            block_step(0, 0)
        else:
            lax.fori_loop(1, 4, block_step, 0)
            packed_ref[pl.ds(0, C), :] = jnp.concatenate([gqkvT_ref[...], gproj_ref[...]], axis=1)
            gain_row = jnp.broadcast_to(ggain_ref[...], (C, 128)).T[0:1]
            tail = jnp.zeros((packed_ref.shape[0] - C, packed_ref.shape[1]), f32)
            tail = jnp.concatenate(
                [jnp.concatenate([gain_row, jnp.zeros((1, 3 * C), f32)], axis=1), tail[1:]], axis=0
            )
            packed_ref[pl.ds(C, packed_ref.shape[0] - C), :] = tail

    return window_kernel


def window_grads(first, arrays, krow, gain_row, wqkv, wp, partial=()):
    if first:
        extent_a, extent_b, width = WIN, WIN, arrays[0].shape[2]
    else:
        extent_a, extent_b, width = arrays[0].shape[1:]
    return pl.pallas_call(
        make_window_kernel(first),
        out_shape=[
            jax.ShapeDtypeStruct((extent_a, extent_b, width), jnp.float32),
            jax.ShapeDtypeStruct((C, 3 * C), jnp.float32),
            jax.ShapeDtypeStruct((C, C), jnp.float32),
            jax.ShapeDtypeStruct((C, 1), jnp.float32),
        ]
        + ([] if first else [jax.ShapeDtypeStruct((PACKED_ROWS, 4 * C), jnp.float32)]),
        scratch_shapes=[
            pltpu.VMEM((3 * C, CELLS), jnp.float32),
            pltpu.VMEM((C, CELLS), jnp.float32),
            pltpu.VMEM((3 * C, CELLS), jnp.float32),
            pltpu.VMEM((CELLS, CELLS), jnp.float32),
        ],
    )(*arrays, krow, gain_row, wqkv, wp, *partial)


SUM_AXES = ("gy", "gx", "gz")


def swapped(block, axis, distance):
    return lax.ppermute(block, axis, [(i, i ^ distance) for i in range(lax.axis_size(axis))])


def summed_everywhere(matrix):
    sizes = [lax.axis_size(axis) for axis in SUM_AXES]
    if any(size & (size - 1) for size in sizes):
        return lax.psum(matrix, SUM_AXES)
    devices = 1
    for size in sizes:
        devices *= size
    unit = devices * 8 if devices * 8 <= 2 * matrix.shape[0] else devices
    padded = -(-matrix.shape[0] // unit) * unit
    values = jnp.pad(matrix, ((0, padded - matrix.shape[0]), (0, 0)))
    steps = []
    for axis, size in zip(SUM_AXES, sizes):
        distance = 1
        while distance < size:
            bit = (lax.axis_index(axis) // distance) % 2
            half = values.shape[0] // 2
            keep = lax.dynamic_slice_in_dim(values, bit * half, half)
            send = lax.dynamic_slice_in_dim(values, (1 - bit) * half, half)
            values = keep + swapped(send, axis, distance)
            steps.append((axis, distance))
            distance *= 2
    for axis, distance in reversed(steps):
        bit = (lax.axis_index(axis) // distance) % 2
        other = swapped(values, axis, distance)
        half = values.shape[0]
        joined = jnp.zeros((2 * half,) + values.shape[1:], values.dtype)
        joined = lax.dynamic_update_slice_in_dim(joined, values, bit * half, 0)
        values = lax.dynamic_update_slice_in_dim(joined, other, (1 - bit) * half, 0)
    return values[: matrix.shape[0]]


def halo_route(distance_a, distance_b):
    size_a = lax.axis_size("gx")
    size_b = lax.axis_size(("gy", "gz"))
    route = []
    for ia in range(size_a):
        for ib in range(size_b):
            target = ((ia + distance_a) % size_a) * size_b + (ib + distance_b) % size_b
            route.append((ia * size_b + ib, target))
    return route


def moved(block, distance_a, distance_b):
    return lax.ppermute(block, ("gx", "gy", "gz"), halo_route(distance_a, distance_b))


def shifted_block(both):
    from_a = moved(both[:, :SHIFT, SHIFT:], -1, 0)
    from_b = moved(both[:, SHIFT:, :SHIFT], 0, -1)
    from_ab = moved(both[:, :SHIFT, :SHIFT], -1, -1)
    upper = jnp.concatenate([both[:, SHIFT:, SHIFT:], from_b], axis=2)
    lower = jnp.concatenate([from_a, from_ab], axis=2)
    return jnp.concatenate([upper, lower], axis=1)


def unshifted_sum(grads_out, grad_shifted):
    narrow = grad_shifted.astype(jnp.bfloat16)
    to_a = moved(narrow[-SHIFT:, :-SHIFT], 1, 0).astype(jnp.float32)
    to_b = moved(narrow[:-SHIFT, -SHIFT:], 0, 1).astype(jnp.float32)
    to_ab = moved(narrow[-SHIFT:, -SHIFT:], 1, 1).astype(jnp.float32)
    upper = jnp.concatenate([to_ab, to_a], axis=1)
    lower = jnp.concatenate([to_b, grad_shifted[:-SHIFT, :-SHIFT]], axis=1)
    branch = jnp.concatenate([upper, lower], axis=0)
    return (grads_out.astype(jnp.float32) + branch.astype(jnp.float32)).astype(jnp.bfloat16)


def per_device(tokens, grads_out, labels, ln_gain, qkv_weight, proj_weight):
    brick_a, brick_b = (tokens.shape[0], tokens.shape[1])
    brick_c = NZ
    channels = C
    both = shifted_block(jnp.stack([tokens, grads_out]))
    extent_a = brick_a * lax.axis_size("gx")
    extent_b = brick_b * lax.axis_size(("gy", "gz"))
    first_index = lax.axis_index("gx") * brick_a + jnp.arange(brick_a, dtype=jnp.int32)
    second_index = lax.axis_index(("gy", "gz")) * brick_b + jnp.arange(brick_b, dtype=jnp.int32)
    wrap_first = (first_index >= extent_a - SHIFT).astype(jnp.int32)
    wrap_second = (second_index >= extent_b - SHIFT).astype(jnp.int32)
    wrap_third = (jnp.arange(brick_c, dtype=jnp.int32) >= brick_c - SHIFT).astype(jnp.int32)
    region = (
        wrap_first[:, None, None] * 4 + wrap_second[None, :, None] * 2 + wrap_third[None, None, :]
    )
    mask_key = to_windows_key(labels * 8 + region)

    constants = (
        mask_key[:, None, :],
        ln_gain.reshape(1, channels),
        qkv_weight,
        proj_weight,
    )
    partial = window_grads(True, (tokens, grads_out), *constants)
    grad_branch, _, _, _, packed = window_grads(False, (both,), *constants, partial=partial)
    summed = summed_everywhere(packed)
    qkv_grad = summed[:channels, : 3 * channels]
    proj_grad = summed[:channels, 3 * channels :]
    gain_grad = summed[channels, :channels]
    grad_tokens = unshifted_sum(grads_out, grad_branch)
    return (grad_tokens, gain_grad.reshape(-1), qkv_grad.reshape(-1), proj_grad.reshape(-1))


def solution(mesh):
    return jax.shard_map(
        per_device,
        mesh=mesh,
        in_specs=(
            P("gx", ("gy", "gz"), None),
            P("gx", ("gy", "gz"), None),
            P("gx", ("gy", "gz"), None),
            P(),
            P(),
            P(),
        ),
        out_specs=(P("gx", ("gy", "gz"), None), P(), P(), P()),
        check_vma=False,
    )
```

```python
import jax
import jax.numpy as jnp
from jax import lax
from jax.experimental import pallas as pl
from jax.experimental.pallas import tpu as pltpu
from jax.sharding import PartitionSpec as P

HEADS = 6
C = 192
WIN = 8
SHIFT = 4
NZ = 16
CELLS = WIN**3
HEAD = C // HEADS
SCALE = HEAD ** (-0.5)
EXP2_SCALE = SCALE * 1.4426950408889634


def passed_along(block, axis, distance):
    devices = range(lax.axis_size(axis))
    route = [((i - distance) % len(devices), i) for i in devices]
    return lax.ppermute(block, axis, route)


def to_windows_cm(values):
    extent_a, extent_b, extent_c, ch = values.shape
    shaped = values.reshape(extent_a // WIN, WIN, extent_b // WIN, WIN, extent_c // WIN, WIN, ch)
    return shaped.transpose(0, 2, 4, 6, 1, 3, 5).reshape(-1, ch, CELLS)


def from_windows_cm(values, extent_a, extent_b, extent_c):
    ch = values.shape[1]
    shaped = values.reshape(extent_a // WIN, extent_b // WIN, extent_c // WIN, ch, WIN, WIN, WIN)
    return shaped.transpose(0, 4, 1, 5, 2, 6, 3).reshape(extent_a, extent_b, extent_c, ch)


def to_windows_key(values):
    extent_a, extent_b, extent_c = values.shape
    shaped = values.reshape(extent_a // WIN, WIN, extent_b // WIN, WIN, extent_c // WIN, WIN)
    return shaped.transpose(0, 2, 4, 5, 1, 3).reshape(-1, CELLS)


def make_window_kernel(first):
    def window_kernel(*refs):
        if first:
            (tok_ref, grd_ref, krow_ref, gain_ref, wqkv_ref, wp_ref,
             gs_ref, gqkvT_ref, gproj_ref, ggain_ref, qkv_s, ga_s, drow_s, bias_s) = refs
        else:
            (both_ref, krow_ref, gain_ref, wqkv_ref, wp_ref,
             gs0_ref, gqkvT0_ref, gproj0_ref, ggain0_ref,
             gs_ref, gqkvT_ref, gproj_ref, ggain_ref, qkv_s, ga_s, drow_s, bias_s) = refs
        f32 = jnp.float32
        bf16 = jnp.bfloat16
        if first:
            gqkvT_ref[...] = jnp.zeros_like(gqkvT_ref)
            gproj_ref[...] = jnp.zeros_like(gproj_ref)
            ggain_ref[...] = jnp.zeros_like(ggain_ref)
        else:
            gqkvT_ref[...] = gqkvT0_ref[...]
            gproj_ref[...] = gproj0_ref[...]
            ggain_ref[...] = ggain0_ref[...]
            gs_ref[pl.ds(0, WIN), pl.ds(0, WIN), :] = gs0_ref[...]
        gain = jnp.broadcast_to(gain_ref[...], (8, C)).T[:, 0:1]
        wqkv_t = wqkv_ref[...].astype(f32).T.astype(bf16)
        nt = (((1,), (1,)), ((), ()))
        pair = 2 * C
        n_pairs = NZ // 2

        def gathered(which, i, j, l):
            pieces = []
            for q in range(WIN // 2):
                p = (WIN // 2 * l + SHIFT // 2 + q) % n_pairs
                if first:
                    source = (tok_ref, grd_ref)[which]
                    block = source[pl.ds(SHIFT, WIN), :, pl.ds(p * pair, pair)].astype(f32)
                    block = block[:, SHIFT:SHIFT + WIN]
                else:
                    block = both_ref[which, pl.ds(i * WIN, WIN), :, pl.ds(p * pair, pair)]
                    block = block.astype(f32)
                    block = jnp.where(j == 0, block[:, :WIN], block[:, WIN:])
                block = block.reshape(WIN * WIN, pair)
                pieces.append(block[:, :C])
                pieces.append(block[:, C:])
            return jnp.concatenate(pieces, axis=0).T

        def scattered(values_t, i, j, l):
            rows = values_t.T
            for q in range(WIN // 2):
                p = (WIN // 2 * l + SHIFT // 2 + q) % n_pairs
                even = rows[2 * q * WIN * WIN:(2 * q + 1) * WIN * WIN]
                odd = rows[(2 * q + 1) * WIN * WIN:(2 * q + 2) * WIN * WIN]
                block = jnp.concatenate([even, odd], axis=1).reshape(WIN, WIN, pair)
                if first:
                    gs_ref[:, :, pl.ds(p * pair, pair)] = block
                else:
                    gs_ref[
                        pl.ds(i * WIN, WIN),
                        pl.ds(pl.multiple_of(j * WIN, WIN), WIN),
                        pl.ds(p * pair, pair),
                    ] = block

        def window(ij, l):
            i = ij // 2
            j = ij % 2
            w = ij * 2 + l
            x = gathered(0, i, j, l)
            row_mean = jnp.mean(x, axis=0, keepdims=True)
            centred = x - row_mean
            inv_std = lax.rsqrt(jnp.mean(centred * centred, axis=0, keepdims=True) + 1e-05)
            x_hat = centred * inv_std
            normed = (x_hat * gain).astype(bf16)
            qkv_t = jnp.dot(wqkv_t, normed, preferred_element_type=f32)
            qkv_s[...] = qkv_t.astype(bf16).astype(f32)
            g = gathered(1, i, j, l).astype(bf16)
            ga_t = jnp.dot(wp_ref[...], g, preferred_element_type=f32)
            ga_s[...] = ga_t.astype(bf16).astype(f32)
            key_row = krow_ref[w].astype(f32)
            key_col = jnp.broadcast_to(key_row, (8, CELLS)).T[:, 0:1]
            bias_s[...] = jnp.where(key_col == key_row, 0.0, -jnp.inf)

            def head_step(h, carry):
                qo = pl.multiple_of(h * HEAD, HEAD)
                q_t = qkv_s[pl.ds(qo, HEAD), :]
                k_t = qkv_s[pl.ds(qo + C, HEAD), :]
                v_t = qkv_s[pl.ds(qo + 2 * C, HEAD), :]
                ga_th = ga_s[pl.ds(qo, HEAD), :]
                q = q_t.T.astype(bf16)
                scores = jnp.dot(q, k_t.astype(bf16), preferred_element_type=f32)
                weights = jnp.exp2(scores * EXP2_SCALE + bias_s[...])
                probs = weights / jnp.sum(weights, axis=1, keepdims=True)
                probs_bf = probs.astype(bf16)
                att_t = lax.dot_general(v_t.astype(bf16), probs_bf, nt, preferred_element_type=f32)
                att_t = att_t.astype(bf16)
                gproj_ref[pl.ds(qo, HEAD), :] += lax.dot_general(
                    att_t, g, nt, preferred_element_type=f32
                )
                ga = ga_th.T.astype(bf16)
                grad_probs = jnp.dot(ga, v_t.astype(bf16), preferred_element_type=f32)
                dv_t = jnp.dot(ga_th.astype(bf16), probs_bf, preferred_element_type=f32)
                row_total = jnp.sum(probs * grad_probs, axis=1, keepdims=True)
                grad_scores = (probs * (grad_probs - row_total) * SCALE).astype(bf16)
                dq_t = lax.dot_general(k_t.astype(bf16), grad_scores, nt, preferred_element_type=f32)
                dk_t = jnp.dot(q_t.astype(bf16), grad_scores, preferred_element_type=f32)
                drow_s[pl.ds(qo, HEAD), :] = dq_t.astype(bf16).astype(f32)
                drow_s[pl.ds(qo + C, HEAD), :] = dk_t.astype(bf16).astype(f32)
                drow_s[pl.ds(qo + 2 * C, HEAD), :] = dv_t.astype(bf16).astype(f32)
                return carry

            lax.fori_loop(0, HEADS, head_step, 0, unroll=3)
            rows_t = drow_s[...].astype(bf16)
            gqkvT_ref[...] += lax.dot_general(normed, rows_t, nt, preferred_element_type=f32)
            grad_normed = jnp.dot(wqkv_ref[...], rows_t, preferred_element_type=f32)
            ggain_ref[...] += jnp.sum(grad_normed * x_hat, axis=1, keepdims=True)
            scaled = grad_normed * gain
            grad_shifted = inv_std * (
                scaled
                - jnp.mean(scaled, axis=0, keepdims=True)
                - x_hat * jnp.mean(scaled * x_hat, axis=0, keepdims=True)
            )
            scattered(grad_shifted.astype(bf16).astype(f32), i, j, l)

        def block_step(ij, carry):
            for l in range(2):
                window(ij, l)
            return carry

        if first:
            block_step(0, 0)
        else:
            lax.fori_loop(1, 4, block_step, 0)

    return window_kernel


def window_grads(first, arrays, krow, gain_row, wqkv, wp, partial=()):
    if first:
        extent_a, extent_b, width = WIN, WIN, arrays[0].shape[2]
    else:
        extent_a, extent_b, width = arrays[0].shape[1:]
    return pl.pallas_call(
        make_window_kernel(first),
        out_shape=[
            jax.ShapeDtypeStruct((extent_a, extent_b, width), jnp.float32),
            jax.ShapeDtypeStruct((C, 3 * C), jnp.float32),
            jax.ShapeDtypeStruct((C, C), jnp.float32),
            jax.ShapeDtypeStruct((C, 1), jnp.float32),
        ],
        scratch_shapes=[
            pltpu.VMEM((3 * C, CELLS), jnp.float32),
            pltpu.VMEM((C, CELLS), jnp.float32),
            pltpu.VMEM((3 * C, CELLS), jnp.float32),
            pltpu.VMEM((CELLS, CELLS), jnp.float32),
        ],
    )(*arrays, krow, gain_row, wqkv, wp, *partial)


SUM_AXES = ("gy", "gz", "gx")


def swapped(block, axis, distance):
    return lax.ppermute(block, axis, [(i, i ^ distance) for i in range(lax.axis_size(axis))])


def summed_everywhere(matrix):
    sizes = [lax.axis_size(axis) for axis in SUM_AXES]
    if any(size & (size - 1) for size in sizes):
        return lax.psum(matrix, SUM_AXES)
    devices = 1
    for size in sizes:
        devices *= size
    unit = devices * 8 if devices * 8 <= 2 * matrix.shape[0] else devices
    padded = -(-matrix.shape[0] // unit) * unit
    values = jnp.pad(matrix, ((0, padded - matrix.shape[0]), (0, 0)))
    steps = []
    for axis, size in zip(SUM_AXES, sizes):
        distance = 1
        while distance < size:
            bit = (lax.axis_index(axis) // distance) % 2
            half = values.shape[0] // 2
            keep = lax.dynamic_slice_in_dim(values, bit * half, half)
            send = lax.dynamic_slice_in_dim(values, (1 - bit) * half, half)
            values = keep + swapped(send, axis, distance)
            steps.append((axis, distance))
            distance *= 2
    for axis, distance in reversed(steps):
        bit = (lax.axis_index(axis) // distance) % 2
        other = swapped(values, axis, distance)
        half = values.shape[0]
        joined = jnp.zeros((2 * half,) + values.shape[1:], values.dtype)
        joined = lax.dynamic_update_slice_in_dim(joined, values, bit * half, 0)
        values = lax.dynamic_update_slice_in_dim(joined, other, (1 - bit) * half, 0)
    return values[: matrix.shape[0]]


def halo_route(distance_a, distance_b):
    size_a = lax.axis_size("gx")
    size_b = lax.axis_size(("gy", "gz"))
    route = []
    for ia in range(size_a):
        for ib in range(size_b):
            target = ((ia + distance_a) % size_a) * size_b + (ib + distance_b) % size_b
            route.append((ia * size_b + ib, target))
    return route


def moved(block, distance_a, distance_b):
    return lax.ppermute(block, ("gx", "gy", "gz"), halo_route(distance_a, distance_b))


def shifted_block(both):
    from_a = moved(both[:, :SHIFT, SHIFT:], -1, 0)
    from_b = moved(both[:, SHIFT:, :SHIFT], 0, -1)
    from_ab = moved(both[:, :SHIFT, :SHIFT], -1, -1)
    upper = jnp.concatenate([both[:, SHIFT:, SHIFT:], from_b], axis=2)
    lower = jnp.concatenate([from_a, from_ab], axis=2)
    return jnp.concatenate([upper, lower], axis=1)


def unshifted_sum(grads_out, grad_shifted):
    narrow = grad_shifted.astype(jnp.bfloat16)
    to_a = moved(narrow[-SHIFT:, :-SHIFT], 1, 0).astype(jnp.float32)
    to_b = moved(narrow[:-SHIFT, -SHIFT:], 0, 1).astype(jnp.float32)
    to_ab = moved(narrow[-SHIFT:, -SHIFT:], 1, 1).astype(jnp.float32)
    upper = jnp.concatenate([to_ab, to_a], axis=1)
    lower = jnp.concatenate([to_b, grad_shifted[:-SHIFT, :-SHIFT]], axis=1)
    branch = jnp.concatenate([upper, lower], axis=0)
    return (grads_out.astype(jnp.float32) + branch.astype(jnp.float32)).astype(jnp.bfloat16)


def per_device(tokens, grads_out, labels, ln_gain, qkv_weight, proj_weight):
    brick_a, brick_b = (tokens.shape[0], tokens.shape[1])
    brick_c = NZ
    channels = C
    both = shifted_block(jnp.stack([tokens, grads_out]))
    extent_a = brick_a * lax.axis_size("gx")
    extent_b = brick_b * lax.axis_size(("gy", "gz"))
    first_index = lax.axis_index("gx") * brick_a + jnp.arange(brick_a, dtype=jnp.int32)
    second_index = lax.axis_index(("gy", "gz")) * brick_b + jnp.arange(brick_b, dtype=jnp.int32)
    wrap_first = (first_index >= extent_a - SHIFT).astype(jnp.int32)
    wrap_second = (second_index >= extent_b - SHIFT).astype(jnp.int32)
    wrap_third = (jnp.arange(brick_c, dtype=jnp.int32) >= brick_c - SHIFT).astype(jnp.int32)
    region = (
        wrap_first[:, None, None] * 4 + wrap_second[None, :, None] * 2 + wrap_third[None, None, :]
    )
    mask_key = to_windows_key(labels * 8 + region)

    constants = (
        mask_key[:, None, :],
        ln_gain.reshape(1, channels),
        qkv_weight,
        proj_weight,
    )
    partial = window_grads(True, (tokens, grads_out), *constants)
    grad_branch, qkv_part, proj_grad, gain_grad = window_grads(
        False, (both,), *constants, partial=partial
    )
    width = 4 * channels
    gain_row = jnp.pad(gain_grad.reshape(1, channels), ((0, 0), (0, width - channels)))
    summed = summed_everywhere(
        jnp.concatenate([jnp.concatenate([qkv_part, proj_grad], axis=1), gain_row], axis=0)
    )
    qkv_grad = summed[:channels, : 3 * channels]
    proj_grad = summed[:channels, 3 * channels :]
    gain_grad = summed[channels, :channels]
    grad_tokens = unshifted_sum(grads_out, grad_branch)
    return (grad_tokens, gain_grad.reshape(-1), qkv_grad.reshape(-1), proj_grad.reshape(-1))


def solution(mesh):
    return jax.shard_map(
        per_device,
        mesh=mesh,
        in_specs=(
            P("gx", ("gy", "gz"), None),
            P("gx", ("gy", "gz"), None),
            P("gx", ("gy", "gz"), None),
            P(),
            P(),
            P(),
        ),
        out_specs=(P("gx", ("gy", "gz"), None), P(), P(), P()),
        check_vma=False,
    )
```

```python
import jax
import jax.numpy as jnp
from jax import lax
from jax.experimental import pallas as pl
from jax.experimental.pallas import tpu as pltpu
from jax.sharding import PartitionSpec as P

HEADS = 6
C = 192
WIN = 8
SHIFT = 4
NZ = 16
CELLS = WIN**3
HEAD = C // HEADS
SCALE = HEAD ** (-0.5)
EXP2_SCALE = SCALE * 1.4426950408889634


def passed_along(block, axis, distance):
    devices = range(lax.axis_size(axis))
    route = [((i - distance) % len(devices), i) for i in devices]
    return lax.ppermute(block, axis, route)


def to_windows_cm(values):
    extent_a, extent_b, extent_c, ch = values.shape
    shaped = values.reshape(extent_a // WIN, WIN, extent_b // WIN, WIN, extent_c // WIN, WIN, ch)
    return shaped.transpose(0, 2, 4, 6, 1, 3, 5).reshape(-1, ch, CELLS)


def from_windows_cm(values, extent_a, extent_b, extent_c):
    ch = values.shape[1]
    shaped = values.reshape(extent_a // WIN, extent_b // WIN, extent_c // WIN, ch, WIN, WIN, WIN)
    return shaped.transpose(0, 4, 1, 5, 2, 6, 3).reshape(extent_a, extent_b, extent_c, ch)


def to_windows_key(values):
    extent_a, extent_b, extent_c = values.shape
    shaped = values.reshape(extent_a // WIN, WIN, extent_b // WIN, WIN, extent_c // WIN, WIN)
    return shaped.transpose(0, 2, 4, 5, 1, 3).reshape(-1, CELLS)


def make_window_kernel(first):
    def window_kernel(*refs):
        if first:
            (tok_ref, grd_ref, krow_ref, gain_ref, wqkv_ref, wp_ref,
             gs_ref, gqkvT_ref, gproj_ref, ggain_ref, qkv_s, ga_s, drow_s, bias_s) = refs
        else:
            (both_ref, krow_ref, gain_ref, wqkv_ref, wp_ref,
             gs0_ref, gqkvT0_ref, gproj0_ref, ggain0_ref,
             gs_ref, gqkvT_ref, gproj_ref, ggain_ref, qkv_s, ga_s, drow_s, bias_s) = refs
        f32 = jnp.float32
        bf16 = jnp.bfloat16
        if first:
            gqkvT_ref[...] = jnp.zeros_like(gqkvT_ref)
            gproj_ref[...] = jnp.zeros_like(gproj_ref)
            ggain_ref[...] = jnp.zeros_like(ggain_ref)
        else:
            gqkvT_ref[...] = gqkvT0_ref[...]
            gproj_ref[...] = gproj0_ref[...]
            ggain_ref[...] = ggain0_ref[...]
            gs_ref[pl.ds(0, WIN), pl.ds(0, WIN), :] = gs0_ref[...]
        gain = jnp.broadcast_to(gain_ref[...], (8, C)).T[:, 0:1]
        wqkv_t = wqkv_ref[...].astype(f32).T.astype(bf16)
        nt = (((1,), (1,)), ((), ()))
        pair = 2 * C
        n_pairs = NZ // 2

        def gathered(which, i, j, l):
            pieces = []
            for q in range(WIN // 2):
                p = (WIN // 2 * l + SHIFT // 2 + q) % n_pairs
                if first:
                    source = (tok_ref, grd_ref)[which]
                    block = source[pl.ds(SHIFT, WIN), :, pl.ds(p * pair, pair)].astype(f32)
                    block = block[:, SHIFT:SHIFT + WIN]
                else:
                    block = both_ref[which, pl.ds(i * WIN, WIN), :, pl.ds(p * pair, pair)]
                    block = block.astype(f32)
                    block = jnp.where(j == 0, block[:, :WIN], block[:, WIN:])
                block = block.reshape(WIN * WIN, pair)
                pieces.append(block[:, :C])
                pieces.append(block[:, C:])
            return jnp.concatenate(pieces, axis=0).T

        def scattered(values_t, i, j, l):
            rows = values_t.T
            for q in range(WIN // 2):
                p = (WIN // 2 * l + SHIFT // 2 + q) % n_pairs
                even = rows[2 * q * WIN * WIN:(2 * q + 1) * WIN * WIN]
                odd = rows[(2 * q + 1) * WIN * WIN:(2 * q + 2) * WIN * WIN]
                block = jnp.concatenate([even, odd], axis=1).reshape(WIN, WIN, pair)
                if first:
                    gs_ref[:, :, pl.ds(p * pair, pair)] = block
                else:
                    gs_ref[
                        pl.ds(i * WIN, WIN),
                        pl.ds(pl.multiple_of(j * WIN, WIN), WIN),
                        pl.ds(p * pair, pair),
                    ] = block

        def window(ij, l):
            i = ij // 2
            j = ij % 2
            w = ij * 2 + l
            x = gathered(0, i, j, l)
            row_mean = jnp.mean(x, axis=0, keepdims=True)
            centred = x - row_mean
            inv_std = lax.rsqrt(jnp.mean(centred * centred, axis=0, keepdims=True) + 1e-05)
            x_hat = centred * inv_std
            normed = (x_hat * gain).astype(bf16)
            qkv_t = jnp.dot(wqkv_t, normed, preferred_element_type=f32)
            qkv_s[...] = qkv_t.astype(bf16).astype(f32)
            g = gathered(1, i, j, l).astype(bf16)
            ga_t = jnp.dot(wp_ref[...], g, preferred_element_type=f32)
            ga_s[...] = ga_t.astype(bf16).astype(f32)
            key_row = krow_ref[w].astype(f32)
            key_col = jnp.broadcast_to(key_row, (8, CELLS)).T[:, 0:1]
            bias_s[...] = jnp.where(key_col == key_row, 0.0, -jnp.inf)

            def head_step(h, carry):
                qo = pl.multiple_of(h * HEAD, HEAD)
                q_t = qkv_s[pl.ds(qo, HEAD), :]
                k_t = qkv_s[pl.ds(qo + C, HEAD), :]
                v_t = qkv_s[pl.ds(qo + 2 * C, HEAD), :]
                ga_th = ga_s[pl.ds(qo, HEAD), :]
                q = q_t.T.astype(bf16)
                scores = jnp.dot(q, k_t.astype(bf16), preferred_element_type=f32)
                weights = jnp.exp2(scores * EXP2_SCALE + bias_s[...])
                probs = weights / jnp.sum(weights, axis=1, keepdims=True)
                probs_bf = probs.astype(bf16)
                att_t = lax.dot_general(v_t.astype(bf16), probs_bf, nt, preferred_element_type=f32)
                att_t = att_t.astype(bf16)
                gproj_ref[pl.ds(qo, HEAD), :] += lax.dot_general(
                    att_t, g, nt, preferred_element_type=f32
                )
                ga = ga_th.T.astype(bf16)
                grad_probs = jnp.dot(ga, v_t.astype(bf16), preferred_element_type=f32)
                dv_t = jnp.dot(ga_th.astype(bf16), probs_bf, preferred_element_type=f32)
                row_total = jnp.sum(probs * grad_probs, axis=1, keepdims=True)
                grad_scores = (probs * (grad_probs - row_total) * SCALE).astype(bf16)
                dq_t = lax.dot_general(k_t.astype(bf16), grad_scores, nt, preferred_element_type=f32)
                dk_t = jnp.dot(q_t.astype(bf16), grad_scores, preferred_element_type=f32)
                drow_s[pl.ds(qo, HEAD), :] = dq_t.astype(bf16).astype(f32)
                drow_s[pl.ds(qo + C, HEAD), :] = dk_t.astype(bf16).astype(f32)
                drow_s[pl.ds(qo + 2 * C, HEAD), :] = dv_t.astype(bf16).astype(f32)
                return carry

            lax.fori_loop(0, HEADS, head_step, 0, unroll=3)
            rows_t = drow_s[...].astype(bf16)
            gqkvT_ref[...] += lax.dot_general(normed, rows_t, nt, preferred_element_type=f32)
            grad_normed = jnp.dot(wqkv_ref[...], rows_t, preferred_element_type=f32)
            ggain_ref[...] += jnp.sum(grad_normed * x_hat, axis=1, keepdims=True)
            scaled = grad_normed * gain
            grad_shifted = inv_std * (
                scaled
                - jnp.mean(scaled, axis=0, keepdims=True)
                - x_hat * jnp.mean(scaled * x_hat, axis=0, keepdims=True)
            )
            scattered(grad_shifted.astype(bf16).astype(f32), i, j, l)

        def block_step(ij, carry):
            for l in range(2):
                window(ij, l)
            return carry

        if first:
            block_step(0, 0)
        else:
            lax.fori_loop(1, 4, block_step, 0)

    return window_kernel


def window_grads(first, arrays, krow, gain_row, wqkv, wp, partial=()):
    if first:
        extent_a, extent_b, width = WIN, WIN, arrays[0].shape[2]
    else:
        extent_a, extent_b, width = arrays[0].shape[1:]
    return pl.pallas_call(
        make_window_kernel(first),
        out_shape=[
            jax.ShapeDtypeStruct((extent_a, extent_b, width), jnp.float32),
            jax.ShapeDtypeStruct((C, 3 * C), jnp.float32),
            jax.ShapeDtypeStruct((C, C), jnp.float32),
            jax.ShapeDtypeStruct((C, 1), jnp.float32),
        ],
        scratch_shapes=[
            pltpu.VMEM((3 * C, CELLS), jnp.float32),
            pltpu.VMEM((C, CELLS), jnp.float32),
            pltpu.VMEM((3 * C, CELLS), jnp.float32),
            pltpu.VMEM((CELLS, CELLS), jnp.float32),
        ],
    )(*arrays, krow, gain_row, wqkv, wp, *partial)


SUM_AXES = ("gz", "gy", "gx")


def swapped(block, axis, distance):
    return lax.ppermute(block, axis, [(i, i ^ distance) for i in range(lax.axis_size(axis))])


def summed_everywhere(matrix):
    sizes = [lax.axis_size(axis) for axis in SUM_AXES]
    if any(size & (size - 1) for size in sizes):
        return lax.psum(matrix, SUM_AXES)
    devices = 1
    for size in sizes:
        devices *= size
    unit = devices * 8 if devices * 8 <= 2 * matrix.shape[0] else devices
    padded = -(-matrix.shape[0] // unit) * unit
    values = jnp.pad(matrix, ((0, padded - matrix.shape[0]), (0, 0)))
    steps = []
    for axis, size in zip(SUM_AXES, sizes):
        distance = 1
        while distance < size:
            bit = (lax.axis_index(axis) // distance) % 2
            half = values.shape[0] // 2
            keep = lax.dynamic_slice_in_dim(values, bit * half, half)
            send = lax.dynamic_slice_in_dim(values, (1 - bit) * half, half)
            values = keep + swapped(send, axis, distance)
            steps.append((axis, distance))
            distance *= 2
    for axis, distance in reversed(steps):
        bit = (lax.axis_index(axis) // distance) % 2
        other = swapped(values, axis, distance)
        half = values.shape[0]
        joined = jnp.zeros((2 * half,) + values.shape[1:], values.dtype)
        joined = lax.dynamic_update_slice_in_dim(joined, values, bit * half, 0)
        values = lax.dynamic_update_slice_in_dim(joined, other, (1 - bit) * half, 0)
    return values[: matrix.shape[0]]


def halo_route(distance_a, distance_b):
    size_a = lax.axis_size("gx")
    size_b = lax.axis_size(("gy", "gz"))
    route = []
    for ia in range(size_a):
        for ib in range(size_b):
            target = ((ia + distance_a) % size_a) * size_b + (ib + distance_b) % size_b
            route.append((ia * size_b + ib, target))
    return route


def moved(block, distance_a, distance_b):
    return lax.ppermute(block, ("gx", "gy", "gz"), halo_route(distance_a, distance_b))


def shifted_block(both):
    from_a = moved(both[:, :SHIFT, SHIFT:], -1, 0)
    from_b = moved(both[:, SHIFT:, :SHIFT], 0, -1)
    from_ab = moved(both[:, :SHIFT, :SHIFT], -1, -1)
    upper = jnp.concatenate([both[:, SHIFT:, SHIFT:], from_b], axis=2)
    lower = jnp.concatenate([from_a, from_ab], axis=2)
    return jnp.concatenate([upper, lower], axis=1)


def unshifted_sum(grads_out, grad_shifted):
    narrow = grad_shifted.astype(jnp.bfloat16)
    to_a = moved(narrow[-SHIFT:, :-SHIFT], 1, 0).astype(jnp.float32)
    to_b = moved(narrow[:-SHIFT, -SHIFT:], 0, 1).astype(jnp.float32)
    to_ab = moved(narrow[-SHIFT:, -SHIFT:], 1, 1).astype(jnp.float32)
    upper = jnp.concatenate([to_ab, to_a], axis=1)
    lower = jnp.concatenate([to_b, grad_shifted[:-SHIFT, :-SHIFT]], axis=1)
    branch = jnp.concatenate([upper, lower], axis=0)
    return (grads_out.astype(jnp.float32) + branch.astype(jnp.float32)).astype(jnp.bfloat16)


def per_device(tokens, grads_out, labels, ln_gain, qkv_weight, proj_weight):
    brick_a, brick_b = (tokens.shape[0], tokens.shape[1])
    brick_c = NZ
    channels = C
    both = shifted_block(jnp.stack([tokens, grads_out]))
    extent_a = brick_a * lax.axis_size("gx")
    extent_b = brick_b * lax.axis_size(("gy", "gz"))
    first_index = lax.axis_index("gx") * brick_a + jnp.arange(brick_a, dtype=jnp.int32)
    second_index = lax.axis_index(("gy", "gz")) * brick_b + jnp.arange(brick_b, dtype=jnp.int32)
    wrap_first = (first_index >= extent_a - SHIFT).astype(jnp.int32)
    wrap_second = (second_index >= extent_b - SHIFT).astype(jnp.int32)
    wrap_third = (jnp.arange(brick_c, dtype=jnp.int32) >= brick_c - SHIFT).astype(jnp.int32)
    region = (
        wrap_first[:, None, None] * 4 + wrap_second[None, :, None] * 2 + wrap_third[None, None, :]
    )
    mask_key = to_windows_key(labels * 8 + region)

    constants = (
        mask_key[:, None, :],
        ln_gain.reshape(1, channels),
        qkv_weight,
        proj_weight,
    )
    partial = window_grads(True, (tokens, grads_out), *constants)
    grad_branch, qkv_part, proj_grad, gain_grad = window_grads(
        False, (both,), *constants, partial=partial
    )
    width = 4 * channels
    gain_row = jnp.pad(gain_grad.reshape(1, channels), ((0, 0), (0, width - channels)))
    summed = summed_everywhere(
        jnp.concatenate([jnp.concatenate([qkv_part, proj_grad], axis=1), gain_row], axis=0)
    )
    qkv_grad = summed[:channels, : 3 * channels]
    proj_grad = summed[:channels, 3 * channels :]
    gain_grad = summed[channels, :channels]
    grad_tokens = unshifted_sum(grads_out, grad_branch)
    return (grad_tokens, gain_grad.reshape(-1), qkv_grad.reshape(-1), proj_grad.reshape(-1))


def solution(mesh):
    return jax.shard_map(
        per_device,
        mesh=mesh,
        in_specs=(
            P("gx", ("gy", "gz"), None),
            P("gx", ("gy", "gz"), None),
            P("gx", ("gy", "gz"), None),
            P(),
            P(),
            P(),
        ),
        out_specs=(P("gx", ("gy", "gz"), None), P(), P(), P()),
        check_vma=False,
    )
```

```python
import jax
import jax.numpy as jnp
from jax import lax
from jax.experimental import pallas as pl
from jax.experimental.pallas import tpu as pltpu
from jax.sharding import PartitionSpec as P

HEADS = 6
C = 192
WIN = 8
SHIFT = 4
NZ = 16
CELLS = WIN**3
HEAD = C // HEADS
SCALE = HEAD ** (-0.5)
EXP2_SCALE = SCALE * 1.4426950408889634


def passed_along(block, axis, distance):
    devices = range(lax.axis_size(axis))
    route = [((i - distance) % len(devices), i) for i in devices]
    return lax.ppermute(block, axis, route)


def to_windows_cm(values):
    extent_a, extent_b, extent_c, ch = values.shape
    shaped = values.reshape(extent_a // WIN, WIN, extent_b // WIN, WIN, extent_c // WIN, WIN, ch)
    return shaped.transpose(0, 2, 4, 6, 1, 3, 5).reshape(-1, ch, CELLS)


def from_windows_cm(values, extent_a, extent_b, extent_c):
    ch = values.shape[1]
    shaped = values.reshape(extent_a // WIN, extent_b // WIN, extent_c // WIN, ch, WIN, WIN, WIN)
    return shaped.transpose(0, 4, 1, 5, 2, 6, 3).reshape(extent_a, extent_b, extent_c, ch)


def to_windows_key(values):
    extent_a, extent_b, extent_c = values.shape
    shaped = values.reshape(extent_a // WIN, WIN, extent_b // WIN, WIN, extent_c // WIN, WIN)
    return shaped.transpose(0, 2, 4, 5, 1, 3).reshape(-1, CELLS)


def make_window_kernel(first):
    def window_kernel(*refs):
        if first:
            (tok_ref, grd_ref, krow_ref, gain_ref, wqkv_ref, wp_ref,
             gs_ref, gqkvT_ref, gproj_ref, ggain_ref, qkv_s, ga_s, drow_s, bias_s) = refs
        else:
            (both_ref, krow_ref, gain_ref, wqkv_ref, wp_ref,
             gs0_ref, gqkvT0_ref, gproj0_ref, ggain0_ref,
             gs_ref, gqkvT_ref, gproj_ref, ggain_ref, qkv_s, ga_s, drow_s, bias_s) = refs
        f32 = jnp.float32
        bf16 = jnp.bfloat16
        if first:
            gqkvT_ref[...] = jnp.zeros_like(gqkvT_ref)
            gproj_ref[...] = jnp.zeros_like(gproj_ref)
            ggain_ref[...] = jnp.zeros_like(ggain_ref)
        else:
            gqkvT_ref[...] = gqkvT0_ref[...]
            gproj_ref[...] = gproj0_ref[...]
            ggain_ref[...] = ggain0_ref[...]
            gs_ref[pl.ds(0, WIN), pl.ds(0, WIN), :] = gs0_ref[...]
        gain = jnp.broadcast_to(gain_ref[...], (8, C)).T[:, 0:1]
        wqkv_t = wqkv_ref[...].astype(f32).T.astype(bf16)
        nt = (((1,), (1,)), ((), ()))
        pair = 2 * C
        n_pairs = NZ // 2

        def gathered(which, i, j, l):
            pieces = []
            for q in range(WIN // 2):
                p = (WIN // 2 * l + SHIFT // 2 + q) % n_pairs
                if first:
                    source = (tok_ref, grd_ref)[which]
                    block = source[pl.ds(SHIFT, WIN), :, pl.ds(p * pair, pair)].astype(f32)
                    block = block[:, SHIFT:SHIFT + WIN]
                else:
                    block = both_ref[which, pl.ds(i * WIN, WIN), :, pl.ds(p * pair, pair)]
                    block = block.astype(f32)
                    block = jnp.where(j == 0, block[:, :WIN], block[:, WIN:])
                block = block.reshape(WIN * WIN, pair)
                pieces.append(block[:, :C])
                pieces.append(block[:, C:])
            return jnp.concatenate(pieces, axis=0).T

        def scattered(values_t, i, j, l):
            rows = values_t.T
            for q in range(WIN // 2):
                p = (WIN // 2 * l + SHIFT // 2 + q) % n_pairs
                even = rows[2 * q * WIN * WIN:(2 * q + 1) * WIN * WIN]
                odd = rows[(2 * q + 1) * WIN * WIN:(2 * q + 2) * WIN * WIN]
                block = jnp.concatenate([even, odd], axis=1).reshape(WIN, WIN, pair)
                if first:
                    gs_ref[:, :, pl.ds(p * pair, pair)] = block
                else:
                    gs_ref[
                        pl.ds(i * WIN, WIN),
                        pl.ds(pl.multiple_of(j * WIN, WIN), WIN),
                        pl.ds(p * pair, pair),
                    ] = block

        def window(ij, l):
            i = ij // 2
            j = ij % 2
            w = ij * 2 + l
            x = gathered(0, i, j, l)
            row_mean = jnp.mean(x, axis=0, keepdims=True)
            centred = x - row_mean
            inv_std = lax.rsqrt(jnp.mean(centred * centred, axis=0, keepdims=True) + 1e-05)
            x_hat = centred * inv_std
            normed = (x_hat * gain).astype(bf16)
            qkv_t = jnp.dot(wqkv_t, normed, preferred_element_type=f32)
            qkv_s[...] = qkv_t.astype(bf16).astype(f32)
            g = gathered(1, i, j, l).astype(bf16)
            ga_t = jnp.dot(wp_ref[...], g, preferred_element_type=f32)
            ga_s[...] = ga_t.astype(bf16).astype(f32)
            key_row = krow_ref[w].astype(f32)
            key_col = jnp.broadcast_to(key_row, (8, CELLS)).T[:, 0:1]
            bias_s[...] = jnp.where(key_col == key_row, 0.0, -jnp.inf)

            def head_step(h, carry):
                qo = pl.multiple_of(h * HEAD, HEAD)
                q_t = qkv_s[pl.ds(qo, HEAD), :]
                k_t = qkv_s[pl.ds(qo + C, HEAD), :]
                v_t = qkv_s[pl.ds(qo + 2 * C, HEAD), :]
                ga_th = ga_s[pl.ds(qo, HEAD), :]
                q = q_t.T.astype(bf16)
                scores = jnp.dot(q, k_t.astype(bf16), preferred_element_type=f32)
                weights = jnp.exp2(scores * EXP2_SCALE + bias_s[...])
                probs = weights / jnp.sum(weights, axis=1, keepdims=True)
                probs_bf = probs.astype(bf16)
                att_t = lax.dot_general(v_t.astype(bf16), probs_bf, nt, preferred_element_type=f32)
                att_t = att_t.astype(bf16)
                gproj_ref[pl.ds(qo, HEAD), :] += lax.dot_general(
                    att_t, g, nt, preferred_element_type=f32
                )
                ga = ga_th.T.astype(bf16)
                grad_probs = jnp.dot(ga, v_t.astype(bf16), preferred_element_type=f32)
                dv_t = jnp.dot(ga_th.astype(bf16), probs_bf, preferred_element_type=f32)
                row_total = jnp.sum(probs * grad_probs, axis=1, keepdims=True)
                grad_scores = (probs * (grad_probs - row_total) * SCALE).astype(bf16)
                dq_t = lax.dot_general(k_t.astype(bf16), grad_scores, nt, preferred_element_type=f32)
                dk_t = jnp.dot(q_t.astype(bf16), grad_scores, preferred_element_type=f32)
                drow_s[pl.ds(qo, HEAD), :] = dq_t.astype(bf16).astype(f32)
                drow_s[pl.ds(qo + C, HEAD), :] = dk_t.astype(bf16).astype(f32)
                drow_s[pl.ds(qo + 2 * C, HEAD), :] = dv_t.astype(bf16).astype(f32)
                return carry

            lax.fori_loop(0, HEADS, head_step, 0, unroll=3)
            rows_t = drow_s[...].astype(bf16)
            gqkvT_ref[...] += lax.dot_general(normed, rows_t, nt, preferred_element_type=f32)
            grad_normed = jnp.dot(wqkv_ref[...], rows_t, preferred_element_type=f32)
            ggain_ref[...] += jnp.sum(grad_normed * x_hat, axis=1, keepdims=True)
            scaled = grad_normed * gain
            grad_shifted = inv_std * (
                scaled
                - jnp.mean(scaled, axis=0, keepdims=True)
                - x_hat * jnp.mean(scaled * x_hat, axis=0, keepdims=True)
            )
            scattered(grad_shifted.astype(bf16).astype(f32), i, j, l)

        def block_step(ij, carry):
            for l in range(2):
                window(ij, l)
            return carry

        if first:
            block_step(0, 0)
        else:
            lax.fori_loop(1, 4, block_step, 0)

    return window_kernel


def window_grads(first, arrays, krow, gain_row, wqkv, wp, partial=()):
    if first:
        extent_a, extent_b, width = WIN, WIN, arrays[0].shape[2]
    else:
        extent_a, extent_b, width = arrays[0].shape[1:]
    return pl.pallas_call(
        make_window_kernel(first),
        out_shape=[
            jax.ShapeDtypeStruct((extent_a, extent_b, width), jnp.float32),
            jax.ShapeDtypeStruct((C, 3 * C), jnp.float32),
            jax.ShapeDtypeStruct((C, C), jnp.float32),
            jax.ShapeDtypeStruct((C, 1), jnp.float32),
        ],
        scratch_shapes=[
            pltpu.VMEM((3 * C, CELLS), jnp.float32),
            pltpu.VMEM((C, CELLS), jnp.float32),
            pltpu.VMEM((3 * C, CELLS), jnp.float32),
            pltpu.VMEM((CELLS, CELLS), jnp.float32),
        ],
    )(*arrays, krow, gain_row, wqkv, wp, *partial)


SUM_AXES = ("gy", "gz", "gx")


def swapped(block, axis, distance):
    return lax.ppermute(block, axis, [(i, i ^ distance) for i in range(lax.axis_size(axis))])


def summed_everywhere(matrix):
    sizes = [lax.axis_size(axis) for axis in SUM_AXES]
    if any(size & (size - 1) for size in sizes):
        return lax.psum(matrix, SUM_AXES)
    devices = 1
    for size in sizes:
        devices *= size
    unit = devices * 8 if devices * 8 <= 2 * matrix.shape[0] else devices
    padded = -(-matrix.shape[0] // unit) * unit
    values = jnp.pad(matrix, ((0, padded - matrix.shape[0]), (0, 0)))
    order = []
    for axis, size in zip(SUM_AXES, sizes):
        distance = 1
        while distance < size:
            order.append((axis, distance))
            distance *= 2
    order.sort(key=lambda step: (step[0] != SUM_AXES[0] or step[1] != 1, step[1] > 1))
    steps = []
    for axis, distance in order:
        bit = (lax.axis_index(axis) // distance) % 2
        half = values.shape[0] // 2
        keep = lax.dynamic_slice_in_dim(values, bit * half, half)
        send = lax.dynamic_slice_in_dim(values, (1 - bit) * half, half)
        values = keep + swapped(send, axis, distance)
        steps.append((axis, distance))
    for axis, distance in reversed(steps):
        bit = (lax.axis_index(axis) // distance) % 2
        other = swapped(values, axis, distance)
        half = values.shape[0]
        joined = jnp.zeros((2 * half,) + values.shape[1:], values.dtype)
        joined = lax.dynamic_update_slice_in_dim(joined, values, bit * half, 0)
        values = lax.dynamic_update_slice_in_dim(joined, other, (1 - bit) * half, 0)
    return values[: matrix.shape[0]]


def halo_route(distance_a, distance_b):
    size_a = lax.axis_size("gx")
    size_b = lax.axis_size(("gy", "gz"))
    route = []
    for ia in range(size_a):
        for ib in range(size_b):
            target = ((ia + distance_a) % size_a) * size_b + (ib + distance_b) % size_b
            route.append((ia * size_b + ib, target))
    return route


def moved(block, distance_a, distance_b):
    return lax.ppermute(block, ("gx", "gy", "gz"), halo_route(distance_a, distance_b))


def shifted_block(both):
    from_a = moved(both[:, :SHIFT, SHIFT:], -1, 0)
    from_b = moved(both[:, SHIFT:, :SHIFT], 0, -1)
    from_ab = moved(both[:, :SHIFT, :SHIFT], -1, -1)
    upper = jnp.concatenate([both[:, SHIFT:, SHIFT:], from_b], axis=2)
    lower = jnp.concatenate([from_a, from_ab], axis=2)
    return jnp.concatenate([upper, lower], axis=1)


def unshifted_sum(grads_out, grad_shifted):
    narrow = grad_shifted.astype(jnp.bfloat16)
    to_a = moved(narrow[-SHIFT:, :-SHIFT], 1, 0).astype(jnp.float32)
    to_b = moved(narrow[:-SHIFT, -SHIFT:], 0, 1).astype(jnp.float32)
    to_ab = moved(narrow[-SHIFT:, -SHIFT:], 1, 1).astype(jnp.float32)
    upper = jnp.concatenate([to_ab, to_a], axis=1)
    lower = jnp.concatenate([to_b, grad_shifted[:-SHIFT, :-SHIFT]], axis=1)
    branch = jnp.concatenate([upper, lower], axis=0)
    return (grads_out.astype(jnp.float32) + branch.astype(jnp.float32)).astype(jnp.bfloat16)


def per_device(tokens, grads_out, labels, ln_gain, qkv_weight, proj_weight):
    brick_a, brick_b = (tokens.shape[0], tokens.shape[1])
    brick_c = NZ
    channels = C
    both = shifted_block(jnp.stack([tokens, grads_out]))
    extent_a = brick_a * lax.axis_size("gx")
    extent_b = brick_b * lax.axis_size(("gy", "gz"))
    first_index = lax.axis_index("gx") * brick_a + jnp.arange(brick_a, dtype=jnp.int32)
    second_index = lax.axis_index(("gy", "gz")) * brick_b + jnp.arange(brick_b, dtype=jnp.int32)
    wrap_first = (first_index >= extent_a - SHIFT).astype(jnp.int32)
    wrap_second = (second_index >= extent_b - SHIFT).astype(jnp.int32)
    wrap_third = (jnp.arange(brick_c, dtype=jnp.int32) >= brick_c - SHIFT).astype(jnp.int32)
    region = (
        wrap_first[:, None, None] * 4 + wrap_second[None, :, None] * 2 + wrap_third[None, None, :]
    )
    mask_key = to_windows_key(labels * 8 + region)

    constants = (
        mask_key[:, None, :],
        ln_gain.reshape(1, channels),
        qkv_weight,
        proj_weight,
    )
    partial = window_grads(True, (tokens, grads_out), *constants)
    grad_branch, qkv_part, proj_grad, gain_grad = window_grads(
        False, (both,), *constants, partial=partial
    )
    width = 4 * channels
    gain_row = jnp.pad(gain_grad.reshape(1, channels), ((0, 0), (0, width - channels)))
    summed = summed_everywhere(
        jnp.concatenate([jnp.concatenate([qkv_part, proj_grad], axis=1), gain_row], axis=0)
    )
    qkv_grad = summed[:channels, : 3 * channels]
    proj_grad = summed[:channels, 3 * channels :]
    gain_grad = summed[channels, :channels]
    grad_tokens = unshifted_sum(grads_out, grad_branch)
    return (grad_tokens, gain_grad.reshape(-1), qkv_grad.reshape(-1), proj_grad.reshape(-1))


def solution(mesh):
    return jax.shard_map(
        per_device,
        mesh=mesh,
        in_specs=(
            P("gx", ("gy", "gz"), None),
            P("gx", ("gy", "gz"), None),
            P("gx", ("gy", "gz"), None),
            P(),
            P(),
            P(),
        ),
        out_specs=(P("gx", ("gy", "gz"), None), P(), P(), P()),
        check_vma=False,
    )
```

```python
import jax
import jax.numpy as jnp
from jax import lax
from jax.experimental import pallas as pl
from jax.experimental.pallas import tpu as pltpu
from jax.sharding import PartitionSpec as P

HEADS = 6
C = 192
WIN = 8
SHIFT = 4
NZ = 16
CELLS = WIN**3
HEAD = C // HEADS
SCALE = HEAD ** (-0.5)
EXP2_SCALE = SCALE * 1.4426950408889634


def passed_along(block, axis, distance):
    devices = range(lax.axis_size(axis))
    route = [((i - distance) % len(devices), i) for i in devices]
    return lax.ppermute(block, axis, route)


def to_windows_cm(values):
    extent_a, extent_b, extent_c, ch = values.shape
    shaped = values.reshape(extent_a // WIN, WIN, extent_b // WIN, WIN, extent_c // WIN, WIN, ch)
    return shaped.transpose(0, 2, 4, 6, 1, 3, 5).reshape(-1, ch, CELLS)


def from_windows_cm(values, extent_a, extent_b, extent_c):
    ch = values.shape[1]
    shaped = values.reshape(extent_a // WIN, extent_b // WIN, extent_c // WIN, ch, WIN, WIN, WIN)
    return shaped.transpose(0, 4, 1, 5, 2, 6, 3).reshape(extent_a, extent_b, extent_c, ch)


def to_windows_key(values):
    extent_a, extent_b, extent_c = values.shape
    shaped = values.reshape(extent_a // WIN, WIN, extent_b // WIN, WIN, extent_c // WIN, WIN)
    return shaped.transpose(0, 2, 4, 5, 1, 3).reshape(-1, CELLS)


def make_window_kernel(first):
    def window_kernel(*refs):
        if first:
            (tok_ref, grd_ref, krow_ref, gain_ref, wqkv_ref, wp_ref,
             gs_ref, gqkvT_ref, gproj_ref, ggain_ref, qkv_s, ga_s, drow_s, bias_s) = refs
        else:
            (both_ref, krow_ref, gain_ref, wqkv_ref, wp_ref,
             gs0_ref, gqkvT0_ref, gproj0_ref, ggain0_ref,
             gs_ref, gqkvT_ref, gproj_ref, ggain_ref, qkv_s, ga_s, drow_s, bias_s) = refs
        f32 = jnp.float32
        bf16 = jnp.bfloat16
        if first:
            gqkvT_ref[...] = jnp.zeros_like(gqkvT_ref)
            gproj_ref[...] = jnp.zeros_like(gproj_ref)
            ggain_ref[...] = jnp.zeros_like(ggain_ref)
        else:
            gqkvT_ref[...] = gqkvT0_ref[...]
            gproj_ref[...] = gproj0_ref[...]
            ggain_ref[...] = ggain0_ref[...]
            gs_ref[pl.ds(0, WIN), pl.ds(0, WIN), :] = gs0_ref[...]
        gain = jnp.broadcast_to(gain_ref[...], (8, C)).T[:, 0:1]
        wqkv_t = wqkv_ref[...].astype(f32).T.astype(bf16)
        nt = (((1,), (1,)), ((), ()))
        pair = 2 * C
        n_pairs = NZ // 2

        def gathered(which, i, j, l):
            pieces = []
            for q in range(WIN // 2):
                p = (WIN // 2 * l + SHIFT // 2 + q) % n_pairs
                if first:
                    source = (tok_ref, grd_ref)[which]
                    block = source[pl.ds(SHIFT, WIN), :, pl.ds(p * pair, pair)].astype(f32)
                    block = block[:, SHIFT:SHIFT + WIN]
                else:
                    block = both_ref[which, pl.ds(i * WIN, WIN), :, pl.ds(p * pair, pair)]
                    block = block.astype(f32)
                    block = jnp.where(j == 0, block[:, :WIN], block[:, WIN:])
                block = block.reshape(WIN * WIN, pair)
                pieces.append(block[:, :C])
                pieces.append(block[:, C:])
            return jnp.concatenate(pieces, axis=0).T

        def scattered(values_t, i, j, l):
            rows = values_t.T
            for q in range(WIN // 2):
                p = (WIN // 2 * l + SHIFT // 2 + q) % n_pairs
                even = rows[2 * q * WIN * WIN:(2 * q + 1) * WIN * WIN]
                odd = rows[(2 * q + 1) * WIN * WIN:(2 * q + 2) * WIN * WIN]
                block = jnp.concatenate([even, odd], axis=1).reshape(WIN, WIN, pair)
                if first:
                    gs_ref[:, :, pl.ds(p * pair, pair)] = block
                else:
                    gs_ref[
                        pl.ds(i * WIN, WIN),
                        pl.ds(pl.multiple_of(j * WIN, WIN), WIN),
                        pl.ds(p * pair, pair),
                    ] = block

        def window(ij, l):
            i = ij // 2
            j = ij % 2
            w = ij * 2 + l
            x = gathered(0, i, j, l)
            row_mean = jnp.mean(x, axis=0, keepdims=True)
            centred = x - row_mean
            inv_std = lax.rsqrt(jnp.mean(centred * centred, axis=0, keepdims=True) + 1e-05)
            x_hat = centred * inv_std
            normed = (x_hat * gain).astype(bf16)
            qkv_t = jnp.dot(wqkv_t, normed, preferred_element_type=f32)
            qkv_s[...] = qkv_t.astype(bf16).astype(f32)
            g = gathered(1, i, j, l).astype(bf16)
            ga_t = jnp.dot(wp_ref[...], g, preferred_element_type=f32)
            ga_s[...] = ga_t.astype(bf16).astype(f32)
            key_row = krow_ref[w].astype(f32)
            key_col = jnp.broadcast_to(key_row, (8, CELLS)).T[:, 0:1]
            bias_s[...] = jnp.where(key_col == key_row, 0.0, -jnp.inf)

            def head_step(h, carry):
                qo = pl.multiple_of(h * HEAD, HEAD)
                q_t = qkv_s[pl.ds(qo, HEAD), :]
                k_t = qkv_s[pl.ds(qo + C, HEAD), :]
                v_t = qkv_s[pl.ds(qo + 2 * C, HEAD), :]
                ga_th = ga_s[pl.ds(qo, HEAD), :]
                q = q_t.T.astype(bf16)
                scores = jnp.dot(q, k_t.astype(bf16), preferred_element_type=f32)
                weights = jnp.exp2(scores * EXP2_SCALE + bias_s[...])
                probs = weights / jnp.sum(weights, axis=1, keepdims=True)
                probs_bf = probs.astype(bf16)
                att_t = lax.dot_general(v_t.astype(bf16), probs_bf, nt, preferred_element_type=f32)
                att_t = att_t.astype(bf16)
                gproj_ref[pl.ds(qo, HEAD), :] += lax.dot_general(
                    att_t, g, nt, preferred_element_type=f32
                )
                ga = ga_th.T.astype(bf16)
                grad_probs = jnp.dot(ga, v_t.astype(bf16), preferred_element_type=f32)
                dv_t = jnp.dot(ga_th.astype(bf16), probs_bf, preferred_element_type=f32)
                row_total = jnp.sum(probs * grad_probs, axis=1, keepdims=True)
                grad_scores = (probs * (grad_probs - row_total) * SCALE).astype(bf16)
                dq_t = lax.dot_general(k_t.astype(bf16), grad_scores, nt, preferred_element_type=f32)
                dk_t = jnp.dot(q_t.astype(bf16), grad_scores, preferred_element_type=f32)
                drow_s[pl.ds(qo, HEAD), :] = dq_t.astype(bf16).astype(f32)
                drow_s[pl.ds(qo + C, HEAD), :] = dk_t.astype(bf16).astype(f32)
                drow_s[pl.ds(qo + 2 * C, HEAD), :] = dv_t.astype(bf16).astype(f32)
                return carry

            lax.fori_loop(0, HEADS, head_step, 0, unroll=2)
            rows_t = drow_s[...].astype(bf16)
            gqkvT_ref[...] += lax.dot_general(normed, rows_t, nt, preferred_element_type=f32)
            grad_normed = jnp.dot(wqkv_ref[...], rows_t, preferred_element_type=f32)
            ggain_ref[...] += jnp.sum(grad_normed * x_hat, axis=1, keepdims=True)
            scaled = grad_normed * gain
            grad_shifted = inv_std * (
                scaled
                - jnp.mean(scaled, axis=0, keepdims=True)
                - x_hat * jnp.mean(scaled * x_hat, axis=0, keepdims=True)
            )
            scattered(grad_shifted.astype(bf16).astype(f32), i, j, l)

        def block_step(ij, carry):
            for l in range(2):
                window(ij, l)
            return carry

        if first:
            block_step(0, 0)
        else:
            lax.fori_loop(1, 4, block_step, 0)

    return window_kernel


def window_grads(first, arrays, krow, gain_row, wqkv, wp, partial=()):
    if first:
        extent_a, extent_b, width = WIN, WIN, arrays[0].shape[2]
    else:
        extent_a, extent_b, width = arrays[0].shape[1:]
    return pl.pallas_call(
        make_window_kernel(first),
        out_shape=[
            jax.ShapeDtypeStruct((extent_a, extent_b, width), jnp.float32),
            jax.ShapeDtypeStruct((C, 3 * C), jnp.float32),
            jax.ShapeDtypeStruct((C, C), jnp.float32),
            jax.ShapeDtypeStruct((C, 1), jnp.float32),
        ],
        scratch_shapes=[
            pltpu.VMEM((3 * C, CELLS), jnp.float32),
            pltpu.VMEM((C, CELLS), jnp.float32),
            pltpu.VMEM((3 * C, CELLS), jnp.float32),
            pltpu.VMEM((CELLS, CELLS), jnp.float32),
        ],
    )(*arrays, krow, gain_row, wqkv, wp, *partial)


SUM_AXES = ("gy", "gz", "gx")


def swapped(block, axis, distance):
    return lax.ppermute(block, axis, [(i, i ^ distance) for i in range(lax.axis_size(axis))])


def summed_everywhere(matrix):
    sizes = [lax.axis_size(axis) for axis in SUM_AXES]
    if any(size & (size - 1) for size in sizes):
        return lax.psum(matrix, SUM_AXES)
    devices = 1
    for size in sizes:
        devices *= size
    unit = devices * 8 if devices * 8 <= 2 * matrix.shape[0] else devices
    padded = -(-matrix.shape[0] // unit) * unit
    values = jnp.pad(matrix, ((0, padded - matrix.shape[0]), (0, 0)))
    steps = []
    for axis, size in zip(SUM_AXES, sizes):
        distance = 1
        while distance < size:
            bit = (lax.axis_index(axis) // distance) % 2
            half = values.shape[0] // 2
            keep = lax.dynamic_slice_in_dim(values, bit * half, half)
            send = lax.dynamic_slice_in_dim(values, (1 - bit) * half, half)
            values = keep + swapped(send, axis, distance)
            steps.append((axis, distance))
            distance *= 2
    for axis, distance in reversed(steps):
        bit = (lax.axis_index(axis) // distance) % 2
        other = swapped(values, axis, distance)
        half = values.shape[0]
        joined = jnp.zeros((2 * half,) + values.shape[1:], values.dtype)
        joined = lax.dynamic_update_slice_in_dim(joined, values, bit * half, 0)
        values = lax.dynamic_update_slice_in_dim(joined, other, (1 - bit) * half, 0)
    return values[: matrix.shape[0]]


def halo_route(distance_a, distance_b):
    size_a = lax.axis_size("gx")
    size_b = lax.axis_size(("gy", "gz"))
    route = []
    for ia in range(size_a):
        for ib in range(size_b):
            target = ((ia + distance_a) % size_a) * size_b + (ib + distance_b) % size_b
            route.append((ia * size_b + ib, target))
    return route


def moved(block, distance_a, distance_b):
    return lax.ppermute(block, ("gx", "gy", "gz"), halo_route(distance_a, distance_b))


def shifted_block(both):
    from_a = moved(both[:, :SHIFT, SHIFT:], -1, 0)
    from_b = moved(both[:, SHIFT:, :SHIFT], 0, -1)
    from_ab = moved(both[:, :SHIFT, :SHIFT], -1, -1)
    upper = jnp.concatenate([both[:, SHIFT:, SHIFT:], from_b], axis=2)
    lower = jnp.concatenate([from_a, from_ab], axis=2)
    return jnp.concatenate([upper, lower], axis=1)


def unshifted_sum(grads_out, grad_shifted):
    narrow = grad_shifted.astype(jnp.bfloat16)
    to_a = moved(narrow[-SHIFT:, :-SHIFT], 1, 0).astype(jnp.float32)
    to_b = moved(narrow[:-SHIFT, -SHIFT:], 0, 1).astype(jnp.float32)
    to_ab = moved(narrow[-SHIFT:, -SHIFT:], 1, 1).astype(jnp.float32)
    upper = jnp.concatenate([to_ab, to_a], axis=1)
    lower = jnp.concatenate([to_b, grad_shifted[:-SHIFT, :-SHIFT]], axis=1)
    branch = jnp.concatenate([upper, lower], axis=0)
    return (grads_out.astype(jnp.float32) + branch.astype(jnp.float32)).astype(jnp.bfloat16)


def per_device(tokens, grads_out, labels, ln_gain, qkv_weight, proj_weight):
    brick_a, brick_b = (tokens.shape[0], tokens.shape[1])
    brick_c = NZ
    channels = C
    both = shifted_block(jnp.stack([tokens, grads_out]))
    extent_a = brick_a * lax.axis_size("gx")
    extent_b = brick_b * lax.axis_size(("gy", "gz"))
    first_index = lax.axis_index("gx") * brick_a + jnp.arange(brick_a, dtype=jnp.int32)
    second_index = lax.axis_index(("gy", "gz")) * brick_b + jnp.arange(brick_b, dtype=jnp.int32)
    wrap_first = (first_index >= extent_a - SHIFT).astype(jnp.int32)
    wrap_second = (second_index >= extent_b - SHIFT).astype(jnp.int32)
    wrap_third = (jnp.arange(brick_c, dtype=jnp.int32) >= brick_c - SHIFT).astype(jnp.int32)
    region = (
        wrap_first[:, None, None] * 4 + wrap_second[None, :, None] * 2 + wrap_third[None, None, :]
    )
    mask_key = to_windows_key(labels * 8 + region)

    constants = (
        mask_key[:, None, :],
        ln_gain.reshape(1, channels),
        qkv_weight,
        proj_weight,
    )
    partial = window_grads(True, (tokens, grads_out), *constants)
    grad_branch, qkv_part, proj_grad, gain_grad = window_grads(
        False, (both,), *constants, partial=partial
    )
    width = 4 * channels
    gain_row = jnp.pad(gain_grad.reshape(1, channels), ((0, 0), (0, width - channels)))
    summed = summed_everywhere(
        jnp.concatenate([jnp.concatenate([qkv_part, proj_grad], axis=1), gain_row], axis=0)
    )
    qkv_grad = summed[:channels, : 3 * channels]
    proj_grad = summed[:channels, 3 * channels :]
    gain_grad = summed[channels, :channels]
    grad_tokens = unshifted_sum(grads_out, grad_branch)
    return (grad_tokens, gain_grad.reshape(-1), qkv_grad.reshape(-1), proj_grad.reshape(-1))


def solution(mesh):
    return jax.shard_map(
        per_device,
        mesh=mesh,
        in_specs=(
            P("gx", ("gy", "gz"), None),
            P("gx", ("gy", "gz"), None),
            P("gx", ("gy", "gz"), None),
            P(),
            P(),
            P(),
        ),
        out_specs=(P("gx", ("gy", "gz"), None), P(), P(), P()),
        check_vma=False,
    )
```
